128 devices in a mesh: store: 32 (over x, y, core), tensor: 4 (over z).
Axes of the slice: x: 4, y: 4, z: 4, core: 2. Of those that a mesh axis runs over, the one named last changes fastest.
Arguments:
- questions: bfloat16 [8192, 8192], P('store', 'tensor'), may hold values from -6 to 6
- w_query: bfloat16 [8192, 4096], P(None, 'tensor'), may hold values from -0.0625 to 0.0625
- w_key: bfloat16 [8192, 512], P(None, 'tensor'), may hold values from -0.0625 to 0.0625
- w_value: bfloat16 [8192, 512], P(None, 'tensor'), may hold values from -0.0625 to 0.0625
- passage_keys: bfloat16 [128, 512, 512], P('store', None, 'tensor'), may hold values from -240 to 240
- passage_values: bfloat16 [128, 512, 512], P('store', None, 'tensor'), may hold values from -6 to 6
- passage_ids: int32 [64, 16], P('store'), may hold values from 0 to 127, as said below
- slot_order: int32 [64, 16], P('store'), may hold values from 0 to 15, each once within a row
Outputs:
- context: bfloat16 [8192, 4096], P('store', 'tensor')
The draws below stay inside these ranges and needn't reach their ends.
Inputs may be any that keep to these rules, and one draw needn't show every extreme that they name: `passage_ids`: passage p is stored at index p // 4 of store. Among the 32 entries of the questions of one index of store, at most 2 name passages stored at one index, and on every index some stored index is named exactly 2 times. A question may name a passage more than once.
All inputs are finite; a program needn't handle non-finite values.
Results may differ from the reference program's by a relative error of at most 0.015.
The reference program's roundings to bfloat16 on the way count: a program that leaves them out, or rounds other values in their place, can miss the bound.
Values may be sent and summed in bfloat16 or wider, within the bound.
No kernel may reach another device: no remote copies, remote signals or barrier semaphores. Data moves between devices by JAX's collectives and lax.ppermute only.
A program may use at most 192 MiB of HBM per device.

```python
import jax
import jax.numpy as jnp
from jax import lax

D = 8192
HD = 128
QH = 32
KVH = 4
QLEN = 128
PLEN = 512
RETR = 16
Q_DEV = 2
PASS_DEV = 4
CAP = 2
QUESTIONS = 64
PASSAGES = 128
TOKENS = 8192


def draw_passage_keys(key, part):
    first = jax.random.fold_in(jax.random.fold_in(key, 11), 0)
    base = jnp.clip(jax.random.normal(first, (PASSAGES, PLEN, KVH * HD), jnp.float32), -6.0, 6.0)
    return base.astype(jnp.bfloat16)


def draw_passage_ids(key, part):
    owners_count = QUESTIONS // Q_DEV
    listed = Q_DEV * RETR
    slots = owners_count * CAP

    def one_device(sub):
        first, second, third = jax.random.split(sub, 3)
        favored = jax.random.randint(first, (), 0, owners_count)
        index = jnp.arange(slots, dtype=jnp.int32)
        noise = jax.random.randint(second, (slots,), 1, 1 << 20)
        score = jnp.where(index // CAP == favored, index, noise * slots + index)
        order = jnp.argsort(score)
        owners = order[:listed] // CAP
        local = jax.random.randint(third, (listed,), 0, PASS_DEV)
        return owners * PASS_DEV + local
    keys = jax.random.split(jax.random.fold_in(key, 23), owners_count)
    ids = jax.vmap(one_device)(keys)
    return ids.reshape(QUESTIONS, RETR).astype(jnp.int32)


def shard_levels(key, dims, cuts, least, largest):
    level = 1.0
    for position, blocks in cuts:
        heights = jax.random.uniform(jax.random.fold_in(jax.random.fold_in(key, 6), position), (blocks,), jnp.float32, least / len(cuts), largest / len(cuts))
        level = level * jnp.repeat(jnp.exp(heights), dims[position] // blocks).reshape((-1,) + (1,) * (len(dims) - 1 - position))
    return level


def gaussian(rng, dims, spread, bound, cuts=(), held_as=jnp.bfloat16):
    entries = jax.random.normal(rng, dims, jnp.float32) * spread
    if len(cuts) > 0:
        entries = shard_levels(rng, dims, cuts, -0.22, 0.18) * entries
    return jnp.clip(entries, min=-bound, max=bound).astype(held_as)


def setup_inputs(seed: int = 0) -> dict:
    key_of = jax.random.split(jax.random.key(seed), 9)
    return {
        "questions": gaussian(key_of[0], (TOKENS, D), 1.0, 6.0, ((0, 32), (1, 4))),
        "w_query": gaussian(key_of[1], (D, QH * HD), D ** -0.5, 0.0625, ((1, 4),)),
        "w_key": gaussian(key_of[2], (D, KVH * HD), D ** -0.5, 0.0625, ((1, 4),)),
        "w_value": gaussian(key_of[3], (D, KVH * HD), D ** -0.5, 0.0625, ((1, 4),)),
        "passage_keys": draw_passage_keys(jax.random.fold_in(key_of[8], 71), 0),
        "passage_values": gaussian(key_of[5], (PASSAGES, PLEN, KVH * HD), 1.0, 6.0, ((0, 32), (2, 4))),
        "passage_ids": draw_passage_ids(jax.random.fold_in(key_of[8], 71), 0),
        "slot_order": jax.vmap(lambda own: jax.random.permutation(own, RETR))(jax.random.split(key_of[7], QUESTIONS)).reshape((QUESTIONS, RETR)).astype(jnp.int32),
    }


def angles(positions):
    freqs = 500000.0 ** (-(jnp.arange(HD // 2, dtype=jnp.float32) * 2.0) / HD)
    turned = positions[..., None] * freqs
    return jnp.cos(turned), jnp.sin(turned)


def rotate(values, cosine, sine):
    half = values.shape[-1] // 2
    first = values[..., :half]
    second = values[..., half:]
    return jnp.concatenate([first * cosine - second * sine, second * cosine + first * sine], axis=-1)


def attend(query, keys_shift, vals, self_keys, self_vals):
    scale = HD ** -0.5
    scores = jnp.einsum("tghd,rpgd->ghtrp", query.astype(jnp.float32), keys_shift.astype(jnp.float32)) * scale
    peak = jnp.max(scores, axis=-1)
    expo = jnp.exp(scores - peak[..., None])
    total = jnp.sum(expo, axis=-1)
    part = jnp.einsum("ghtrp,rpgd->ghtrd", expo.astype(jnp.bfloat16).astype(jnp.float32), vals.astype(jnp.float32))
    length = query.shape[0]
    causal = jnp.arange(length)[:, None] >= jnp.arange(length)[None, :]
    own = jnp.einsum("tghd,ugd->ghtu", query.astype(jnp.float32), self_keys.astype(jnp.float32)) * scale
    own = jnp.where(causal, own, -1e30)
    own_peak = jnp.max(own, axis=-1)
    own_expo = jnp.where(causal, jnp.exp(own - own_peak[..., None]), 0.0)
    own_total = jnp.sum(own_expo, axis=-1)
    own_part = jnp.einsum("ghtu,ugd->ghtd", own_expo.astype(jnp.bfloat16).astype(jnp.float32), self_vals.astype(jnp.float32))
    top = jnp.maximum(jnp.max(peak, axis=-1), own_peak)
    weight = jnp.exp(peak - top[..., None])
    own_weight = jnp.exp(own_peak - top)
    denom = jnp.sum(weight * total, axis=-1) + own_weight * own_total
    numer = jnp.sum(weight[..., None] * part, axis=-2) + own_weight[..., None] * own_part
    result = numer / denom[..., None]
    return jnp.transpose(result, (2, 0, 1, 3)).reshape(length, -1).astype(jnp.bfloat16)


def reference(questions, w_query, w_key, w_value, passage_keys, passage_values, passage_ids, slot_order):
    kv_heads = w_key.shape[1] // HD
    q_heads = w_query.shape[1] // HD
    group = q_heads // kv_heads
    count = questions.shape[0] // QLEN
    qpos = (RETR * PLEN + jnp.arange(QLEN)).astype(jnp.float32)
    cosine, sine = angles(qpos)
    cosine = cosine[None, :, None, :]
    sine = sine[None, :, None, :]
    qf = jnp.dot(questions, w_query, preferred_element_type=jnp.float32).reshape(count, QLEN, q_heads, HD)
    query = rotate(qf, cosine, sine).astype(jnp.bfloat16).reshape(count, QLEN, kv_heads, group, HD)
    kf = jnp.dot(questions, w_key, preferred_element_type=jnp.float32).reshape(count, QLEN, kv_heads, HD)
    self_key = rotate(kf, cosine, sine).astype(jnp.bfloat16)
    self_value = jnp.dot(questions, w_value, preferred_element_type=jnp.float32).astype(jnp.bfloat16).reshape(count, QLEN, kv_heads, HD)

    def one_question(item):
        qv, keys_own, vals_own, chosen, order = item
        start = (order * PLEN).astype(jnp.float32)
        cs, sn = angles(start)
        raw = passage_keys[chosen].reshape(RETR, PLEN, kv_heads, HD).astype(jnp.float32)
        shifted = rotate(raw, cs[:, None, None, :], sn[:, None, None, :]).astype(jnp.bfloat16)
        vals = passage_values[chosen].reshape(RETR, PLEN, kv_heads, HD)
        return attend(qv, shifted, vals, keys_own, vals_own)

    out = lax.map(one_question, (query, self_key, self_value, passage_ids, slot_order))
    return out.reshape(count * QLEN, q_heads * HD)
```

```python
import functools

import jax
import jax.numpy as jnp
from jax import lax
from jax.experimental import pallas as pl
from jax.experimental.pallas import tpu as pltpu
from jax.sharding import PartitionSpec as P

HD = 128
QLEN = 128
PLEN = 512
RETR = 16
CAP = 2


def angles(positions):
    freqs = 500000.0 ** (-(jnp.arange(HD // 2, dtype=jnp.float32) * 2.0) / HD)
    turned = positions[..., None] * freqs
    return (jnp.cos(turned), jnp.sin(turned))


def rotate(values, cosine, sine):
    half = values.shape[-1] // 2
    first = values[..., :half]
    second = values[..., half:]
    return jnp.concatenate(
        [first * cosine - second * sine, second * cosine + first * sine], axis=-1
    )


def block_kernel(tab_ref, remap_ref, q_ref, kv_ref, m_in, l_in, a_in, m_ref, l_ref, a_ref):
    o = pl.program_id(0)

    @pl.when(o == 0)
    def _():
        m_ref[...] = m_in[...]
        l_ref[...] = l_in[...]
        a_ref[...] = a_in[...]

    qi = tab_ref[o]

    @pl.when(qi >= 0)
    def _():
        q = q_ref[qi]
        k = kv_ref[0, 0]
        v = kv_ref[0, 1]
        s = lax.dot_general(
            q, k, (((1,), (1,)), ((), ())), preferred_element_type=jnp.float32
        ) * (HD ** (-0.5))
        m = jnp.max(s, axis=1, keepdims=True)
        e = jnp.exp(s - m)
        l = jnp.sum(e, axis=1, keepdims=True)
        p = jnp.dot(e.astype(jnp.bfloat16), v, preferred_element_type=jnp.float32)
        m_old = m_ref[qi]
        m_new = jnp.maximum(m_old, m)
        w_old = jnp.exp(m_old - m_new)
        w_new = jnp.exp(m - m_new)
        l_ref[qi] = w_old * l_ref[qi] + w_new * l
        a_ref[qi] = w_old * a_ref[qi] + w_new * p
        m_ref[qi] = m_new


def attend_chunk(tab, remap, query, recv, m, l, acc):
    owners = recv.shape[0]
    nq, rows, hd = query.shape
    plen = recv.shape[2]
    full3 = lambda shape: pl.BlockSpec(shape, lambda o, t, r: (0, 0, 0))
    grid_spec = pltpu.PrefetchScalarGridSpec(
        num_scalar_prefetch=2,
        grid=(owners,),
        in_specs=[
            full3((nq, rows, hd)),
            pl.BlockSpec((1, 2, plen, hd), lambda o, t, r: (r[o], 0, 0, 0)),
            full3((nq, rows, 1)),
            full3((nq, rows, 1)),
            full3((nq, rows, hd)),
        ],
        out_specs=[full3((nq, rows, 1)), full3((nq, rows, 1)), full3((nq, rows, hd))],
    )
    flops = 4 * nq * rows * plen * hd * owners // 2
    return pl.pallas_call(
        block_kernel,
        grid_spec=grid_spec,
        out_shape=[
            jax.ShapeDtypeStruct(m.shape, jnp.float32),
            jax.ShapeDtypeStruct(l.shape, jnp.float32),
            jax.ShapeDtypeStruct(acc.shape, jnp.float32),
        ],
        input_output_aliases={4: 0, 5: 1, 6: 2},
        compiler_params=pltpu.CompilerParams(
            dimension_semantics=("arbitrary",), vmem_limit_bytes=48 * 1024 * 1024
        ),
        cost_estimate=pl.CostEstimate(
            flops=flops,
            transcendentals=nq * rows * plen * owners // 2,
            bytes_accessed=recv.size * 2 + 2 * acc.size * 4,
        ),
    )(tab, remap, query, recv, m, l, acc)


def per_device(
    questions, w_query, w_key, w_value, passage_keys, passage_values, passage_ids, slot_order
):
    kv_heads = w_key.shape[1] // HD
    q_heads = w_query.shape[1] // HD
    group = q_heads // kv_heads
    tok_rows = questions.shape[0]
    count = tok_rows // QLEN
    stored = passage_keys.shape[0]
    owners_count = lax.axis_size("store")
    me = lax.axis_index("store")

    listing = jnp.stack([passage_ids.reshape(-1), slot_order.reshape(-1)])
    every = lax.all_gather(listing, "store", axis=0)
    listed = count * RETR
    all_ids = every[:, 0]
    all_pos = every[:, 1]
    all_owner = all_ids // stored
    all_local = all_ids % stored
    mine = (all_owner == me).astype(jnp.int32)
    all_rank = jnp.cumsum(mine, axis=1) - mine

    sends = []
    for c in range(CAP):
        sel = mine * (all_rank == c).astype(jnp.int32)
        loc = jnp.sum(sel * all_local, axis=1)
        pos = jnp.sum(sel * all_pos, axis=1)
        raw = passage_keys[loc].astype(jnp.float32)
        cs, sn = angles((pos * PLEN).astype(jnp.float32))
        shifted = rotate(raw, cs[:, None, :], sn[:, None, :]).astype(jnp.bfloat16)
        vals = passage_values[loc]
        sends.append(jnp.stack([shifted, vals], axis=1))

    recvs = [
        lax.all_to_all(s, "store", split_axis=0, concat_axis=0, tiled=True) for s in sends
    ]

    piece = lax.all_gather(questions, "tensor", axis=1, tiled=True)
    qf = jnp.dot(piece, w_query, preferred_element_type=jnp.float32)
    kf = jnp.dot(piece, w_key, preferred_element_type=jnp.float32)
    vf = jnp.dot(piece, w_value, preferred_element_type=jnp.float32)
    qpos = (RETR * PLEN + jnp.arange(QLEN)).astype(jnp.float32)
    cosine, sine = angles(qpos)
    cosine = cosine[None, :, None, :]
    sine = sine[None, :, None, :]
    query = rotate(qf.reshape(count, QLEN, q_heads, HD), cosine, sine).astype(jnp.bfloat16)
    self_key = rotate(kf.reshape(count, QLEN, kv_heads, HD), cosine, sine).astype(jnp.bfloat16)
    self_key = self_key.reshape(count, QLEN, HD)
    self_value = vf.astype(jnp.bfloat16).reshape(count, QLEN, HD)
    query = jnp.transpose(query, (0, 2, 1, 3))

    scale = HD ** (-0.5)
    own = jnp.einsum("qhtd,qud->qhtu", query, self_key, preferred_element_type=jnp.float32) * scale
    causal = jnp.arange(QLEN)[:, None] >= jnp.arange(QLEN)[None, :]
    own = jnp.where(causal, own, -1e30)
    own_peak = jnp.max(own, axis=-1, keepdims=True)
    own_expo = jnp.where(causal, jnp.exp(own - own_peak), 0.0)
    own_total = jnp.sum(own_expo, axis=-1, keepdims=True)
    own_part = jnp.einsum(
        "qhtu,qud->qhtd", own_expo.astype(jnp.bfloat16), self_value,
        preferred_element_type=jnp.float32,
    )
    rows = q_heads * QLEN
    m = own_peak.reshape(count, rows, 1)
    l = own_total.reshape(count, rows, 1)
    acc = own_part.reshape(count, rows, HD)
    qflat = query.reshape(count, rows, HD)

    my_ids = passage_ids.reshape(-1)
    my_owner = my_ids // stored
    onehot = (my_owner[:, None] == jnp.arange(owners_count, dtype=jnp.int32)[None, :]).astype(
        jnp.int32
    )
    before = jnp.cumsum(onehot, axis=0) - onehot
    my_rank = jnp.sum(before * onehot, axis=1)
    qidx = jnp.arange(listed, dtype=jnp.int32) // RETR
    slots = jnp.arange(owners_count, dtype=jnp.int32)
    for c in range(CAP):
        hit = onehot * (my_rank == c).astype(jnp.int32)[:, None]
        valid = jnp.sum(hit, axis=0)
        tab = jnp.sum(hit * qidx[:, None], axis=0) + valid - 1
        remap = lax.cummax(jnp.where(valid > 0, slots, 0), axis=0)
        m, l, acc = attend_chunk(tab, remap, qflat, recvs[c], m, l, acc)

    ctx = (acc / l).reshape(count, q_heads, QLEN, HD)
    ctx = jnp.transpose(ctx, (0, 2, 1, 3)).reshape(tok_rows, q_heads * HD)
    return ctx.astype(jnp.bfloat16)


def solution(mesh):
    in_specs = (
        P("store", "tensor"),
        P(None, "tensor"),
        P(None, "tensor"),
        P(None, "tensor"),
        P("store", None, "tensor"),
        P("store", None, "tensor"),
        P("store", None),
        P("store", None),
    )
    out_specs = P("store", "tensor")
    return jax.shard_map(
        per_device, mesh=mesh, in_specs=in_specs, out_specs=out_specs, check_vma=False
    )
```

```python
import functools

import jax
import jax.numpy as jnp
from jax import lax
from jax.experimental import pallas as pl
from jax.experimental.pallas import tpu as pltpu
from jax.sharding import PartitionSpec as P

HD = 128
QLEN = 128
PLEN = 512
RETR = 16
CAP = 2


def angles(positions):
    freqs = 500000.0 ** (-(jnp.arange(HD // 2, dtype=jnp.float32) * 2.0) / HD)
    turned = positions[..., None] * freqs
    return (jnp.cos(turned), jnp.sin(turned))


def rotate(values, cosine, sine):
    half = values.shape[-1] // 2
    first = values[..., :half]
    second = values[..., half:]
    return jnp.concatenate(
        [first * cosine - second * sine, second * cosine + first * sine], axis=-1
    )


def send_kernel(loc_ref, k_ref, v_ref, c_ref, s_ref, out_ref):
    k = k_ref[0].astype(jnp.float32)
    turned = pltpu.roll(k, k.shape[-1] // 2, 1)
    out_ref[0, 0] = (k * c_ref[0] + turned * s_ref[0]).astype(jnp.bfloat16)
    out_ref[0, 1] = v_ref[0]


def build_send(loc, cos_full, sin_full, passage_keys, passage_values):
    owners = loc.shape[0]
    _, plen, hd = passage_keys.shape
    grid_spec = pltpu.PrefetchScalarGridSpec(
        num_scalar_prefetch=1,
        grid=(owners,),
        in_specs=[
            pl.BlockSpec((1, plen, hd), lambda d, loc: (loc[d], 0, 0)),
            pl.BlockSpec((1, plen, hd), lambda d, loc: (loc[d], 0, 0)),
            pl.BlockSpec((1, 1, hd), lambda d, loc: (d, 0, 0)),
            pl.BlockSpec((1, 1, hd), lambda d, loc: (d, 0, 0)),
        ],
        out_specs=pl.BlockSpec((1, 2, plen, hd), lambda d, loc: (d, 0, 0, 0)),
    )
    return pl.pallas_call(
        send_kernel,
        grid_spec=grid_spec,
        out_shape=jax.ShapeDtypeStruct((owners, 2, plen, hd), jnp.bfloat16),
        compiler_params=pltpu.CompilerParams(dimension_semantics=("arbitrary",)),
        cost_estimate=pl.CostEstimate(
            flops=4 * owners * plen * hd, transcendentals=0,
            bytes_accessed=owners * plen * hd * 2 * 4,
        ),
    )(loc, passage_keys, passage_values, cos_full, sin_full)


def block_kernel(tab_ref, remap_ref, q_ref, kv_ref, m_in, l_in, a_in, m_ref, l_ref, a_ref):
    o = pl.program_id(0)

    @pl.when(o == 0)
    def _():
        m_ref[...] = m_in[...]
        l_ref[...] = l_in[...]
        a_ref[...] = a_in[...]

    qi = tab_ref[o]
    tile = HD
    heads = q_ref.shape[1] // tile

    @pl.when(qi >= 0)
    def _():
        k = kv_ref[0, 0]
        v = kv_ref[0, 1]

        def body(h, carry):
            rows = pl.ds(pl.multiple_of(h * tile, tile), tile)
            q = q_ref[qi, rows, :]
            s = lax.dot_general(
                q, k, (((1,), (1,)), ((), ())), preferred_element_type=jnp.float32
            ) * (HD ** (-0.5))
            m = jnp.max(s, axis=1, keepdims=True)
            e = jnp.exp(s - m)
            l = jnp.sum(e, axis=1, keepdims=True)
            p = jnp.dot(e.astype(jnp.bfloat16), v, preferred_element_type=jnp.float32)
            m_old = m_ref[qi, rows, :]
            m_new = jnp.maximum(m_old, m)
            w_old = jnp.exp(m_old - m_new)
            w_new = jnp.exp(m - m_new)
            l_ref[qi, rows, :] = w_old * l_ref[qi, rows, :] + w_new * l
            a_ref[qi, rows, :] = w_old * a_ref[qi, rows, :] + w_new * p
            m_ref[qi, rows, :] = m_new
            return carry

        lax.fori_loop(0, heads, body, 0)


def attend_chunk(tab, remap, query, recv, m, l, acc):
    owners = recv.shape[0]
    nq, rows, hd = query.shape
    plen = recv.shape[2]
    full3 = lambda shape: pl.BlockSpec(shape, lambda o, t, r: (0, 0, 0))
    grid_spec = pltpu.PrefetchScalarGridSpec(
        num_scalar_prefetch=2,
        grid=(owners,),
        in_specs=[
            full3((nq, rows, hd)),
            pl.BlockSpec((1, 2, plen, hd), lambda o, t, r: (r[o], 0, 0, 0)),
            full3((nq, rows, 1)),
            full3((nq, rows, 1)),
            full3((nq, rows, hd)),
        ],
        out_specs=[full3((nq, rows, 1)), full3((nq, rows, 1)), full3((nq, rows, hd))],
    )
    flops = 4 * nq * rows * plen * hd * owners // 2
    return pl.pallas_call(
        block_kernel,
        grid_spec=grid_spec,
        out_shape=[
            jax.ShapeDtypeStruct(m.shape, jnp.float32),
            jax.ShapeDtypeStruct(l.shape, jnp.float32),
            jax.ShapeDtypeStruct(acc.shape, jnp.float32),
        ],
        input_output_aliases={4: 0, 5: 1, 6: 2},
        compiler_params=pltpu.CompilerParams(
            dimension_semantics=("arbitrary",), vmem_limit_bytes=48 * 1024 * 1024
        ),
        cost_estimate=pl.CostEstimate(
            flops=flops,
            transcendentals=nq * rows * plen * owners // 2,
            bytes_accessed=recv.size * 2 + 2 * acc.size * 4,
        ),
    )(tab, remap, query, recv, m, l, acc)


def per_device(
    questions, w_query, w_key, w_value, passage_keys, passage_values, passage_ids, slot_order
):
    kv_heads = w_key.shape[1] // HD
    q_heads = w_query.shape[1] // HD
    group = q_heads // kv_heads
    tok_rows = questions.shape[0]
    count = tok_rows // QLEN
    stored = passage_keys.shape[0]
    owners_count = lax.axis_size("store")
    me = lax.axis_index("store")

    listing = jnp.stack([passage_ids.reshape(-1), slot_order.reshape(-1)])
    every = lax.all_gather(listing.astype(jnp.float32), "store", axis=0)
    every = every.astype(jnp.int32)
    listed = count * RETR
    all_ids = every[:, 0]
    all_pos = every[:, 1]
    all_owner = all_ids // stored
    all_local = all_ids % stored
    mine = (all_owner == me).astype(jnp.int32)
    all_rank = jnp.cumsum(mine, axis=1) - mine

    sends = []
    for c in range(CAP):
        sel = mine * (all_rank == c).astype(jnp.int32)
        loc = jnp.sum(sel * all_local, axis=1)
        pos = jnp.sum(sel * all_pos, axis=1)
        cs, sn = angles((pos * PLEN).astype(jnp.float32))
        cos_full = jnp.concatenate([cs, cs], axis=-1)[:, None, :]
        sin_full = jnp.concatenate([-sn, sn], axis=-1)[:, None, :]
        sends.append(build_send(loc, cos_full, sin_full, passage_keys, passage_values))

    recvs = [
        lax.all_to_all(s, "store", split_axis=0, concat_axis=0, tiled=True) for s in sends
    ]

    piece = lax.all_gather(questions, "tensor", axis=1, tiled=True)
    qf = jnp.dot(piece, w_query, preferred_element_type=jnp.float32)
    kf = jnp.dot(piece, w_key, preferred_element_type=jnp.float32)
    vf = jnp.dot(piece, w_value, preferred_element_type=jnp.float32)
    qpos = (RETR * PLEN + jnp.arange(QLEN)).astype(jnp.float32)
    cosine, sine = angles(qpos)
    cosine = cosine[None, :, None, :]
    sine = sine[None, :, None, :]
    query = rotate(qf.reshape(count, QLEN, q_heads, HD), cosine, sine).astype(jnp.bfloat16)
    self_key = rotate(kf.reshape(count, QLEN, kv_heads, HD), cosine, sine).astype(jnp.bfloat16)
    self_key = self_key.reshape(count, QLEN, HD)
    self_value = vf.astype(jnp.bfloat16).reshape(count, QLEN, HD)
    query = jnp.transpose(query, (0, 2, 1, 3))

    scale = HD ** (-0.5)
    own = jnp.einsum("qhtd,qud->qhtu", query, self_key, preferred_element_type=jnp.float32) * scale
    causal = jnp.arange(QLEN)[:, None] >= jnp.arange(QLEN)[None, :]
    own = jnp.where(causal, own, -1e30)
    own_peak = jnp.max(own, axis=-1, keepdims=True)
    own_expo = jnp.where(causal, jnp.exp(own - own_peak), 0.0)
    own_total = jnp.sum(own_expo, axis=-1, keepdims=True)
    own_part = jnp.einsum(
        "qhtu,qud->qhtd", own_expo.astype(jnp.bfloat16), self_value,
        preferred_element_type=jnp.float32,
    )
    rows = q_heads * QLEN
    m = own_peak.reshape(count, rows, 1)
    l = own_total.reshape(count, rows, 1)
    acc = own_part.reshape(count, rows, HD)
    qflat = query.reshape(count, rows, HD)

    my_ids = passage_ids.reshape(-1)
    my_owner = my_ids // stored
    onehot = (my_owner[:, None] == jnp.arange(owners_count, dtype=jnp.int32)[None, :]).astype(
        jnp.int32
    )
    before = jnp.cumsum(onehot, axis=0) - onehot
    my_rank = jnp.sum(before * onehot, axis=1)
    qidx = jnp.arange(listed, dtype=jnp.int32) // RETR
    slots = jnp.arange(owners_count, dtype=jnp.int32)
    for c in range(CAP):
        hit = onehot * (my_rank == c).astype(jnp.int32)[:, None]
        valid = jnp.sum(hit, axis=0)
        tab = jnp.sum(hit * qidx[:, None], axis=0) + valid - 1
        remap = lax.cummax(jnp.where(valid > 0, slots, 0), axis=0)
        m, l, acc = attend_chunk(tab, remap, qflat, recvs[c], m, l, acc)

    ctx = (acc / l).reshape(count, q_heads, QLEN, HD)
    ctx = jnp.transpose(ctx, (0, 2, 1, 3)).reshape(tok_rows, q_heads * HD)
    return ctx.astype(jnp.bfloat16)


def solution(mesh):
    in_specs = (
        P("store", "tensor"),
        P(None, "tensor"),
        P(None, "tensor"),
        P(None, "tensor"),
        P("store", None, "tensor"),
        P("store", None, "tensor"),
        P("store", None),
        P("store", None),
    )
    out_specs = P("store", "tensor")
    return jax.shard_map(
        per_device, mesh=mesh, in_specs=in_specs, out_specs=out_specs, check_vma=False
    )
```

```python
import functools

import jax
import jax.numpy as jnp
from jax import lax
from jax.experimental import pallas as pl
from jax.experimental.pallas import tpu as pltpu
from jax.sharding import PartitionSpec as P

HD = 128
QLEN = 128
PLEN = 512
RETR = 16
CAP = 2


def angles(positions):
    freqs = 500000.0 ** (-(jnp.arange(HD // 2, dtype=jnp.float32) * 2.0) / HD)
    turned = positions[..., None] * freqs
    return (jnp.cos(turned), jnp.sin(turned))


def rotate(values, cosine, sine):
    half = values.shape[-1] // 2
    first = values[..., :half]
    second = values[..., half:]
    return jnp.concatenate(
        [first * cosine - second * sine, second * cosine + first * sine], axis=-1
    )


def send_kernel(loc_ref, k_ref, v_ref, c_ref, s_ref, out_ref):
    per = out_ref.shape[0]
    base = pl.program_id(0) * per

    def body(j, carry):
        loc = loc_ref[base + j]
        k = k_ref[loc].astype(jnp.float32)
        turned = pltpu.roll(k, k.shape[-1] // 2, 1)
        cos_row = c_ref[pl.ds(base + j, 1), :]
        sin_row = s_ref[pl.ds(base + j, 1), :]
        out_ref[j, 0] = (k * cos_row + turned * sin_row).astype(jnp.bfloat16)
        out_ref[j, 1] = v_ref[loc]
        return carry

    lax.fori_loop(0, per, body, 0)


def build_send(loc, cos_full, sin_full, passage_keys, passage_values):
    owners = loc.shape[0]
    stored, plen, hd = passage_keys.shape
    per = 8
    full = lambda shape: pl.BlockSpec(shape, lambda i, loc: (0,) * len(shape))
    grid_spec = pltpu.PrefetchScalarGridSpec(
        num_scalar_prefetch=1,
        grid=(owners // per,),
        in_specs=[
            full((stored, plen, hd)),
            full((stored, plen, hd)),
            full((owners, hd)),
            full((owners, hd)),
        ],
        out_specs=pl.BlockSpec((per, 2, plen, hd), lambda i, loc: (i, 0, 0, 0)),
    )
    return pl.pallas_call(
        send_kernel,
        grid_spec=grid_spec,
        out_shape=jax.ShapeDtypeStruct((owners, 2, plen, hd), jnp.bfloat16),
        compiler_params=pltpu.CompilerParams(dimension_semantics=("arbitrary",)),
        cost_estimate=pl.CostEstimate(
            flops=4 * owners * plen * hd, transcendentals=0,
            bytes_accessed=owners * plen * hd * 2 * 2 + 2 * passage_keys.size * 2,
        ),
    )(loc, passage_keys, passage_values, cos_full, sin_full)


def block_kernel(tab_ref, remap_ref, q_ref, kv_ref, m_in, l_in, a_in, m_ref, l_ref, a_ref):
    o = pl.program_id(0)

    @pl.when(o == 0)
    def _():
        m_ref[...] = m_in[...]
        l_ref[...] = l_in[...]
        a_ref[...] = a_in[...]

    qi = tab_ref[o]

    @pl.when(qi >= 0)
    def _():
        q = q_ref[qi]
        k = kv_ref[0, 0]
        v = kv_ref[0, 1]
        s = lax.dot_general(
            q, k, (((1,), (1,)), ((), ())), preferred_element_type=jnp.float32
        ) * (HD ** (-0.5))
        m = jnp.max(s, axis=1, keepdims=True)
        e = jnp.exp(s - m)
        l = jnp.sum(e, axis=1, keepdims=True)
        p = jnp.dot(e.astype(jnp.bfloat16), v, preferred_element_type=jnp.float32)
        m_old = m_ref[qi]
        m_new = jnp.maximum(m_old, m)
        w_old = jnp.exp(m_old - m_new)
        w_new = jnp.exp(m - m_new)
        l_ref[qi] = w_old * l_ref[qi] + w_new * l
        a_ref[qi] = w_old * a_ref[qi] + w_new * p
        m_ref[qi] = m_new


def attend_chunk(tab, remap, query, recv, m, l, acc):
    owners = recv.shape[0]
    nq, rows, hd = query.shape
    plen = recv.shape[2]
    full3 = lambda shape: pl.BlockSpec(shape, lambda o, t, r: (0, 0, 0))
    grid_spec = pltpu.PrefetchScalarGridSpec(
        num_scalar_prefetch=2,
        grid=(owners,),
        in_specs=[
            full3((nq, rows, hd)),
            pl.BlockSpec((1, 2, plen, hd), lambda o, t, r: (r[o], 0, 0, 0)),
            full3((nq, rows, 1)),
            full3((nq, rows, 1)),
            full3((nq, rows, hd)),
        ],
        out_specs=[full3((nq, rows, 1)), full3((nq, rows, 1)), full3((nq, rows, hd))],
    )
    flops = 4 * nq * rows * plen * hd * owners // 2
    return pl.pallas_call(
        block_kernel,
        grid_spec=grid_spec,
        out_shape=[
            jax.ShapeDtypeStruct(m.shape, jnp.float32),
            jax.ShapeDtypeStruct(l.shape, jnp.float32),
            jax.ShapeDtypeStruct(acc.shape, jnp.float32),
        ],
        input_output_aliases={4: 0, 5: 1, 6: 2},
        compiler_params=pltpu.CompilerParams(
            dimension_semantics=("arbitrary",), vmem_limit_bytes=48 * 1024 * 1024
        ),
        cost_estimate=pl.CostEstimate(
            flops=flops,
            transcendentals=nq * rows * plen * owners // 2,
            bytes_accessed=recv.size * 2 + 2 * acc.size * 4,
        ),
    )(tab, remap, query, recv, m, l, acc)


def per_device(
    questions, w_query, w_key, w_value, passage_keys, passage_values, passage_ids, slot_order
):
    kv_heads = w_key.shape[1] // HD
    q_heads = w_query.shape[1] // HD
    group = q_heads // kv_heads
    tok_rows = questions.shape[0]
    count = tok_rows // QLEN
    stored = passage_keys.shape[0]
    owners_count = lax.axis_size("store")
    me = lax.axis_index("store")

    listed = count * RETR
    my_ids = passage_ids.reshape(-1)
    my_pos = slot_order.reshape(-1)
    my_owner = my_ids // stored
    onehot = (my_owner[:, None] == jnp.arange(owners_count, dtype=jnp.int32)[None, :]).astype(
        jnp.int32
    )
    before = jnp.cumsum(onehot, axis=0) - onehot
    my_rank = jnp.sum(before * onehot, axis=1)
    hits = [onehot * (my_rank == c).astype(jnp.int32)[:, None] for c in range(CAP)]

    request = jnp.stack(
        [
            jnp.stack(
                [jnp.sum(h * (my_ids % stored)[:, None], axis=0),
                 jnp.sum(h * my_pos[:, None], axis=0)],
                axis=1,
            )
            for h in hits
        ],
        axis=1,
    )
    incoming = lax.all_to_all(request, "store", split_axis=0, concat_axis=0, tiled=True)

    sends = []
    for c in range(CAP):
        loc = incoming[:, c, 0]
        pos = incoming[:, c, 1]
        cs, sn = angles((pos * PLEN).astype(jnp.float32))
        cos_full = jnp.concatenate([cs, cs], axis=-1)
        sin_full = jnp.concatenate([-sn, sn], axis=-1)
        sends.append(build_send(loc, cos_full, sin_full, passage_keys, passage_values))

    recvs = [
        lax.all_to_all(s, "store", split_axis=0, concat_axis=0, tiled=True) for s in sends
    ]

    piece = lax.all_gather(questions, "tensor", axis=1, tiled=True)
    qf = jnp.dot(piece, w_query, preferred_element_type=jnp.float32)
    kf = jnp.dot(piece, w_key, preferred_element_type=jnp.float32)
    vf = jnp.dot(piece, w_value, preferred_element_type=jnp.float32)
    qpos = (RETR * PLEN + jnp.arange(QLEN)).astype(jnp.float32)
    cosine, sine = angles(qpos)
    cosine = cosine[None, :, None, :]
    sine = sine[None, :, None, :]
    query = rotate(qf.reshape(count, QLEN, q_heads, HD), cosine, sine).astype(jnp.bfloat16)
    self_key = rotate(kf.reshape(count, QLEN, kv_heads, HD), cosine, sine).astype(jnp.bfloat16)
    self_key = self_key.reshape(count, QLEN, HD)
    self_value = vf.astype(jnp.bfloat16).reshape(count, QLEN, HD)
    query = jnp.transpose(query, (0, 2, 1, 3))

    scale = HD ** (-0.5)
    own = jnp.einsum("qhtd,qud->qhtu", query, self_key, preferred_element_type=jnp.float32) * scale
    causal = jnp.arange(QLEN)[:, None] >= jnp.arange(QLEN)[None, :]
    own = jnp.where(causal, own, -1e30)
    own_peak = jnp.max(own, axis=-1, keepdims=True)
    own_expo = jnp.where(causal, jnp.exp(own - own_peak), 0.0)
    own_total = jnp.sum(own_expo, axis=-1, keepdims=True)
    own_part = jnp.einsum(
        "qhtu,qud->qhtd", own_expo.astype(jnp.bfloat16), self_value,
        preferred_element_type=jnp.float32,
    )
    rows = q_heads * QLEN
    m = own_peak.reshape(count, rows, 1)
    l = own_total.reshape(count, rows, 1)
    acc = own_part.reshape(count, rows, HD)
    qflat = query.reshape(count, rows, HD)

    qidx = jnp.arange(listed, dtype=jnp.int32) // RETR
    slots = jnp.arange(owners_count, dtype=jnp.int32)
    for c in range(CAP):
        hit = hits[c]
        valid = jnp.sum(hit, axis=0)
        tab = jnp.sum(hit * qidx[:, None], axis=0) + valid - 1
        remap = lax.cummax(jnp.where(valid > 0, slots, 0), axis=0)
        m, l, acc = attend_chunk(tab, remap, qflat, recvs[c], m, l, acc)

    ctx = (acc / l).reshape(count, q_heads, QLEN, HD)
    ctx = jnp.transpose(ctx, (0, 2, 1, 3)).reshape(tok_rows, q_heads * HD)
    return ctx.astype(jnp.bfloat16)


def solution(mesh):
    in_specs = (
        P("store", "tensor"),
        P(None, "tensor"),
        P(None, "tensor"),
        P(None, "tensor"),
        P("store", None, "tensor"),
        P("store", None, "tensor"),
        P("store", None),
        P("store", None),
    )
    out_specs = P("store", "tensor")
    return jax.shard_map(
        per_device, mesh=mesh, in_specs=in_specs, out_specs=out_specs, check_vma=False
    )
```

```python
import functools

import jax
import jax.numpy as jnp
from jax import lax
from jax.experimental import pallas as pl
from jax.experimental.pallas import tpu as pltpu
from jax.sharding import PartitionSpec as P

HD = 128
QLEN = 128
PLEN = 512
RETR = 16
CAP = 2


def angles(positions):
    freqs = 500000.0 ** (-(jnp.arange(HD // 2, dtype=jnp.float32) * 2.0) / HD)
    turned = positions[..., None] * freqs
    return (jnp.cos(turned), jnp.sin(turned))


def rotate(values, cosine, sine):
    half = values.shape[-1] // 2
    first = values[..., :half]
    second = values[..., half:]
    return jnp.concatenate(
        [first * cosine - second * sine, second * cosine + first * sine], axis=-1
    )


def send_kernel(loc_ref, k_ref, v_ref, c_ref, s_ref, out_ref):
    per = out_ref.shape[0]
    base = pl.program_id(0) * per

    def body(j, carry):
        loc = loc_ref[base + j]
        k = k_ref[loc].astype(jnp.float32)
        turned = pltpu.roll(k, k.shape[-1] // 2, 1)
        cos_row = c_ref[pl.ds(base + j, 1), :]
        sin_row = s_ref[pl.ds(base + j, 1), :]
        out_ref[j, 0] = (k * cos_row + turned * sin_row).astype(jnp.bfloat16)
        out_ref[j, 1] = v_ref[loc]
        return carry

    lax.fori_loop(0, per, body, 0)


def build_send(loc, cos_full, sin_full, passage_keys, passage_values):
    owners = loc.shape[0]
    stored, plen, hd = passage_keys.shape
    per = 4
    full = lambda shape: pl.BlockSpec(shape, lambda i, loc: (0,) * len(shape))
    grid_spec = pltpu.PrefetchScalarGridSpec(
        num_scalar_prefetch=1,
        grid=(owners // per,),
        in_specs=[
            full((stored, plen, hd)),
            full((stored, plen, hd)),
            full((owners, hd)),
            full((owners, hd)),
        ],
        out_specs=pl.BlockSpec((per, 2, plen, hd), lambda i, loc: (i, 0, 0, 0)),
    )
    return pl.pallas_call(
        send_kernel,
        grid_spec=grid_spec,
        out_shape=jax.ShapeDtypeStruct((owners, 2, plen, hd), jnp.bfloat16),
        compiler_params=pltpu.CompilerParams(dimension_semantics=("arbitrary",)),
        cost_estimate=pl.CostEstimate(
            flops=4 * owners * plen * hd, transcendentals=0,
            bytes_accessed=owners * plen * hd * 2 * 2 + 2 * passage_keys.size * 2,
        ),
    )(loc, passage_keys, passage_values, cos_full, sin_full)


ROW_TILE = 256
LOG2E = 1.4426950408889634


def block_kernel(tab_ref, remap_ref, q_ref, kv_ref, m_in, l_in, a_in, m_ref, l_ref, a_ref, *out):
    o = pl.program_id(0)

    @pl.when(o == 0)
    def _():
        m_ref[...] = m_in[...]
        l_ref[...] = l_in[...]
        a_ref[...] = a_in[...]

    qi = tab_ref[o]

    @pl.when(qi >= 0)
    def _():
        k = kv_ref[0, 0]
        v = kv_ref[0, 1]
        for r0 in range(0, q_ref.shape[1], ROW_TILE):
            rows = pl.ds(r0, ROW_TILE)
            q = q_ref[qi, rows, :]
            s = lax.dot_general(
                q, k, (((1,), (1,)), ((), ())), preferred_element_type=jnp.float32
            )
            m = jnp.max(s, axis=1, keepdims=True)
            c = (HD ** (-0.5)) * LOG2E
            e = jnp.exp2(s * c - m * c)
            l = jnp.sum(e, axis=1, keepdims=True)
            p = jnp.dot(e.astype(jnp.bfloat16), v, preferred_element_type=jnp.float32)
            m = m * (HD ** (-0.5))
            m_old = m_ref[qi, rows, :]
            m_new = jnp.maximum(m_old, m)
            w_old = jnp.exp(m_old - m_new)
            w_new = jnp.exp(m - m_new)
            l_ref[qi, rows, :] = w_old * l_ref[qi, rows, :] + w_new * l
            a_ref[qi, rows, :] = w_old * a_ref[qi, rows, :] + w_new * p
            m_ref[qi, rows, :] = m_new

    if out:
        (ctx_ref,) = out

        @pl.when(o == pl.num_programs(0) - 1)
        def _():
            qlen = ctx_ref.shape[0] // q_ref.shape[0]
            for j in range(q_ref.shape[0]):
                for h in range(q_ref.shape[1] // qlen):
                    rows = pl.ds(h * qlen, qlen)
                    ctx_ref[pl.ds(j * qlen, qlen), pl.ds(h * HD, HD)] = (
                        a_ref[j, rows, :] / l_ref[j, rows, :]
                    ).astype(ctx_ref.dtype)


def attend_chunk(tab, remap, query, recv, m, l, acc, final=False):
    owners = recv.shape[0]
    nq, rows, hd = query.shape
    plen = recv.shape[2]
    full3 = lambda shape: pl.BlockSpec(shape, lambda o, t, r: (0, 0, 0))
    grid_spec = pltpu.PrefetchScalarGridSpec(
        num_scalar_prefetch=2,
        grid=(owners,),
        in_specs=[
            full3((nq, rows, hd)),
            pl.BlockSpec((1, 2, plen, hd), lambda o, t, r: (r[o], 0, 0, 0)),
            full3((nq, rows, 1)),
            full3((nq, rows, 1)),
            full3((nq, rows, hd)),
        ],
        out_specs=[full3((nq, rows, 1)), full3((nq, rows, 1)), full3((nq, rows, hd))]
        + ([pl.BlockSpec((nq * QLEN, rows // QLEN * hd), lambda o, t, r: (0, 0))] if final else []),
    )
    flops = 4 * nq * rows * plen * hd * owners // 2
    return pl.pallas_call(
        block_kernel,
        grid_spec=grid_spec,
        out_shape=[
            jax.ShapeDtypeStruct(m.shape, jnp.float32),
            jax.ShapeDtypeStruct(l.shape, jnp.float32),
            jax.ShapeDtypeStruct(acc.shape, jnp.float32),
        ]
        + ([jax.ShapeDtypeStruct((nq * QLEN, rows // QLEN * hd), jnp.bfloat16)] if final else []),
        input_output_aliases={4: 0, 5: 1, 6: 2},
        compiler_params=pltpu.CompilerParams(
            dimension_semantics=("arbitrary",), vmem_limit_bytes=48 * 1024 * 1024
        ),
        cost_estimate=pl.CostEstimate(
            flops=flops,
            transcendentals=nq * rows * plen * owners // 2,
            bytes_accessed=recv.size * 2 + 2 * acc.size * 4,
        ),
    )(tab, remap, query, recv, m, l, acc)


def per_device(
    questions, w_query, w_key, w_value, passage_keys, passage_values, passage_ids, slot_order
):
    kv_heads = w_key.shape[1] // HD
    q_heads = w_query.shape[1] // HD
    group = q_heads // kv_heads
    tok_rows = questions.shape[0]
    count = tok_rows // QLEN
    stored = passage_keys.shape[0]
    owners_count = lax.axis_size("store")
    me = lax.axis_index("store")

    listed = count * RETR
    my_ids = passage_ids.reshape(-1)
    my_pos = slot_order.reshape(-1)
    my_owner = my_ids // stored
    onehot = (my_owner[:, None] == jnp.arange(owners_count, dtype=jnp.int32)[None, :]).astype(
        jnp.int32
    )
    before = jnp.cumsum(onehot, axis=0) - onehot
    my_rank = jnp.sum(before * onehot, axis=1)
    hits = [onehot * (my_rank == c).astype(jnp.int32)[:, None] for c in range(CAP)]

    request = jnp.stack(
        [
            jnp.stack(
                [jnp.sum(h * (my_ids % stored)[:, None], axis=0),
                 jnp.sum(h * my_pos[:, None], axis=0)],
                axis=1,
            )
            for h in hits
        ],
        axis=1,
    )
    incoming = lax.all_to_all(request, "store", split_axis=0, concat_axis=0, tiled=True)

    sends = []
    for c in range(CAP):
        loc = incoming[:, c, 0]
        pos = incoming[:, c, 1]
        cs, sn = angles((pos * PLEN).astype(jnp.float32))
        cos_full = jnp.concatenate([cs, cs], axis=-1)
        sin_full = jnp.concatenate([-sn, sn], axis=-1)
        sends.append(build_send(loc, cos_full, sin_full, passage_keys, passage_values))

    recvs = [
        lax.all_to_all(s, "store", split_axis=0, concat_axis=0, tiled=True) for s in sends
    ]

    piece = lax.all_gather(questions, "tensor", axis=1, tiled=True)
    qf = jnp.dot(piece, w_query, preferred_element_type=jnp.float32)
    kf = jnp.dot(piece, w_key, preferred_element_type=jnp.float32)
    vf = jnp.dot(piece, w_value, preferred_element_type=jnp.float32)
    qpos = (RETR * PLEN + jnp.arange(QLEN)).astype(jnp.float32)
    cosine, sine = angles(qpos)
    cosine = cosine[None, :, None, :]
    sine = sine[None, :, None, :]
    query = rotate(qf.reshape(count, QLEN, q_heads, HD), cosine, sine).astype(jnp.bfloat16)
    self_key = rotate(kf.reshape(count, QLEN, kv_heads, HD), cosine, sine).astype(jnp.bfloat16)
    self_key = self_key.reshape(count, QLEN, HD)
    self_value = vf.astype(jnp.bfloat16).reshape(count, QLEN, HD)
    query = jnp.transpose(query, (0, 2, 1, 3))

    scale = HD ** (-0.5)
    own = jnp.einsum("qhtd,qud->qhtu", query, self_key, preferred_element_type=jnp.float32) * scale
    causal = jnp.arange(QLEN)[:, None] >= jnp.arange(QLEN)[None, :]
    own = jnp.where(causal, own, -1e30)
    own_peak = jnp.max(own, axis=-1, keepdims=True)
    own_expo = jnp.where(causal, jnp.exp(own - own_peak), 0.0)
    own_total = jnp.sum(own_expo, axis=-1, keepdims=True)
    own_part = jnp.einsum(
        "qhtu,qud->qhtd", own_expo.astype(jnp.bfloat16), self_value,
        preferred_element_type=jnp.float32,
    )
    rows = q_heads * QLEN
    m = own_peak.reshape(count, rows, 1)
    l = own_total.reshape(count, rows, 1)
    acc = own_part.reshape(count, rows, HD)
    qflat = query.reshape(count, rows, HD)

    qidx = jnp.arange(listed, dtype=jnp.int32) // RETR
    slots = jnp.arange(owners_count, dtype=jnp.int32)
    for c in range(CAP):
        hit = hits[c]
        valid = jnp.sum(hit, axis=0)
        tab = jnp.sum(hit * qidx[:, None], axis=0) + valid - 1
        remap = lax.cummax(jnp.where(valid > 0, slots, 0), axis=0)
        outs = attend_chunk(tab, remap, qflat, recvs[c], m, l, acc, final=c == CAP - 1)
        m, l, acc = outs[:3]
    return outs[3]


def solution(mesh):
    in_specs = (
        P("store", "tensor"),
        P(None, "tensor"),
        P(None, "tensor"),
        P(None, "tensor"),
        P("store", None, "tensor"),
        P("store", None, "tensor"),
        P("store", None),
        P("store", None),
    )
    out_specs = P("store", "tensor")
    return jax.shard_map(
        per_device, mesh=mesh, in_specs=in_specs, out_specs=out_specs, check_vma=False
    )
```

```python
import functools

import jax
import jax.numpy as jnp
from jax import lax
from jax.experimental import pallas as pl
from jax.experimental.pallas import tpu as pltpu
from jax.sharding import PartitionSpec as P

HD = 128
QLEN = 128
PLEN = 512
RETR = 16
CAP = 2


def angles(positions):
    freqs = 500000.0 ** (-(jnp.arange(HD // 2, dtype=jnp.float32) * 2.0) / HD)
    turned = positions[..., None] * freqs
    return (jnp.cos(turned), jnp.sin(turned))


def rotate(values, cosine, sine):
    half = values.shape[-1] // 2
    first = values[..., :half]
    second = values[..., half:]
    return jnp.concatenate(
        [first * cosine - second * sine, second * cosine + first * sine], axis=-1
    )


def send_kernel(loc_ref, k_ref, v_ref, c_ref, s_ref, out_ref):
    per = out_ref.shape[0]
    base = pl.program_id(0) * per

    def body(j, carry):
        loc = loc_ref[base + j]
        k = k_ref[loc].astype(jnp.float32)
        turned = pltpu.roll(k, k.shape[-1] // 2, 1)
        cos_row = c_ref[pl.ds(base + j, 1), :]
        sin_row = s_ref[pl.ds(base + j, 1), :]
        out_ref[j, 0] = (k * cos_row + turned * sin_row).astype(jnp.bfloat16)
        out_ref[j, 1] = v_ref[loc]
        return carry

    lax.fori_loop(0, per, body, 0)


def build_send(loc, cos_full, sin_full, passage_keys, passage_values):
    owners = loc.shape[0]
    stored, plen, hd = passage_keys.shape
    per = 8
    full = lambda shape: pl.BlockSpec(shape, lambda i, loc: (0,) * len(shape))
    grid_spec = pltpu.PrefetchScalarGridSpec(
        num_scalar_prefetch=1,
        grid=(owners // per,),
        in_specs=[
            full((stored, plen, hd)),
            full((stored, plen, hd)),
            full((owners, hd)),
            full((owners, hd)),
        ],
        out_specs=pl.BlockSpec((per, 2, plen, hd), lambda i, loc: (i, 0, 0, 0)),
    )
    return pl.pallas_call(
        send_kernel,
        grid_spec=grid_spec,
        out_shape=jax.ShapeDtypeStruct((owners, 2, plen, hd), jnp.bfloat16),
        compiler_params=pltpu.CompilerParams(dimension_semantics=("arbitrary",)),
        cost_estimate=pl.CostEstimate(
            flops=4 * owners * plen * hd, transcendentals=0,
            bytes_accessed=owners * plen * hd * 2 * 2 + 2 * passage_keys.size * 2,
        ),
    )(loc, passage_keys, passage_values, cos_full, sin_full)


ROW_TILE = 256
LOG2E = 1.4426950408889634


def block_kernel(tab_ref, remap_ref, q_ref, kv_ref, m_in, l_in, a_in, m_ref, l_ref, a_ref):
    o = pl.program_id(0)

    @pl.when(o == 0)
    def _():
        m_ref[...] = m_in[...]
        l_ref[...] = l_in[...]
        a_ref[...] = a_in[...]

    qi = tab_ref[o]

    @pl.when(qi >= 0)
    def _():
        k = kv_ref[0, 0]
        v = kv_ref[0, 1]
        for r0 in range(0, q_ref.shape[1], ROW_TILE):
            rows = pl.ds(r0, ROW_TILE)
            q = q_ref[qi, rows, :]
            s = lax.dot_general(
                q, k, (((1,), (1,)), ((), ())), preferred_element_type=jnp.float32
            )
            m = jnp.max(s, axis=1, keepdims=True)
            c = (HD ** (-0.5)) * LOG2E
            e = jnp.exp2(s * c - m * c)
            l = jnp.sum(e, axis=1, keepdims=True)
            p = jnp.dot(e.astype(jnp.bfloat16), v, preferred_element_type=jnp.float32)
            m = m * (HD ** (-0.5))
            m_old = m_ref[qi, rows, :]
            m_new = jnp.maximum(m_old, m)
            w_old = jnp.exp(m_old - m_new)
            w_new = jnp.exp(m - m_new)
            l_ref[qi, rows, :] = w_old * l_ref[qi, rows, :] + w_new * l
            a_ref[qi, rows, :] = w_old * a_ref[qi, rows, :] + w_new * p
            m_ref[qi, rows, :] = m_new


def attend_chunk(tab, remap, query, recv, m, l, acc):
    owners = recv.shape[0]
    nq, rows, hd = query.shape
    plen = recv.shape[2]
    full3 = lambda shape: pl.BlockSpec(shape, lambda o, t, r: (0, 0, 0))
    grid_spec = pltpu.PrefetchScalarGridSpec(
        num_scalar_prefetch=2,
        grid=(owners,),
        in_specs=[
            full3((nq, rows, hd)),
            pl.BlockSpec((1, 2, plen, hd), lambda o, t, r: (r[o], 0, 0, 0)),
            full3((nq, rows, 1)),
            full3((nq, rows, 1)),
            full3((nq, rows, hd)),
        ],
        out_specs=[full3((nq, rows, 1)), full3((nq, rows, 1)), full3((nq, rows, hd))],
    )
    flops = 4 * nq * rows * plen * hd * owners // 2
    return pl.pallas_call(
        block_kernel,
        grid_spec=grid_spec,
        out_shape=[
            jax.ShapeDtypeStruct(m.shape, jnp.float32),
            jax.ShapeDtypeStruct(l.shape, jnp.float32),
            jax.ShapeDtypeStruct(acc.shape, jnp.float32),
        ],
        input_output_aliases={4: 0, 5: 1, 6: 2},
        compiler_params=pltpu.CompilerParams(
            dimension_semantics=("arbitrary",), vmem_limit_bytes=48 * 1024 * 1024
        ),
        cost_estimate=pl.CostEstimate(
            flops=flops,
            transcendentals=nq * rows * plen * owners // 2,
            bytes_accessed=recv.size * 2 + 2 * acc.size * 4,
        ),
    )(tab, remap, query, recv, m, l, acc)


def per_device(
    questions, w_query, w_key, w_value, passage_keys, passage_values, passage_ids, slot_order
):
    kv_heads = w_key.shape[1] // HD
    q_heads = w_query.shape[1] // HD
    group = q_heads // kv_heads
    tok_rows = questions.shape[0]
    count = tok_rows // QLEN
    stored = passage_keys.shape[0]
    owners_count = lax.axis_size("store")
    me = lax.axis_index("store")

    listed = count * RETR
    my_ids = passage_ids.reshape(-1)
    my_pos = slot_order.reshape(-1)
    my_owner = my_ids // stored
    onehot = (my_owner[:, None] == jnp.arange(owners_count, dtype=jnp.int32)[None, :]).astype(
        jnp.int32
    )
    before = jnp.cumsum(onehot, axis=0) - onehot
    my_rank = jnp.sum(before * onehot, axis=1)
    hits = [onehot * (my_rank == c).astype(jnp.int32)[:, None] for c in range(CAP)]

    request = jnp.stack(
        [
            jnp.stack(
                [jnp.sum(h * (my_ids % stored)[:, None], axis=0),
                 jnp.sum(h * my_pos[:, None], axis=0)],
                axis=1,
            )
            for h in hits
        ],
        axis=1,
    )
    incoming = lax.all_to_all(request, "store", split_axis=0, concat_axis=0, tiled=True)

    sends = []
    for c in range(CAP):
        loc = incoming[:, c, 0]
        pos = incoming[:, c, 1]
        cs, sn = angles((pos * PLEN).astype(jnp.float32))
        cos_full = jnp.concatenate([cs, cs], axis=-1)
        sin_full = jnp.concatenate([-sn, sn], axis=-1)
        sends.append(build_send(loc, cos_full, sin_full, passage_keys, passage_values))

    recvs = [
        lax.all_to_all(s, "store", split_axis=0, concat_axis=0, tiled=True) for s in sends
    ]

    piece = lax.all_gather(questions, "tensor", axis=1, tiled=True)
    qf = jnp.dot(piece, w_query, preferred_element_type=jnp.float32)
    kf = jnp.dot(piece, w_key, preferred_element_type=jnp.float32)
    vf = jnp.dot(piece, w_value, preferred_element_type=jnp.float32)
    qpos = (RETR * PLEN + jnp.arange(QLEN)).astype(jnp.float32)
    cosine, sine = angles(qpos)
    cosine = cosine[None, :, None, :]
    sine = sine[None, :, None, :]
    query = rotate(qf.reshape(count, QLEN, q_heads, HD), cosine, sine).astype(jnp.bfloat16)
    self_key = rotate(kf.reshape(count, QLEN, kv_heads, HD), cosine, sine).astype(jnp.bfloat16)
    self_key = self_key.reshape(count, QLEN, HD)
    self_value = vf.astype(jnp.bfloat16).reshape(count, QLEN, HD)
    query = jnp.transpose(query, (0, 2, 1, 3))

    scale = HD ** (-0.5)
    own = jnp.einsum("qhtd,qud->qhtu", query, self_key, preferred_element_type=jnp.float32) * scale
    causal = jnp.arange(QLEN)[:, None] >= jnp.arange(QLEN)[None, :]
    own = jnp.where(causal, own, -1e30)
    own_peak = jnp.max(own, axis=-1, keepdims=True)
    own_expo = jnp.where(causal, jnp.exp(own - own_peak), 0.0)
    own_total = jnp.sum(own_expo, axis=-1, keepdims=True)
    own_part = jnp.einsum(
        "qhtu,qud->qhtd", own_expo.astype(jnp.bfloat16), self_value,
        preferred_element_type=jnp.float32,
    )
    rows = q_heads * QLEN
    m = own_peak.reshape(count, rows, 1)
    l = own_total.reshape(count, rows, 1)
    acc = own_part.reshape(count, rows, HD)
    qflat = query.reshape(count, rows, HD)

    qidx = jnp.arange(listed, dtype=jnp.int32) // RETR
    slots = jnp.arange(owners_count, dtype=jnp.int32)
    for c in range(CAP):
        hit = hits[c]
        valid = jnp.sum(hit, axis=0)
        tab = jnp.sum(hit * qidx[:, None], axis=0) + valid - 1
        remap = lax.cummax(jnp.where(valid > 0, slots, 0), axis=0)
        m, l, acc = attend_chunk(tab, remap, qflat, recvs[c], m, l, acc)

    ctx = (acc / l).reshape(count, q_heads, QLEN, HD)
    ctx = jnp.transpose(ctx, (0, 2, 1, 3)).reshape(tok_rows, q_heads * HD)
    return ctx.astype(jnp.bfloat16)


def solution(mesh):
    in_specs = (
        P("store", "tensor"),
        P(None, "tensor"),
        P(None, "tensor"),
        P(None, "tensor"),
        P("store", None, "tensor"),
        P("store", None, "tensor"),
        P("store", None),
        P("store", None),
    )
    out_specs = P("store", "tensor")
    return jax.shard_map(
        per_device, mesh=mesh, in_specs=in_specs, out_specs=out_specs, check_vma=False
    )
```

```python
import functools

import jax
import jax.numpy as jnp
from jax import lax
from jax.experimental import pallas as pl
from jax.experimental.pallas import tpu as pltpu
from jax.sharding import PartitionSpec as P

HD = 128
QLEN = 128
PLEN = 512
RETR = 16
CAP = 2


def angles(positions):
    freqs = 500000.0 ** (-(jnp.arange(HD // 2, dtype=jnp.float32) * 2.0) / HD)
    turned = positions[..., None] * freqs
    return (jnp.cos(turned), jnp.sin(turned))


def rotate(values, cosine, sine):
    half = values.shape[-1] // 2
    first = values[..., :half]
    second = values[..., half:]
    return jnp.concatenate(
        [first * cosine - second * sine, second * cosine + first * sine], axis=-1
    )


def send_kernel(loc_ref, k_ref, v_ref, c_ref, s_ref, out_ref):
    per = out_ref.shape[0]
    base = pl.program_id(0) * per

    def body(j, carry):
        loc = loc_ref[base + j]
        k = k_ref[loc].astype(jnp.float32)
        turned = pltpu.roll(k, k.shape[-1] // 2, 1)
        cos_row = c_ref[pl.ds(base + j, 1), :]
        sin_row = s_ref[pl.ds(base + j, 1), :]
        out_ref[j, 0] = (k * cos_row + turned * sin_row).astype(jnp.bfloat16)
        out_ref[j, 1] = v_ref[loc]
        return carry

    lax.fori_loop(0, per, body, 0)


def build_send(loc, cos_full, sin_full, passage_keys, passage_values):
    owners = loc.shape[0]
    stored, plen, hd = passage_keys.shape
    per = 8
    full = lambda shape: pl.BlockSpec(shape, lambda i, loc: (0,) * len(shape))
    grid_spec = pltpu.PrefetchScalarGridSpec(
        num_scalar_prefetch=1,
        grid=(owners // per,),
        in_specs=[
            full((stored, plen, hd)),
            full((stored, plen, hd)),
            full((owners, hd)),
            full((owners, hd)),
        ],
        out_specs=pl.BlockSpec((per, 2, plen, hd), lambda i, loc: (i, 0, 0, 0)),
    )
    return pl.pallas_call(
        send_kernel,
        grid_spec=grid_spec,
        out_shape=jax.ShapeDtypeStruct((owners, 2, plen, hd), jnp.bfloat16),
        compiler_params=pltpu.CompilerParams(dimension_semantics=("arbitrary",)),
        cost_estimate=pl.CostEstimate(
            flops=4 * owners * plen * hd, transcendentals=0,
            bytes_accessed=owners * plen * hd * 2 * 2 + 2 * passage_keys.size * 2,
        ),
    )(loc, passage_keys, passage_values, cos_full, sin_full)


ROW_TILE = 1024
LOG2E = 1.4426950408889634


def block_kernel(tab_ref, remap_ref, q_ref, kv_ref, m_in, l_in, a_in, m_ref, l_ref, a_ref):
    o = pl.program_id(0)

    @pl.when(o == 0)
    def _():
        m_ref[...] = m_in[...]
        l_ref[...] = l_in[...]
        a_ref[...] = a_in[...]

    qi = tab_ref[o]

    @pl.when(qi >= 0)
    def _():
        k = kv_ref[0, 0]
        v = kv_ref[0, 1]
        c = (HD ** (-0.5)) * LOG2E
        for r0 in range(0, q_ref.shape[2], ROW_TILE):
            cols = pl.ds(r0, ROW_TILE)
            s = jnp.dot(k, q_ref[qi, :, cols], preferred_element_type=jnp.float32)
            m = jnp.max(s, axis=0, keepdims=True)
            e = jnp.exp2(s * c - m * c)
            l = jnp.sum(e, axis=0, keepdims=True)
            p = lax.dot_general(
                v, e.astype(jnp.bfloat16), (((0,), (0,)), ((), ())),
                preferred_element_type=jnp.float32,
            )
            m = m * (HD ** (-0.5))
            m_old = m_ref[qi, :, cols]
            m_new = jnp.maximum(m_old, m)
            w_old = jnp.exp(m_old - m_new)
            w_new = jnp.exp(m - m_new)
            l_ref[qi, :, cols] = w_old * l_ref[qi, :, cols] + w_new * l
            a_ref[qi, :, cols] = w_old * a_ref[qi, :, cols] + w_new * p
            m_ref[qi, :, cols] = m_new


def attend_chunk(tab, remap, query_t, recv, m, l, acc):
    owners = recv.shape[0]
    nq, hd, rows = query_t.shape
    plen = recv.shape[2]
    full3 = lambda shape: pl.BlockSpec(shape, lambda o, t, r: (0, 0, 0))
    grid_spec = pltpu.PrefetchScalarGridSpec(
        num_scalar_prefetch=2,
        grid=(owners,),
        in_specs=[
            full3((nq, hd, rows)),
            pl.BlockSpec((1, 2, plen, hd), lambda o, t, r: (r[o], 0, 0, 0)),
            full3((nq, 1, rows)),
            full3((nq, 1, rows)),
            full3((nq, hd, rows)),
        ],
        out_specs=[full3((nq, 1, rows)), full3((nq, 1, rows)), full3((nq, hd, rows))],
    )
    flops = 4 * nq * rows * plen * hd * owners // 2
    return pl.pallas_call(
        block_kernel,
        grid_spec=grid_spec,
        out_shape=[
            jax.ShapeDtypeStruct(m.shape, jnp.float32),
            jax.ShapeDtypeStruct(l.shape, jnp.float32),
            jax.ShapeDtypeStruct(acc.shape, jnp.float32),
        ],
        input_output_aliases={4: 0, 5: 1, 6: 2},
        compiler_params=pltpu.CompilerParams(
            dimension_semantics=("arbitrary",), vmem_limit_bytes=48 * 1024 * 1024
        ),
        cost_estimate=pl.CostEstimate(
            flops=flops,
            transcendentals=nq * rows * plen * owners // 2,
            bytes_accessed=recv.size * 2 + 2 * acc.size * 4,
        ),
    )(tab, remap, query_t, recv, m, l, acc)


def per_device(
    questions, w_query, w_key, w_value, passage_keys, passage_values, passage_ids, slot_order
):
    kv_heads = w_key.shape[1] // HD
    q_heads = w_query.shape[1] // HD
    group = q_heads // kv_heads
    tok_rows = questions.shape[0]
    count = tok_rows // QLEN
    stored = passage_keys.shape[0]
    owners_count = lax.axis_size("store")
    me = lax.axis_index("store")

    listed = count * RETR
    my_ids = passage_ids.reshape(-1)
    my_pos = slot_order.reshape(-1)
    my_owner = my_ids // stored
    onehot = (my_owner[:, None] == jnp.arange(owners_count, dtype=jnp.int32)[None, :]).astype(
        jnp.int32
    )
    before = jnp.cumsum(onehot, axis=0) - onehot
    my_rank = jnp.sum(before * onehot, axis=1)
    hits = [onehot * (my_rank == c).astype(jnp.int32)[:, None] for c in range(CAP)]

    request = jnp.stack(
        [
            jnp.stack(
                [jnp.sum(h * (my_ids % stored)[:, None], axis=0),
                 jnp.sum(h * my_pos[:, None], axis=0)],
                axis=1,
            )
            for h in hits
        ],
        axis=1,
    )
    incoming = lax.all_to_all(request, "store", split_axis=0, concat_axis=0, tiled=True)

    sends = []
    for c in range(CAP):
        loc = incoming[:, c, 0]
        pos = incoming[:, c, 1]
        cs, sn = angles((pos * PLEN).astype(jnp.float32))
        cos_full = jnp.concatenate([cs, cs], axis=-1)
        sin_full = jnp.concatenate([-sn, sn], axis=-1)
        sends.append(build_send(loc, cos_full, sin_full, passage_keys, passage_values))

    recvs = [
        lax.all_to_all(s, "store", split_axis=0, concat_axis=0, tiled=True) for s in sends
    ]

    piece = lax.all_gather(questions, "tensor", axis=1, tiled=True)
    qf = jnp.dot(piece, w_query, preferred_element_type=jnp.float32)
    kf = jnp.dot(piece, w_key, preferred_element_type=jnp.float32)
    vf = jnp.dot(piece, w_value, preferred_element_type=jnp.float32)
    qpos = (RETR * PLEN + jnp.arange(QLEN)).astype(jnp.float32)
    cosine, sine = angles(qpos)
    cosine = cosine[None, :, None, :]
    sine = sine[None, :, None, :]
    query = rotate(qf.reshape(count, QLEN, q_heads, HD), cosine, sine).astype(jnp.bfloat16)
    self_key = rotate(kf.reshape(count, QLEN, kv_heads, HD), cosine, sine).astype(jnp.bfloat16)
    self_key = self_key.reshape(count, QLEN, HD)
    self_value = vf.astype(jnp.bfloat16).reshape(count, QLEN, HD)
    query = jnp.transpose(query, (0, 2, 1, 3))

    scale = HD ** (-0.5)
    own = jnp.einsum("qhtd,qud->qhtu", query, self_key, preferred_element_type=jnp.float32) * scale
    causal = jnp.arange(QLEN)[:, None] >= jnp.arange(QLEN)[None, :]
    own = jnp.where(causal, own, -1e30)
    own_peak = jnp.max(own, axis=-1, keepdims=True)
    own_expo = jnp.where(causal, jnp.exp(own - own_peak), 0.0)
    own_total = jnp.sum(own_expo, axis=-1, keepdims=True)
    own_part = jnp.einsum(
        "qhtu,qud->qhtd", own_expo.astype(jnp.bfloat16), self_value,
        preferred_element_type=jnp.float32,
    )
    rows = q_heads * QLEN
    m = own_peak.reshape(count, 1, rows)
    l = own_total.reshape(count, 1, rows)
    acc = jnp.transpose(own_part, (0, 3, 1, 2)).reshape(count, HD, rows)
    query_t = jnp.transpose(query, (0, 3, 1, 2)).reshape(count, HD, rows)

    qidx = jnp.arange(listed, dtype=jnp.int32) // RETR
    slots = jnp.arange(owners_count, dtype=jnp.int32)
    for c in range(CAP):
        hit = hits[c]
        valid = jnp.sum(hit, axis=0)
        tab = jnp.sum(hit * qidx[:, None], axis=0) + valid - 1
        remap = lax.cummax(jnp.where(valid > 0, slots, 0), axis=0)
        m, l, acc = attend_chunk(tab, remap, query_t, recvs[c], m, l, acc)

    ctx = (acc / l).reshape(count, HD, q_heads, QLEN)
    ctx = jnp.transpose(ctx, (0, 3, 2, 1)).reshape(tok_rows, q_heads * HD)
    return ctx.astype(jnp.bfloat16)


def solution(mesh):
    in_specs = (
        P("store", "tensor"),
        P(None, "tensor"),
        P(None, "tensor"),
        P(None, "tensor"),
        P("store", None, "tensor"),
        P("store", None, "tensor"),
        P("store", None),
        P("store", None),
    )
    out_specs = P("store", "tensor")
    return jax.shard_map(
        per_device, mesh=mesh, in_specs=in_specs, out_specs=out_specs, check_vma=False
    )
```

```python
import functools

import jax
import jax.numpy as jnp
from jax import lax
from jax.experimental import pallas as pl
from jax.experimental.pallas import tpu as pltpu
from jax.sharding import PartitionSpec as P

HD = 128
QLEN = 128
PLEN = 512
RETR = 16
CAP = 2


def angles(positions):
    freqs = 500000.0 ** (-(jnp.arange(HD // 2, dtype=jnp.float32) * 2.0) / HD)
    turned = positions[..., None] * freqs
    return (jnp.cos(turned), jnp.sin(turned))


def rotate(values, cosine, sine):
    half = values.shape[-1] // 2
    first = values[..., :half]
    second = values[..., half:]
    return jnp.concatenate(
        [first * cosine - second * sine, second * cosine + first * sine], axis=-1
    )


def send_kernel(loc_ref, k_ref, v_ref, c_ref, s_ref, out_ref):
    per = out_ref.shape[0]
    base = pl.program_id(0) * per

    def body(j, carry):
        loc = loc_ref[base + j]
        k = k_ref[loc].astype(jnp.float32)
        turned = pltpu.roll(k, k.shape[-1] // 2, 1)
        cos_row = c_ref[pl.ds(base + j, 1), :]
        sin_row = s_ref[pl.ds(base + j, 1), :]
        out_ref[j, 0] = (k * cos_row + turned * sin_row).astype(jnp.bfloat16)
        out_ref[j, 1] = v_ref[loc]
        return carry

    lax.fori_loop(0, per, body, 0)


def build_send(loc, cos_full, sin_full, passage_keys, passage_values):
    owners = loc.shape[0]
    stored, plen, hd = passage_keys.shape
    per = 8
    full = lambda shape: pl.BlockSpec(shape, lambda i, loc: (0,) * len(shape))
    grid_spec = pltpu.PrefetchScalarGridSpec(
        num_scalar_prefetch=1,
        grid=(owners // per,),
        in_specs=[
            full((stored, plen, hd)),
            full((stored, plen, hd)),
            full((owners, hd)),
            full((owners, hd)),
        ],
        out_specs=pl.BlockSpec((per, 2, plen, hd), lambda i, loc: (i, 0, 0, 0)),
    )
    return pl.pallas_call(
        send_kernel,
        grid_spec=grid_spec,
        out_shape=jax.ShapeDtypeStruct((owners, 2, plen, hd), jnp.bfloat16),
        compiler_params=pltpu.CompilerParams(dimension_semantics=("arbitrary",)),
        cost_estimate=pl.CostEstimate(
            flops=4 * owners * plen * hd, transcendentals=0,
            bytes_accessed=owners * plen * hd * 2 * 2 + 2 * passage_keys.size * 2,
        ),
    )(loc, passage_keys, passage_values, cos_full, sin_full)


ROW_TILE = 1024
LOG2E = 1.4426950408889634


def block_kernel(tab_ref, remap_ref, q_ref, kv_ref, m_in, l_in, a_in, m_ref, l_ref, a_ref):
    o = pl.program_id(0)

    @pl.when(o == 0)
    def _():
        m_ref[...] = m_in[...]
        l_ref[...] = l_in[...]
        a_ref[...] = a_in[...]

    qi = tab_ref[o]

    @pl.when(qi >= 0)
    def _():
        k = kv_ref[0, 0]
        v = kv_ref[0, 1]
        c = (HD ** (-0.5)) * LOG2E
        for r0 in range(0, q_ref.shape[2], ROW_TILE):
            cols = pl.ds(r0, ROW_TILE)
            s = jnp.dot(k, q_ref[qi, :, cols], preferred_element_type=jnp.float32)
            m = jnp.max(s, axis=0, keepdims=True)
            e = jnp.exp2(s * c - m * c)
            l = jnp.sum(e, axis=0, keepdims=True)
            p = lax.dot_general(
                v, e.astype(jnp.bfloat16), (((0,), (0,)), ((), ())),
                preferred_element_type=jnp.float32,
            )
            m = m * (HD ** (-0.5))
            m_old = m_ref[qi, :, cols]
            m_new = jnp.maximum(m_old, m)
            w_old = jnp.exp(m_old - m_new)
            w_new = jnp.exp(m - m_new)
            l_ref[qi, :, cols] = w_old * l_ref[qi, :, cols] + w_new * l
            a_ref[qi, :, cols] = w_old * a_ref[qi, :, cols] + w_new * p
            m_ref[qi, :, cols] = m_new


def attend_chunk(tab, remap, query_t, recv, m, l, acc):
    owners = recv.shape[0]
    nq, hd, rows = query_t.shape
    plen = recv.shape[2]
    full3 = lambda shape: pl.BlockSpec(shape, lambda o, t, r: (0, 0, 0))
    grid_spec = pltpu.PrefetchScalarGridSpec(
        num_scalar_prefetch=2,
        grid=(owners,),
        in_specs=[
            full3((nq, hd, rows)),
            pl.BlockSpec((1, 2, plen, hd), lambda o, t, r: (r[o], 0, 0, 0)),
            full3((nq, 1, rows)),
            full3((nq, 1, rows)),
            full3((nq, hd, rows)),
        ],
        out_specs=[full3((nq, 1, rows)), full3((nq, 1, rows)), full3((nq, hd, rows))],
    )
    flops = 4 * nq * rows * plen * hd * owners // 2
    return pl.pallas_call(
        block_kernel,
        grid_spec=grid_spec,
        out_shape=[
            jax.ShapeDtypeStruct(m.shape, jnp.float32),
            jax.ShapeDtypeStruct(l.shape, jnp.float32),
            jax.ShapeDtypeStruct(acc.shape, jnp.float32),
        ],
        input_output_aliases={4: 0, 5: 1, 6: 2},
        compiler_params=pltpu.CompilerParams(
            dimension_semantics=("arbitrary",), vmem_limit_bytes=48 * 1024 * 1024
        ),
        cost_estimate=pl.CostEstimate(
            flops=flops,
            transcendentals=nq * rows * plen * owners // 2,
            bytes_accessed=recv.size * 2 + 2 * acc.size * 4,
        ),
    )(tab, remap, query_t, recv, m, l, acc)


def translations(n):
    if n == 32:
        dims = (4, 4, 2)
    else:
        dims = (n,)
    moves = []
    for t in range(n):
        rest, parts = t, []
        for d in reversed(dims):
            parts.append(rest % d)
            rest //= d
        parts = parts[::-1]

        def dest(i, parts=parts):
            rest, coords = i, []
            for d in reversed(dims):
                coords.append(rest % d)
                rest //= d
            coords = coords[::-1]
            out = 0
            for c, p, d in zip(coords, parts, dims):
                out = out * d + (c + p) % d
            return out

        moves.append([dest(i) for i in range(n)])
    return moves


def exchange(send, moves, me):
    n = send.shape[0]
    got = []
    for t, dest in enumerate(moves):
        target = jnp.asarray(dest, jnp.int32)[me]
        piece = lax.dynamic_index_in_dim(send, target, 0, keepdims=False)
        if t == 0:
            got.append(piece)
        else:
            got.append(lax.ppermute(piece, "store", [(i, dest[i]) for i in range(n)]))
    return jnp.stack(got)


def per_device(
    questions, w_query, w_key, w_value, passage_keys, passage_values, passage_ids, slot_order
):
    kv_heads = w_key.shape[1] // HD
    q_heads = w_query.shape[1] // HD
    group = q_heads // kv_heads
    tok_rows = questions.shape[0]
    count = tok_rows // QLEN
    stored = passage_keys.shape[0]
    owners_count = lax.axis_size("store")
    me = lax.axis_index("store")

    listed = count * RETR
    my_ids = passage_ids.reshape(-1)
    my_pos = slot_order.reshape(-1)
    my_owner = my_ids // stored
    onehot = (my_owner[:, None] == jnp.arange(owners_count, dtype=jnp.int32)[None, :]).astype(
        jnp.int32
    )
    before = jnp.cumsum(onehot, axis=0) - onehot
    my_rank = jnp.sum(before * onehot, axis=1)
    hits = [onehot * (my_rank == c).astype(jnp.int32)[:, None] for c in range(CAP)]

    request = jnp.stack(
        [
            jnp.stack(
                [jnp.sum(h * (my_ids % stored)[:, None], axis=0),
                 jnp.sum(h * my_pos[:, None], axis=0)],
                axis=1,
            )
            for h in hits
        ],
        axis=1,
    )
    incoming = lax.all_to_all(request, "store", split_axis=0, concat_axis=0, tiled=True)

    sends = []
    for c in range(CAP):
        loc = incoming[:, c, 0]
        pos = incoming[:, c, 1]
        cs, sn = angles((pos * PLEN).astype(jnp.float32))
        cos_full = jnp.concatenate([cs, cs], axis=-1)
        sin_full = jnp.concatenate([-sn, sn], axis=-1)
        sends.append(build_send(loc, cos_full, sin_full, passage_keys, passage_values))

    moves = translations(owners_count)
    recvs = [
        lax.all_to_all(sends[0], "store", split_axis=0, concat_axis=0, tiled=True),
        exchange(sends[1], moves, me),
    ]
    src = []
    for dest in moves:
        inv = [0] * owners_count
        for i, j in enumerate(dest):
            inv[j] = i
        src.append(inv)
    src_of = jnp.asarray(src, jnp.int32)[:, me]

    piece = lax.all_gather(questions, "tensor", axis=1, tiled=True)
    qf = jnp.dot(piece, w_query, preferred_element_type=jnp.float32)
    kf = jnp.dot(piece, w_key, preferred_element_type=jnp.float32)
    vf = jnp.dot(piece, w_value, preferred_element_type=jnp.float32)
    qpos = (RETR * PLEN + jnp.arange(QLEN)).astype(jnp.float32)
    cosine, sine = angles(qpos)
    cosine = cosine[None, :, None, :]
    sine = sine[None, :, None, :]
    query = rotate(qf.reshape(count, QLEN, q_heads, HD), cosine, sine).astype(jnp.bfloat16)
    self_key = rotate(kf.reshape(count, QLEN, kv_heads, HD), cosine, sine).astype(jnp.bfloat16)
    self_key = self_key.reshape(count, QLEN, HD)
    self_value = vf.astype(jnp.bfloat16).reshape(count, QLEN, HD)
    query = jnp.transpose(query, (0, 2, 1, 3))

    scale = HD ** (-0.5)
    own = jnp.einsum("qhtd,qud->qhtu", query, self_key, preferred_element_type=jnp.float32) * scale
    causal = jnp.arange(QLEN)[:, None] >= jnp.arange(QLEN)[None, :]
    own = jnp.where(causal, own, -1e30)
    own_peak = jnp.max(own, axis=-1, keepdims=True)
    own_expo = jnp.where(causal, jnp.exp(own - own_peak), 0.0)
    own_total = jnp.sum(own_expo, axis=-1, keepdims=True)
    own_part = jnp.einsum(
        "qhtu,qud->qhtd", own_expo.astype(jnp.bfloat16), self_value,
        preferred_element_type=jnp.float32,
    )
    rows = q_heads * QLEN
    m = own_peak.reshape(count, 1, rows)
    l = own_total.reshape(count, 1, rows)
    acc = jnp.transpose(own_part, (0, 3, 1, 2)).reshape(count, HD, rows)
    query_t = jnp.transpose(query, (0, 3, 1, 2)).reshape(count, HD, rows)

    qidx = jnp.arange(listed, dtype=jnp.int32) // RETR
    slots = jnp.arange(owners_count, dtype=jnp.int32)
    for c in range(CAP):
        hit = hits[c]
        if c == 1:
            hit = hit[:, src_of]
        valid = jnp.sum(hit, axis=0)
        tab = jnp.sum(hit * qidx[:, None], axis=0) + valid - 1
        remap = lax.cummax(jnp.where(valid > 0, slots, 0), axis=0)
        m, l, acc = attend_chunk(tab, remap, query_t, recvs[c], m, l, acc)

    ctx = (acc / l).reshape(count, HD, q_heads, QLEN)
    ctx = jnp.transpose(ctx, (0, 3, 2, 1)).reshape(tok_rows, q_heads * HD)
    return ctx.astype(jnp.bfloat16)


def solution(mesh):
    in_specs = (
        P("store", "tensor"),
        P(None, "tensor"),
        P(None, "tensor"),
        P(None, "tensor"),
        P("store", None, "tensor"),
        P("store", None, "tensor"),
        P("store", None),
        P("store", None),
    )
    out_specs = P("store", "tensor")
    return jax.shard_map(
        per_device, mesh=mesh, in_specs=in_specs, out_specs=out_specs, check_vma=False
    )
```

```python
import functools

import jax
import jax.numpy as jnp
from jax import lax
from jax.experimental import pallas as pl
from jax.experimental.pallas import tpu as pltpu
from jax.sharding import PartitionSpec as P

HD = 128
QLEN = 128
PLEN = 512
RETR = 16
CAP = 2


def angles(positions):
    freqs = 500000.0 ** (-(jnp.arange(HD // 2, dtype=jnp.float32) * 2.0) / HD)
    turned = positions[..., None] * freqs
    return (jnp.cos(turned), jnp.sin(turned))


def rotate(values, cosine, sine):
    half = values.shape[-1] // 2
    first = values[..., :half]
    second = values[..., half:]
    return jnp.concatenate(
        [first * cosine - second * sine, second * cosine + first * sine], axis=-1
    )


def send_kernel(loc_ref, k_ref, v_ref, c_ref, s_ref, out_ref):
    per = out_ref.shape[0]
    base = pl.program_id(0) * per

    def body(j, carry):
        loc = loc_ref[base + j]
        k = k_ref[loc].astype(jnp.float32)
        turned = pltpu.roll(k, k.shape[-1] // 2, 1)
        cos_row = c_ref[pl.ds(base + j, 1), :]
        sin_row = s_ref[pl.ds(base + j, 1), :]
        out_ref[j, 0] = (k * cos_row + turned * sin_row).astype(jnp.bfloat16)
        out_ref[j, 1] = v_ref[loc]
        return carry

    lax.fori_loop(0, per, body, 0)


def build_send(loc, cos_full, sin_full, passage_keys, passage_values):
    owners = loc.shape[0]
    stored, plen, hd = passage_keys.shape
    per = 8
    full = lambda shape: pl.BlockSpec(shape, lambda i, loc: (0,) * len(shape))
    grid_spec = pltpu.PrefetchScalarGridSpec(
        num_scalar_prefetch=1,
        grid=(owners // per,),
        in_specs=[
            full((stored, plen, hd)),
            full((stored, plen, hd)),
            full((owners, hd)),
            full((owners, hd)),
        ],
        out_specs=pl.BlockSpec((per, 2, plen, hd), lambda i, loc: (i, 0, 0, 0)),
    )
    return pl.pallas_call(
        send_kernel,
        grid_spec=grid_spec,
        out_shape=jax.ShapeDtypeStruct((owners, 2, plen, hd), jnp.bfloat16),
        compiler_params=pltpu.CompilerParams(dimension_semantics=("arbitrary",)),
        cost_estimate=pl.CostEstimate(
            flops=4 * owners * plen * hd, transcendentals=0,
            bytes_accessed=owners * plen * hd * 2 * 2 + 2 * passage_keys.size * 2,
        ),
    )(loc, passage_keys, passage_values, cos_full, sin_full)


ROW_TILE = 1024
LOG2E = 1.4426950408889634


def block_kernel(tab_ref, remap_ref, q_ref, kv_ref, m_in, l_in, a_in, m_ref, l_ref, a_ref):
    o = pl.program_id(0)

    @pl.when(o == 0)
    def _():
        m_ref[...] = m_in[...]
        l_ref[...] = l_in[...]
        a_ref[...] = a_in[...]

    qi = tab_ref[o]

    @pl.when(qi >= 0)
    def _():
        k = kv_ref[0, 0]
        v = kv_ref[0, 1]
        c = (HD ** (-0.5)) * LOG2E
        for r0 in range(0, q_ref.shape[2], ROW_TILE):
            cols = pl.ds(r0, ROW_TILE)
            s = jnp.dot(k, q_ref[qi, :, cols], preferred_element_type=jnp.float32)
            m = jnp.max(s, axis=0, keepdims=True)
            e = jnp.exp2(s * c - m * c)
            l = jnp.sum(e, axis=0, keepdims=True)
            p = lax.dot_general(
                v, e.astype(jnp.bfloat16), (((0,), (0,)), ((), ())),
                preferred_element_type=jnp.float32,
            )
            m = m * (HD ** (-0.5))
            m_old = m_ref[qi, :, cols]
            m_new = jnp.maximum(m_old, m)
            w_old = jnp.exp(m_old - m_new)
            w_new = jnp.exp(m - m_new)
            l_ref[qi, :, cols] = w_old * l_ref[qi, :, cols] + w_new * l
            a_ref[qi, :, cols] = w_old * a_ref[qi, :, cols] + w_new * p
            m_ref[qi, :, cols] = m_new


def attend_chunk(tab, remap, query_t, recv, m, l, acc):
    owners = tab.shape[0]
    nq, hd, rows = query_t.shape
    plen = recv.shape[2]
    full3 = lambda shape: pl.BlockSpec(shape, lambda o, t, r: (0, 0, 0))
    grid_spec = pltpu.PrefetchScalarGridSpec(
        num_scalar_prefetch=2,
        grid=(owners,),
        in_specs=[
            full3((nq, hd, rows)),
            pl.BlockSpec((1, 2, plen, hd), lambda o, t, r: (r[o], 0, 0, 0)),
            full3((nq, 1, rows)),
            full3((nq, 1, rows)),
            full3((nq, hd, rows)),
        ],
        out_specs=[full3((nq, 1, rows)), full3((nq, 1, rows)), full3((nq, hd, rows))],
    )
    flops = 4 * nq * rows * plen * hd * owners // 2
    return pl.pallas_call(
        block_kernel,
        grid_spec=grid_spec,
        out_shape=[
            jax.ShapeDtypeStruct(m.shape, jnp.float32),
            jax.ShapeDtypeStruct(l.shape, jnp.float32),
            jax.ShapeDtypeStruct(acc.shape, jnp.float32),
        ],
        input_output_aliases={4: 0, 5: 1, 6: 2},
        compiler_params=pltpu.CompilerParams(
            dimension_semantics=("arbitrary",), vmem_limit_bytes=48 * 1024 * 1024
        ),
        cost_estimate=pl.CostEstimate(
            flops=flops,
            transcendentals=nq * rows * plen * owners // 2,
            bytes_accessed=recv.size * 2 + 2 * acc.size * 4,
        ),
    )(tab, remap, query_t, recv, m, l, acc)


def per_device(
    questions, w_query, w_key, w_value, passage_keys, passage_values, passage_ids, slot_order
):
    kv_heads = w_key.shape[1] // HD
    q_heads = w_query.shape[1] // HD
    group = q_heads // kv_heads
    tok_rows = questions.shape[0]
    count = tok_rows // QLEN
    stored = passage_keys.shape[0]
    owners_count = lax.axis_size("store")
    me = lax.axis_index("store")

    listed = count * RETR
    my_ids = passage_ids.reshape(-1)
    my_pos = slot_order.reshape(-1)
    my_owner = my_ids // stored
    onehot = (my_owner[:, None] == jnp.arange(owners_count, dtype=jnp.int32)[None, :]).astype(
        jnp.int32
    )
    before = jnp.cumsum(onehot, axis=0) - onehot
    my_rank = jnp.sum(before * onehot, axis=1)
    hits = [onehot * (my_rank == c).astype(jnp.int32)[:, None] for c in range(CAP)]

    request = jnp.stack(
        [
            jnp.stack(
                [jnp.sum(h * (my_ids % stored)[:, None], axis=0),
                 jnp.sum(h * my_pos[:, None], axis=0)],
                axis=1,
            )
            for h in hits
        ],
        axis=1,
    )
    incoming = lax.all_to_all(request, "store", split_axis=0, concat_axis=0, tiled=True)

    sends = []
    for c in range(CAP):
        loc = incoming[:, c, 0]
        pos = incoming[:, c, 1]
        cs, sn = angles((pos * PLEN).astype(jnp.float32))
        cos_full = jnp.concatenate([cs, cs], axis=-1)
        sin_full = jnp.concatenate([-sn, sn], axis=-1)
        sends.append(build_send(loc, cos_full, sin_full, passage_keys, passage_values))

    recvs = [
        lax.all_to_all(s, "store", split_axis=0, concat_axis=0, tiled=True) for s in sends
    ]

    piece = lax.all_gather(questions, "tensor", axis=1, tiled=True)
    qf = jnp.dot(piece, w_query, preferred_element_type=jnp.float32)
    kf = jnp.dot(piece, w_key, preferred_element_type=jnp.float32)
    vf = jnp.dot(piece, w_value, preferred_element_type=jnp.float32)
    qpos = (RETR * PLEN + jnp.arange(QLEN)).astype(jnp.float32)
    cosine, sine = angles(qpos)
    cosine = cosine[None, :, None, :]
    sine = sine[None, :, None, :]
    query = rotate(qf.reshape(count, QLEN, q_heads, HD), cosine, sine).astype(jnp.bfloat16)
    self_key = rotate(kf.reshape(count, QLEN, kv_heads, HD), cosine, sine).astype(jnp.bfloat16)
    self_key = self_key.reshape(count, QLEN, HD)
    self_value = vf.astype(jnp.bfloat16).reshape(count, QLEN, HD)
    query = jnp.transpose(query, (0, 2, 1, 3))

    scale = HD ** (-0.5)
    own = jnp.einsum("qhtd,qud->qhtu", query, self_key, preferred_element_type=jnp.float32) * scale
    causal = jnp.arange(QLEN)[:, None] >= jnp.arange(QLEN)[None, :]
    own = jnp.where(causal, own, -1e30)
    own_peak = jnp.max(own, axis=-1, keepdims=True)
    own_expo = jnp.where(causal, jnp.exp(own - own_peak), 0.0)
    own_total = jnp.sum(own_expo, axis=-1, keepdims=True)
    own_part = jnp.einsum(
        "qhtu,qud->qhtd", own_expo.astype(jnp.bfloat16), self_value,
        preferred_element_type=jnp.float32,
    )
    rows = q_heads * QLEN
    m = own_peak.reshape(count, 1, rows)
    l = own_total.reshape(count, 1, rows)
    acc = jnp.transpose(own_part, (0, 3, 1, 2)).reshape(count, HD, rows)
    query_t = jnp.transpose(query, (0, 3, 1, 2)).reshape(count, HD, rows)

    qidx = jnp.arange(listed, dtype=jnp.int32) // RETR
    slots = jnp.arange(owners_count, dtype=jnp.int32)
    for c in range(CAP):
        hit = hits[c]
        valid = jnp.sum(hit, axis=0)
        tab = jnp.sum(hit * qidx[:, None], axis=0) + valid - 1
        steps = owners_count if c == 0 else min(owners_count, listed // CAP)
        order = jnp.argsort(1 - valid, stable=True).astype(jnp.int32)[:steps]
        tab = tab[order]
        remap = lax.cummax(jnp.where(tab >= 0, order, 0), axis=0)
        m, l, acc = attend_chunk(tab, remap, query_t, recvs[c], m, l, acc)

    ctx = (acc / l).reshape(count, HD, q_heads, QLEN)
    ctx = jnp.transpose(ctx, (0, 3, 2, 1)).reshape(tok_rows, q_heads * HD)
    return ctx.astype(jnp.bfloat16)


def solution(mesh):
    in_specs = (
        P("store", "tensor"),
        P(None, "tensor"),
        P(None, "tensor"),
        P(None, "tensor"),
        P("store", None, "tensor"),
        P("store", None, "tensor"),
        P("store", None),
        P("store", None),
    )
    out_specs = P("store", "tensor")
    return jax.shard_map(
        per_device, mesh=mesh, in_specs=in_specs, out_specs=out_specs, check_vma=False
    )
```

```python
import functools

import jax
import jax.numpy as jnp
from jax import lax
from jax.experimental import pallas as pl
from jax.experimental.pallas import tpu as pltpu
from jax.sharding import PartitionSpec as P

HD = 128
QLEN = 128
PLEN = 512
RETR = 16
CAP = 2


def angles(positions):
    freqs = 500000.0 ** (-(jnp.arange(HD // 2, dtype=jnp.float32) * 2.0) / HD)
    turned = positions[..., None] * freqs
    return (jnp.cos(turned), jnp.sin(turned))


def rotate(values, cosine, sine):
    half = values.shape[-1] // 2
    first = values[..., :half]
    second = values[..., half:]
    return jnp.concatenate(
        [first * cosine - second * sine, second * cosine + first * sine], axis=-1
    )


def send_kernel(loc_ref, k_ref, v_ref, c_ref, s_ref, out_ref):
    per = out_ref.shape[0]
    base = pl.program_id(0) * per

    def body(j, carry):
        loc = loc_ref[base + j]
        k = k_ref[loc].astype(jnp.float32)
        turned = pltpu.roll(k, k.shape[-1] // 2, 1)
        cos_row = c_ref[pl.ds(base + j, 1), :]
        sin_row = s_ref[pl.ds(base + j, 1), :]
        out_ref[j, 0] = (k * cos_row + turned * sin_row).astype(jnp.bfloat16)
        out_ref[j, 1] = v_ref[loc]
        return carry

    lax.fori_loop(0, per, body, 0)


def build_send(loc, cos_full, sin_full, passage_keys, passage_values):
    owners = loc.shape[0]
    stored, plen, hd = passage_keys.shape
    per = 8
    full = lambda shape: pl.BlockSpec(shape, lambda i, loc: (0,) * len(shape))
    grid_spec = pltpu.PrefetchScalarGridSpec(
        num_scalar_prefetch=1,
        grid=(owners // per,),
        in_specs=[
            full((stored, plen, hd)),
            full((stored, plen, hd)),
            full((owners, hd)),
            full((owners, hd)),
        ],
        out_specs=pl.BlockSpec((per, 2, plen, hd), lambda i, loc: (i, 0, 0, 0)),
    )
    return pl.pallas_call(
        send_kernel,
        grid_spec=grid_spec,
        out_shape=jax.ShapeDtypeStruct((owners, 2, plen, hd), jnp.bfloat16),
        compiler_params=pltpu.CompilerParams(dimension_semantics=("arbitrary",)),
        cost_estimate=pl.CostEstimate(
            flops=4 * owners * plen * hd, transcendentals=0,
            bytes_accessed=owners * plen * hd * 2 * 2 + 2 * passage_keys.size * 2,
        ),
    )(loc, passage_keys, passage_values, cos_full, sin_full)


ROW_TILE = 1024
LOG2E = 1.4426950408889634


def block_kernel(tab_ref, remap_ref, q_ref, kv0_ref, kv1_ref, m_in, l_in, a_in, m_ref, l_ref, a_ref):
    o = pl.program_id(0)

    @pl.when(o == 0)
    def _():
        m_ref[...] = m_in[...]
        l_ref[...] = l_in[...]
        a_ref[...] = a_in[...]

    c = (HD ** (-0.5)) * LOG2E
    for j, kv_ref in enumerate((kv0_ref, kv1_ref)):
        qi = tab_ref[2 * o + j]

        @pl.when(qi >= 0)
        def _():
            k = kv_ref[0, 0]
            v = kv_ref[0, 1]
            for r0 in range(0, q_ref.shape[2], ROW_TILE):
                cols = pl.ds(r0, ROW_TILE)
                s = jnp.dot(k, q_ref[qi, :, cols], preferred_element_type=jnp.float32)
                m = jnp.max(s, axis=0, keepdims=True)
                e = jnp.exp2(s * c - m * c)
                l = jnp.sum(e, axis=0, keepdims=True)
                p = lax.dot_general(
                    v, e.astype(jnp.bfloat16), (((0,), (0,)), ((), ())),
                    preferred_element_type=jnp.float32,
                )
                m = m * (HD ** (-0.5))
                m_old = m_ref[qi, :, cols]
                m_new = jnp.maximum(m_old, m)
                w_old = jnp.exp(m_old - m_new)
                w_new = jnp.exp(m - m_new)
                l_ref[qi, :, cols] = w_old * l_ref[qi, :, cols] + w_new * l
                a_ref[qi, :, cols] = w_old * a_ref[qi, :, cols] + w_new * p
                m_ref[qi, :, cols] = m_new


def attend_chunk(tab, remap, query_t, recv, m, l, acc):
    owners = tab.shape[0] // 2
    nq, hd, rows = query_t.shape
    plen = recv.shape[2]
    full3 = lambda shape: pl.BlockSpec(shape, lambda o, t, r: (0, 0, 0))
    grid_spec = pltpu.PrefetchScalarGridSpec(
        num_scalar_prefetch=2,
        grid=(owners,),
        in_specs=[
            full3((nq, hd, rows)),
            pl.BlockSpec((1, 2, plen, hd), lambda o, t, r: (r[2 * o], 0, 0, 0)),
            pl.BlockSpec((1, 2, plen, hd), lambda o, t, r: (r[2 * o + 1], 0, 0, 0)),
            full3((nq, 1, rows)),
            full3((nq, 1, rows)),
            full3((nq, hd, rows)),
        ],
        out_specs=[full3((nq, 1, rows)), full3((nq, 1, rows)), full3((nq, hd, rows))],
    )
    flops = 4 * nq * rows * plen * hd * owners
    return pl.pallas_call(
        block_kernel,
        grid_spec=grid_spec,
        out_shape=[
            jax.ShapeDtypeStruct(m.shape, jnp.float32),
            jax.ShapeDtypeStruct(l.shape, jnp.float32),
            jax.ShapeDtypeStruct(acc.shape, jnp.float32),
        ],
        input_output_aliases={5: 0, 6: 1, 7: 2},
        compiler_params=pltpu.CompilerParams(
            dimension_semantics=("arbitrary",), vmem_limit_bytes=48 * 1024 * 1024
        ),
        cost_estimate=pl.CostEstimate(
            flops=flops,
            transcendentals=nq * rows * plen * owners,
            bytes_accessed=recv.size * 2 + 2 * acc.size * 4,
        ),
    )(tab, remap, query_t, recv, recv, m, l, acc)


def per_device(
    questions, w_query, w_key, w_value, passage_keys, passage_values, passage_ids, slot_order
):
    kv_heads = w_key.shape[1] // HD
    q_heads = w_query.shape[1] // HD
    group = q_heads // kv_heads
    tok_rows = questions.shape[0]
    count = tok_rows // QLEN
    stored = passage_keys.shape[0]
    owners_count = lax.axis_size("store")
    me = lax.axis_index("store")

    listed = count * RETR
    my_ids = passage_ids.reshape(-1)
    my_pos = slot_order.reshape(-1)
    my_owner = my_ids // stored
    onehot = (my_owner[:, None] == jnp.arange(owners_count, dtype=jnp.int32)[None, :]).astype(
        jnp.int32
    )
    before = jnp.cumsum(onehot, axis=0) - onehot
    my_rank = jnp.sum(before * onehot, axis=1)
    hits = [onehot * (my_rank == c).astype(jnp.int32)[:, None] for c in range(CAP)]

    request = jnp.stack(
        [
            jnp.stack(
                [jnp.sum(h * (my_ids % stored)[:, None], axis=0),
                 jnp.sum(h * my_pos[:, None], axis=0)],
                axis=1,
            )
            for h in hits
        ],
        axis=1,
    )
    incoming = lax.all_to_all(request, "store", split_axis=0, concat_axis=0, tiled=True)

    sends = []
    for c in range(CAP):
        loc = incoming[:, c, 0]
        pos = incoming[:, c, 1]
        cs, sn = angles((pos * PLEN).astype(jnp.float32))
        cos_full = jnp.concatenate([cs, cs], axis=-1)
        sin_full = jnp.concatenate([-sn, sn], axis=-1)
        sends.append(build_send(loc, cos_full, sin_full, passage_keys, passage_values))

    recvs = [
        lax.all_to_all(s, "store", split_axis=0, concat_axis=0, tiled=True) for s in sends
    ]

    piece = lax.all_gather(questions, "tensor", axis=1, tiled=True)
    qf = jnp.dot(piece, w_query, preferred_element_type=jnp.float32)
    kf = jnp.dot(piece, w_key, preferred_element_type=jnp.float32)
    vf = jnp.dot(piece, w_value, preferred_element_type=jnp.float32)
    qpos = (RETR * PLEN + jnp.arange(QLEN)).astype(jnp.float32)
    cosine, sine = angles(qpos)
    cosine = cosine[None, :, None, :]
    sine = sine[None, :, None, :]
    query = rotate(qf.reshape(count, QLEN, q_heads, HD), cosine, sine).astype(jnp.bfloat16)
    self_key = rotate(kf.reshape(count, QLEN, kv_heads, HD), cosine, sine).astype(jnp.bfloat16)
    self_key = self_key.reshape(count, QLEN, HD)
    self_value = vf.astype(jnp.bfloat16).reshape(count, QLEN, HD)
    query = jnp.transpose(query, (0, 2, 1, 3))

    scale = HD ** (-0.5)
    own = jnp.einsum("qhtd,qud->qhtu", query, self_key, preferred_element_type=jnp.float32) * scale
    causal = jnp.arange(QLEN)[:, None] >= jnp.arange(QLEN)[None, :]
    own = jnp.where(causal, own, -1e30)
    own_peak = jnp.max(own, axis=-1, keepdims=True)
    own_expo = jnp.where(causal, jnp.exp(own - own_peak), 0.0)
    own_total = jnp.sum(own_expo, axis=-1, keepdims=True)
    own_part = jnp.einsum(
        "qhtu,qud->qhtd", own_expo.astype(jnp.bfloat16), self_value,
        preferred_element_type=jnp.float32,
    )
    rows = q_heads * QLEN
    m = own_peak.reshape(count, 1, rows)
    l = own_total.reshape(count, 1, rows)
    acc = jnp.transpose(own_part, (0, 3, 1, 2)).reshape(count, HD, rows)
    query_t = jnp.transpose(query, (0, 3, 1, 2)).reshape(count, HD, rows)

    qidx = jnp.arange(listed, dtype=jnp.int32) // RETR
    slots = jnp.arange(owners_count, dtype=jnp.int32)
    for c in range(CAP):
        hit = hits[c]
        valid = jnp.sum(hit, axis=0)
        tab = jnp.sum(hit * qidx[:, None], axis=0) + valid - 1
        steps = owners_count if c == 0 else min(owners_count, listed // CAP)
        order = jnp.argsort(1 - valid, stable=True).astype(jnp.int32)[:steps]
        tab = tab[order]
        remap = lax.cummax(jnp.where(tab >= 0, order, 0), axis=0)
        m, l, acc = attend_chunk(tab, remap, query_t, recvs[c], m, l, acc)

    ctx = (acc / l).reshape(count, HD, q_heads, QLEN)
    ctx = jnp.transpose(ctx, (0, 3, 2, 1)).reshape(tok_rows, q_heads * HD)
    return ctx.astype(jnp.bfloat16)


def solution(mesh):
    in_specs = (
        P("store", "tensor"),
        P(None, "tensor"),
        P(None, "tensor"),
        P(None, "tensor"),
        P("store", None, "tensor"),
        P("store", None, "tensor"),
        P("store", None),
        P("store", None),
    )
    out_specs = P("store", "tensor")
    return jax.shard_map(
        per_device, mesh=mesh, in_specs=in_specs, out_specs=out_specs, check_vma=False
    )
```

```python
import functools

import jax
import jax.numpy as jnp
from jax import lax
from jax.experimental import pallas as pl
from jax.experimental.pallas import tpu as pltpu
from jax.sharding import PartitionSpec as P

HD = 128
QLEN = 128
PLEN = 512
RETR = 16
CAP = 2


def angles(positions):
    freqs = 500000.0 ** (-(jnp.arange(HD // 2, dtype=jnp.float32) * 2.0) / HD)
    turned = positions[..., None] * freqs
    return (jnp.cos(turned), jnp.sin(turned))


def rotate(values, cosine, sine):
    half = values.shape[-1] // 2
    first = values[..., :half]
    second = values[..., half:]
    return jnp.concatenate(
        [first * cosine - second * sine, second * cosine + first * sine], axis=-1
    )


def send_kernel(loc_ref, k_ref, v_ref, c_ref, s_ref, out_ref):
    per = out_ref.shape[0]
    base = pl.program_id(0) * per

    def body(j, carry):
        loc = loc_ref[base + j]
        k = k_ref[loc].astype(jnp.float32)
        turned = pltpu.roll(k, k.shape[-1] // 2, 1)
        cos_row = c_ref[pl.ds(base + j, 1), :]
        sin_row = s_ref[pl.ds(base + j, 1), :]
        out_ref[j, 0] = (k * cos_row + turned * sin_row).astype(jnp.bfloat16)
        out_ref[j, 1] = v_ref[loc]
        return carry

    lax.fori_loop(0, per, body, 0)


def build_send(loc, cos_full, sin_full, passage_keys, passage_values):
    owners = loc.shape[0]
    stored, plen, hd = passage_keys.shape
    per = 8
    full = lambda shape: pl.BlockSpec(shape, lambda i, loc: (0,) * len(shape))
    grid_spec = pltpu.PrefetchScalarGridSpec(
        num_scalar_prefetch=1,
        grid=(owners // per,),
        in_specs=[
            full((stored, plen, hd)),
            full((stored, plen, hd)),
            full((owners, hd)),
            full((owners, hd)),
        ],
        out_specs=pl.BlockSpec((per, 2, plen, hd), lambda i, loc: (i, 0, 0, 0)),
    )
    return pl.pallas_call(
        send_kernel,
        grid_spec=grid_spec,
        out_shape=jax.ShapeDtypeStruct((owners, 2, plen, hd), jnp.bfloat16),
        compiler_params=pltpu.CompilerParams(dimension_semantics=("arbitrary",)),
        cost_estimate=pl.CostEstimate(
            flops=4 * owners * plen * hd, transcendentals=0,
            bytes_accessed=owners * plen * hd * 2 * 2 + 2 * passage_keys.size * 2,
        ),
    )(loc, passage_keys, passage_values, cos_full, sin_full)


ROW_TILE = 1024
LOG2E = 1.4426950408889634


def block_kernel(tab_ref, remap_ref, q_ref, kv0_ref, kv1_ref, m_in, l_in, a_in, m_ref, l_ref, a_ref):
    o = pl.program_id(0)

    @pl.when(o == 0)
    def _():
        m_ref[...] = m_in[...]
        l_ref[...] = l_in[...]
        a_ref[...] = a_in[...]

    c = (HD ** (-0.5)) * LOG2E
    for j, kv_ref in enumerate((kv0_ref, kv1_ref)):
        qi = tab_ref[2 * o + j]

        @pl.when(qi >= 0)
        def _():
            k = kv_ref[0, 0]
            v = kv_ref[0, 1]
            for r0 in range(0, q_ref.shape[2], ROW_TILE):
                cols = pl.ds(r0, ROW_TILE)
                s = jnp.dot(k, q_ref[qi, :, cols], preferred_element_type=jnp.float32)
                m = jnp.max(s, axis=0, keepdims=True)
                e = jnp.exp2(s * c - m * c)
                l = jnp.sum(e, axis=0, keepdims=True)
                p = lax.dot_general(
                    v, e.astype(jnp.bfloat16), (((0,), (0,)), ((), ())),
                    preferred_element_type=jnp.float32,
                )
                m = m * (HD ** (-0.5))
                m_old = m_ref[qi, :, cols]
                m_new = jnp.maximum(m_old, m)
                w_old = jnp.exp(m_old - m_new)
                w_new = jnp.exp(m - m_new)
                l_ref[qi, :, cols] = w_old * l_ref[qi, :, cols] + w_new * l
                a_ref[qi, :, cols] = w_old * a_ref[qi, :, cols] + w_new * p
                m_ref[qi, :, cols] = m_new


def attend_chunk(tab, remap, query_t, recv, m, l, acc):
    owners = tab.shape[0] // 2
    nq, hd, rows = query_t.shape
    plen = recv.shape[2]
    full3 = lambda shape: pl.BlockSpec(shape, lambda o, t, r: (0, 0, 0))
    grid_spec = pltpu.PrefetchScalarGridSpec(
        num_scalar_prefetch=2,
        grid=(owners,),
        in_specs=[
            full3((nq, hd, rows)),
            pl.BlockSpec((1, 2, plen, hd), lambda o, t, r: (r[2 * o], 0, 0, 0)),
            pl.BlockSpec((1, 2, plen, hd), lambda o, t, r: (r[2 * o + 1], 0, 0, 0)),
            full3((nq, 1, rows)),
            full3((nq, 1, rows)),
            full3((nq, hd, rows)),
        ],
        out_specs=[full3((nq, 1, rows)), full3((nq, 1, rows)), full3((nq, hd, rows))],
    )
    flops = 4 * nq * rows * plen * hd * owners
    return pl.pallas_call(
        block_kernel,
        grid_spec=grid_spec,
        out_shape=[
            jax.ShapeDtypeStruct(m.shape, jnp.float32),
            jax.ShapeDtypeStruct(l.shape, jnp.float32),
            jax.ShapeDtypeStruct(acc.shape, jnp.float32),
        ],
        input_output_aliases={5: 0, 6: 1, 7: 2},
        compiler_params=pltpu.CompilerParams(
            dimension_semantics=("arbitrary",), vmem_limit_bytes=48 * 1024 * 1024
        ),
        cost_estimate=pl.CostEstimate(
            flops=flops,
            transcendentals=nq * rows * plen * owners,
            bytes_accessed=recv.size * 2 + 2 * acc.size * 4,
        ),
    )(tab, remap, query_t, recv, recv, m, l, acc)


def per_device(
    questions, w_query, w_key, w_value, passage_keys, passage_values, passage_ids, slot_order
):
    kv_heads = w_key.shape[1] // HD
    q_heads = w_query.shape[1] // HD
    group = q_heads // kv_heads
    tok_rows = questions.shape[0]
    count = tok_rows // QLEN
    stored = passage_keys.shape[0]
    owners_count = lax.axis_size("store")
    me = lax.axis_index("store")

    listed = count * RETR
    my_ids = passage_ids.reshape(-1)
    my_pos = slot_order.reshape(-1)
    my_owner = my_ids // stored
    onehot = (my_owner[:, None] == jnp.arange(owners_count, dtype=jnp.int32)[None, :]).astype(
        jnp.int32
    )
    before = jnp.cumsum(onehot, axis=0) - onehot
    my_rank = jnp.sum(before * onehot, axis=1)
    hits = [onehot * (my_rank == c).astype(jnp.int32)[:, None] for c in range(CAP)]

    request = jnp.stack(
        [
            jnp.stack(
                [jnp.sum(h * (my_ids % stored)[:, None], axis=0),
                 jnp.sum(h * my_pos[:, None], axis=0)],
                axis=1,
            )
            for h in hits
        ],
        axis=1,
    )
    incoming = lax.all_to_all(request, "store", split_axis=0, concat_axis=0, tiled=True)

    sends = []
    for c in range(CAP):
        loc = incoming[:, c, 0]
        pos = incoming[:, c, 1]
        cs, sn = angles((pos * PLEN).astype(jnp.float32))
        cos_full = jnp.concatenate([cs, cs], axis=-1)
        sin_full = jnp.concatenate([-sn, sn], axis=-1)
        sends.append(build_send(loc, cos_full, sin_full, passage_keys, passage_values))

    recvs = [
        lax.all_to_all(s, "store", split_axis=0, concat_axis=0, tiled=True) for s in sends
    ]

    parts = lax.axis_size("tensor")
    zi = lax.axis_index("tensor")
    got = [questions] + [
        lax.ppermute(questions, "tensor", [(i, (i + sh) % parts) for i in range(parts)])
        for sh in range(1, parts)
    ]
    got = jnp.stack(got)
    order = (zi - jnp.arange(parts, dtype=jnp.int32)) % parts
    piece = jnp.concatenate(
        [lax.dynamic_index_in_dim(got, order[j], 0, keepdims=False) for j in range(parts)],
        axis=1,
    )
    qf = jnp.dot(piece, w_query, preferred_element_type=jnp.float32)
    kf = jnp.dot(piece, w_key, preferred_element_type=jnp.float32)
    vf = jnp.dot(piece, w_value, preferred_element_type=jnp.float32)
    qpos = (RETR * PLEN + jnp.arange(QLEN)).astype(jnp.float32)
    cosine, sine = angles(qpos)
    cosine = cosine[None, :, None, :]
    sine = sine[None, :, None, :]
    query = rotate(qf.reshape(count, QLEN, q_heads, HD), cosine, sine).astype(jnp.bfloat16)
    self_key = rotate(kf.reshape(count, QLEN, kv_heads, HD), cosine, sine).astype(jnp.bfloat16)
    self_key = self_key.reshape(count, QLEN, HD)
    self_value = vf.astype(jnp.bfloat16).reshape(count, QLEN, HD)
    query = jnp.transpose(query, (0, 2, 1, 3))

    scale = HD ** (-0.5)
    own = jnp.einsum("qhtd,qud->qhtu", query, self_key, preferred_element_type=jnp.float32) * scale
    causal = jnp.arange(QLEN)[:, None] >= jnp.arange(QLEN)[None, :]
    own = jnp.where(causal, own, -1e30)
    own_peak = jnp.max(own, axis=-1, keepdims=True)
    own_expo = jnp.where(causal, jnp.exp(own - own_peak), 0.0)
    own_total = jnp.sum(own_expo, axis=-1, keepdims=True)
    own_part = jnp.einsum(
        "qhtu,qud->qhtd", own_expo.astype(jnp.bfloat16), self_value,
        preferred_element_type=jnp.float32,
    )
    rows = q_heads * QLEN
    m = own_peak.reshape(count, 1, rows)
    l = own_total.reshape(count, 1, rows)
    acc = jnp.transpose(own_part, (0, 3, 1, 2)).reshape(count, HD, rows)
    query_t = jnp.transpose(query, (0, 3, 1, 2)).reshape(count, HD, rows)

    qidx = jnp.arange(listed, dtype=jnp.int32) // RETR
    slots = jnp.arange(owners_count, dtype=jnp.int32)
    for c in range(CAP):
        hit = hits[c]
        valid = jnp.sum(hit, axis=0)
        tab = jnp.sum(hit * qidx[:, None], axis=0) + valid - 1
        steps = owners_count if c == 0 else min(owners_count, listed // CAP)
        order = jnp.argsort(1 - valid, stable=True).astype(jnp.int32)[:steps]
        tab = tab[order]
        remap = lax.cummax(jnp.where(tab >= 0, order, 0), axis=0)
        m, l, acc = attend_chunk(tab, remap, query_t, recvs[c], m, l, acc)

    ctx = (acc / l).reshape(count, HD, q_heads, QLEN)
    ctx = jnp.transpose(ctx, (0, 3, 2, 1)).reshape(tok_rows, q_heads * HD)
    return ctx.astype(jnp.bfloat16)


def solution(mesh):
    in_specs = (
        P("store", "tensor"),
        P(None, "tensor"),
        P(None, "tensor"),
        P(None, "tensor"),
        P("store", None, "tensor"),
        P("store", None, "tensor"),
        P("store", None),
        P("store", None),
    )
    out_specs = P("store", "tensor")
    return jax.shard_map(
        per_device, mesh=mesh, in_specs=in_specs, out_specs=out_specs, check_vma=False
    )
```

```python
import functools

import jax
import jax.numpy as jnp
from jax import lax
from jax.experimental import pallas as pl
from jax.experimental.pallas import tpu as pltpu
from jax.sharding import PartitionSpec as P

HD = 128
QLEN = 128
PLEN = 512
RETR = 16
CAP = 2


def angles(positions):
    freqs = 500000.0 ** (-(jnp.arange(HD // 2, dtype=jnp.float32) * 2.0) / HD)
    turned = positions[..., None] * freqs
    return (jnp.cos(turned), jnp.sin(turned))


def rotate(values, cosine, sine):
    half = values.shape[-1] // 2
    first = values[..., :half]
    second = values[..., half:]
    return jnp.concatenate(
        [first * cosine - second * sine, second * cosine + first * sine], axis=-1
    )


def send_kernel(slot, req_ref, k_ref, v_ref, c_ref, s_ref, out_ref):
    per = out_ref.shape[0]
    base = pl.program_id(0) * per

    def body(j, carry):
        at = ((base + j) * CAP + slot) * 2
        loc = req_ref[at]
        pos = req_ref[at + 1]
        k = k_ref[loc].astype(jnp.float32)
        turned = pltpu.roll(k, k.shape[-1] // 2, 1)
        cos_row = c_ref[pl.ds(pos, 1), :]
        sin_row = s_ref[pl.ds(pos, 1), :]
        out_ref[j, 0] = (k * cos_row + turned * sin_row).astype(jnp.bfloat16)
        out_ref[j, 1] = v_ref[loc]
        return carry

    lax.fori_loop(0, per, body, 0)


def build_send(slot, req, cos_tab, sin_tab, passage_keys, passage_values):
    owners = req.shape[0] // (CAP * 2)
    stored, plen, hd = passage_keys.shape
    per = 8
    full = lambda shape: pl.BlockSpec(shape, lambda i, req: (0,) * len(shape))
    grid_spec = pltpu.PrefetchScalarGridSpec(
        num_scalar_prefetch=1,
        grid=(owners // per,),
        in_specs=[
            full((stored, plen, hd)),
            full((stored, plen, hd)),
            full(cos_tab.shape),
            full(sin_tab.shape),
        ],
        out_specs=pl.BlockSpec((per, 2, plen, hd), lambda i, req: (i, 0, 0, 0)),
    )
    return pl.pallas_call(
        functools.partial(send_kernel, slot),
        grid_spec=grid_spec,
        out_shape=jax.ShapeDtypeStruct((owners, 2, plen, hd), jnp.bfloat16),
        compiler_params=pltpu.CompilerParams(dimension_semantics=("arbitrary",)),
        cost_estimate=pl.CostEstimate(
            flops=4 * owners * plen * hd, transcendentals=0,
            bytes_accessed=owners * plen * hd * 2 * 2 + 2 * passage_keys.size * 2,
        ),
    )(req, passage_keys, passage_values, cos_tab, sin_tab)


ROW_TILE = 1024
LOG2E = 1.4426950408889634


def block_kernel(tab_ref, remap_ref, q_ref, kv0_ref, kv1_ref, m_in, l_in, a_in, m_ref, l_ref, a_ref):
    o = pl.program_id(0)

    @pl.when(o == 0)
    def _():
        m_ref[...] = m_in[...]
        l_ref[...] = l_in[...]
        a_ref[...] = a_in[...]

    c = (HD ** (-0.5)) * LOG2E
    for j, kv_ref in enumerate((kv0_ref, kv1_ref)):
        qi = tab_ref[2 * o + j]

        @pl.when(qi >= 0)
        def _():
            k = kv_ref[0, 0]
            v = kv_ref[0, 1]
            for r0 in range(0, q_ref.shape[2], ROW_TILE):
                cols = pl.ds(r0, ROW_TILE)
                s = jnp.dot(k, q_ref[qi, :, cols], preferred_element_type=jnp.float32)
                m = jnp.max(s, axis=0, keepdims=True)
                e = jnp.exp2(s * c - m * c)
                l = jnp.sum(e, axis=0, keepdims=True)
                p = lax.dot_general(
                    v, e.astype(jnp.bfloat16), (((0,), (0,)), ((), ())),
                    preferred_element_type=jnp.float32,
                )
                m = m * (HD ** (-0.5))
                m_old = m_ref[qi, :, cols]
                m_new = jnp.maximum(m_old, m)
                w_old = jnp.exp(m_old - m_new)
                w_new = jnp.exp(m - m_new)
                l_ref[qi, :, cols] = w_old * l_ref[qi, :, cols] + w_new * l
                a_ref[qi, :, cols] = w_old * a_ref[qi, :, cols] + w_new * p
                m_ref[qi, :, cols] = m_new


def attend_chunk(tab, remap, query_t, recv, m, l, acc):
    owners = tab.shape[0] // 2
    nq, hd, rows = query_t.shape
    plen = recv.shape[2]
    full3 = lambda shape: pl.BlockSpec(shape, lambda o, t, r: (0, 0, 0))
    grid_spec = pltpu.PrefetchScalarGridSpec(
        num_scalar_prefetch=2,
        grid=(owners,),
        in_specs=[
            full3((nq, hd, rows)),
            pl.BlockSpec((1, 2, plen, hd), lambda o, t, r: (r[2 * o], 0, 0, 0)),
            pl.BlockSpec((1, 2, plen, hd), lambda o, t, r: (r[2 * o + 1], 0, 0, 0)),
            full3((nq, 1, rows)),
            full3((nq, 1, rows)),
            full3((nq, hd, rows)),
        ],
        out_specs=[full3((nq, 1, rows)), full3((nq, 1, rows)), full3((nq, hd, rows))],
    )
    flops = 4 * nq * rows * plen * hd * owners
    return pl.pallas_call(
        block_kernel,
        grid_spec=grid_spec,
        out_shape=[
            jax.ShapeDtypeStruct(m.shape, jnp.float32),
            jax.ShapeDtypeStruct(l.shape, jnp.float32),
            jax.ShapeDtypeStruct(acc.shape, jnp.float32),
        ],
        input_output_aliases={5: 0, 6: 1, 7: 2},
        compiler_params=pltpu.CompilerParams(
            dimension_semantics=("arbitrary",), vmem_limit_bytes=48 * 1024 * 1024
        ),
        cost_estimate=pl.CostEstimate(
            flops=flops,
            transcendentals=nq * rows * plen * owners,
            bytes_accessed=recv.size * 2 + 2 * acc.size * 4,
        ),
    )(tab, remap, query_t, recv, recv, m, l, acc)


def per_device(
    questions, w_query, w_key, w_value, passage_keys, passage_values, passage_ids, slot_order
):
    kv_heads = w_key.shape[1] // HD
    q_heads = w_query.shape[1] // HD
    group = q_heads // kv_heads
    tok_rows = questions.shape[0]
    count = tok_rows // QLEN
    stored = passage_keys.shape[0]
    owners_count = lax.axis_size("store")
    me = lax.axis_index("store")

    listed = count * RETR
    my_ids = passage_ids.reshape(-1)
    my_pos = slot_order.reshape(-1)
    my_owner = my_ids // stored
    onehot = (my_owner[:, None] == jnp.arange(owners_count, dtype=jnp.int32)[None, :]).astype(
        jnp.int32
    )
    before = jnp.cumsum(onehot, axis=0) - onehot
    my_rank = jnp.sum(before * onehot, axis=1)
    hits = [onehot * (my_rank == c).astype(jnp.int32)[:, None] for c in range(CAP)]

    request = jnp.stack(
        [
            jnp.stack(
                [jnp.sum(h * (my_ids % stored)[:, None], axis=0),
                 jnp.sum(h * my_pos[:, None], axis=0)],
                axis=1,
            )
            for h in hits
        ],
        axis=1,
    )
    incoming = lax.all_to_all(request, "store", split_axis=0, concat_axis=0, tiled=True)

    cs, sn = angles((jnp.arange(RETR, dtype=jnp.int32) * PLEN).astype(jnp.float32))
    cos_tab = jnp.concatenate([cs, cs], axis=-1)
    sin_tab = jnp.concatenate([-sn, sn], axis=-1)
    req = incoming.reshape(-1)
    sends = [
        build_send(c, req, cos_tab, sin_tab, passage_keys, passage_values) for c in range(CAP)
    ]

    recvs = [
        lax.all_to_all(s, "store", split_axis=0, concat_axis=0, tiled=True) for s in sends
    ]

    parts = lax.axis_size("tensor")
    zi = lax.axis_index("tensor")
    got = [questions] + [
        lax.ppermute(questions, "tensor", [(i, (i + sh) % parts) for i in range(parts)])
        for sh in range(1, parts)
    ]
    got = jnp.stack(got)
    order = (zi - jnp.arange(parts, dtype=jnp.int32)) % parts
    piece = jnp.concatenate(
        [lax.dynamic_index_in_dim(got, order[j], 0, keepdims=False) for j in range(parts)],
        axis=1,
    )
    qf = jnp.dot(piece, w_query, preferred_element_type=jnp.float32)
    kf = jnp.dot(piece, w_key, preferred_element_type=jnp.float32)
    vf = jnp.dot(piece, w_value, preferred_element_type=jnp.float32)
    qpos = (RETR * PLEN + jnp.arange(QLEN)).astype(jnp.float32)
    cosine, sine = angles(qpos)
    cosine = cosine[None, :, None, :]
    sine = sine[None, :, None, :]
    query = rotate(qf.reshape(count, QLEN, q_heads, HD), cosine, sine).astype(jnp.bfloat16)
    self_key = rotate(kf.reshape(count, QLEN, kv_heads, HD), cosine, sine).astype(jnp.bfloat16)
    self_key = self_key.reshape(count, QLEN, HD)
    self_value = vf.astype(jnp.bfloat16).reshape(count, QLEN, HD)
    query = jnp.transpose(query, (0, 2, 1, 3))

    scale = HD ** (-0.5)
    own = jnp.einsum("qhtd,qud->qhtu", query, self_key, preferred_element_type=jnp.float32) * scale
    causal = jnp.arange(QLEN)[:, None] >= jnp.arange(QLEN)[None, :]
    own = jnp.where(causal, own, -1e30)
    own_peak = jnp.max(own, axis=-1, keepdims=True)
    own_expo = jnp.where(causal, jnp.exp(own - own_peak), 0.0)
    own_total = jnp.sum(own_expo, axis=-1, keepdims=True)
    own_part = jnp.einsum(
        "qhtu,qud->qhtd", own_expo.astype(jnp.bfloat16), self_value,
        preferred_element_type=jnp.float32,
    )
    rows = q_heads * QLEN
    m = own_peak.reshape(count, 1, rows)
    l = own_total.reshape(count, 1, rows)
    acc = jnp.transpose(own_part, (0, 3, 1, 2)).reshape(count, HD, rows)
    query_t = jnp.transpose(query, (0, 3, 1, 2)).reshape(count, HD, rows)

    qidx = jnp.arange(listed, dtype=jnp.int32) // RETR
    slots = jnp.arange(owners_count, dtype=jnp.int32)
    for c in range(CAP):
        hit = hits[c]
        valid = jnp.sum(hit, axis=0)
        tab = jnp.sum(hit * qidx[:, None], axis=0) + valid - 1
        steps = owners_count if c == 0 else min(owners_count, listed // CAP)
        order = jnp.argsort(1 - valid, stable=True).astype(jnp.int32)[:steps]
        tab = tab[order]
        remap = lax.cummax(jnp.where(tab >= 0, order, 0), axis=0)
        m, l, acc = attend_chunk(tab, remap, query_t, recvs[c], m, l, acc)

    ctx = (acc / l).reshape(count, HD, q_heads, QLEN)
    ctx = jnp.transpose(ctx, (0, 3, 2, 1)).reshape(tok_rows, q_heads * HD)
    return ctx.astype(jnp.bfloat16)


def solution(mesh):
    in_specs = (
        P("store", "tensor"),
        P(None, "tensor"),
        P(None, "tensor"),
        P(None, "tensor"),
        P("store", None, "tensor"),
        P("store", None, "tensor"),
        P("store", None),
        P("store", None),
    )
    out_specs = P("store", "tensor")
    return jax.shard_map(
        per_device, mesh=mesh, in_specs=in_specs, out_specs=out_specs, check_vma=False
    )
```

```python
import functools

import jax
import jax.numpy as jnp
from jax import lax
from jax.experimental import pallas as pl
from jax.experimental.pallas import tpu as pltpu
from jax.sharding import PartitionSpec as P

HD = 128
QLEN = 128
PLEN = 512
RETR = 16
CAP = 2


def angles(positions):
    freqs = 500000.0 ** (-(jnp.arange(HD // 2, dtype=jnp.float32) * 2.0) / HD)
    turned = positions[..., None] * freqs
    return (jnp.cos(turned), jnp.sin(turned))


def rotate(values, cosine, sine):
    half = values.shape[-1] // 2
    first = values[..., :half]
    second = values[..., half:]
    return jnp.concatenate(
        [first * cosine - second * sine, second * cosine + first * sine], axis=-1
    )


def send_kernel(slot, req_ref, k_ref, v_ref, c_ref, s_ref, out_ref):
    per = out_ref.shape[0]
    base = pl.program_id(0) * per

    def body(j, carry):
        at = ((base + j) * CAP + slot) * 2
        loc = req_ref[at]
        pos = req_ref[at + 1]
        if slot == 0:
            out_ref[j, 0] = k_ref[loc]
        else:
            k = k_ref[loc].astype(jnp.float32)
            turned = pltpu.roll(k, k.shape[-1] // 2, 1)
            cos_row = c_ref[pl.ds(pos, 1), :]
            sin_row = s_ref[pl.ds(pos, 1), :]
            out_ref[j, 0] = (k * cos_row + turned * sin_row).astype(jnp.bfloat16)
        out_ref[j, 1] = v_ref[loc]
        return carry

    lax.fori_loop(0, per, body, 0)


def build_send(slot, req, cos_tab, sin_tab, passage_keys, passage_values):
    owners = req.shape[0] // (CAP * 2)
    stored, plen, hd = passage_keys.shape
    per = 8
    full = lambda shape: pl.BlockSpec(shape, lambda i, req: (0,) * len(shape))
    grid_spec = pltpu.PrefetchScalarGridSpec(
        num_scalar_prefetch=1,
        grid=(owners // per,),
        in_specs=[
            full((stored, plen, hd)),
            full((stored, plen, hd)),
            full(cos_tab.shape),
            full(sin_tab.shape),
        ],
        out_specs=pl.BlockSpec((per, 2, plen, hd), lambda i, req: (i, 0, 0, 0)),
    )
    return pl.pallas_call(
        functools.partial(send_kernel, slot),
        grid_spec=grid_spec,
        out_shape=jax.ShapeDtypeStruct((owners, 2, plen, hd), jnp.bfloat16),
        compiler_params=pltpu.CompilerParams(dimension_semantics=("arbitrary",)),
        cost_estimate=pl.CostEstimate(
            flops=4 * owners * plen * hd, transcendentals=0,
            bytes_accessed=owners * plen * hd * 2 * 2 + 2 * passage_keys.size * 2,
        ),
    )(req, passage_keys, passage_values, cos_tab, sin_tab)


ROW_TILE = 1024
LOG2E = 1.4426950408889634


def block_kernel(
    rotate_keys, tab_ref, remap_ref, pos_ref, q_ref, kv0_ref, kv1_ref, c_ref, s_ref,
    m_in, l_in, a_in, m_ref, l_ref, a_ref,
):
    o = pl.program_id(0)

    @pl.when(o == 0)
    def _():
        m_ref[...] = m_in[...]
        l_ref[...] = l_in[...]
        a_ref[...] = a_in[...]

    c = (HD ** (-0.5)) * LOG2E
    for j, kv_ref in enumerate((kv0_ref, kv1_ref)):
        qi = tab_ref[2 * o + j]

        @pl.when(qi >= 0)
        def _():
            k = kv_ref[0, 0]
            if rotate_keys:
                pos = pos_ref[2 * o + j]
                kf = k.astype(jnp.float32)
                turned = pltpu.roll(kf, kf.shape[-1] // 2, 1)
                k = (
                    kf * c_ref[pl.ds(pos, 1), :] + turned * s_ref[pl.ds(pos, 1), :]
                ).astype(jnp.bfloat16)
            v = kv_ref[0, 1]
            for r0 in range(0, q_ref.shape[2], ROW_TILE):
                cols = pl.ds(r0, ROW_TILE)
                s = jnp.dot(k, q_ref[qi, :, cols], preferred_element_type=jnp.float32)
                m = jnp.max(s, axis=0, keepdims=True)
                e = jnp.exp2(s * c - m * c)
                l = jnp.sum(e, axis=0, keepdims=True)
                p = lax.dot_general(
                    v, e.astype(jnp.bfloat16), (((0,), (0,)), ((), ())),
                    preferred_element_type=jnp.float32,
                )
                m = m * (HD ** (-0.5))
                m_old = m_ref[qi, :, cols]
                m_new = jnp.maximum(m_old, m)
                w_old = jnp.exp(m_old - m_new)
                w_new = jnp.exp(m - m_new)
                l_ref[qi, :, cols] = w_old * l_ref[qi, :, cols] + w_new * l
                a_ref[qi, :, cols] = w_old * a_ref[qi, :, cols] + w_new * p
                m_ref[qi, :, cols] = m_new


def attend_chunk(rotate_keys, tab, remap, pos, cos_tab, sin_tab, query_t, recv, m, l, acc):
    owners = tab.shape[0] // 2
    nq, hd, rows = query_t.shape
    plen = recv.shape[2]
    full3 = lambda shape: pl.BlockSpec(shape, lambda o, t, r, p: (0, 0, 0))
    grid_spec = pltpu.PrefetchScalarGridSpec(
        num_scalar_prefetch=3,
        grid=(owners,),
        in_specs=[
            full3((nq, hd, rows)),
            pl.BlockSpec((1, 2, plen, hd), lambda o, t, r, p: (r[2 * o], 0, 0, 0)),
            pl.BlockSpec((1, 2, plen, hd), lambda o, t, r, p: (r[2 * o + 1], 0, 0, 0)),
            pl.BlockSpec(cos_tab.shape, lambda o, t, r, p: (0, 0)),
            pl.BlockSpec(sin_tab.shape, lambda o, t, r, p: (0, 0)),
            full3((nq, 1, rows)),
            full3((nq, 1, rows)),
            full3((nq, hd, rows)),
        ],
        out_specs=[full3((nq, 1, rows)), full3((nq, 1, rows)), full3((nq, hd, rows))],
    )
    flops = 4 * nq * rows * plen * hd * owners
    return pl.pallas_call(
        functools.partial(block_kernel, rotate_keys),
        grid_spec=grid_spec,
        out_shape=[
            jax.ShapeDtypeStruct(m.shape, jnp.float32),
            jax.ShapeDtypeStruct(l.shape, jnp.float32),
            jax.ShapeDtypeStruct(acc.shape, jnp.float32),
        ],
        input_output_aliases={8: 0, 9: 1, 10: 2},
        compiler_params=pltpu.CompilerParams(
            dimension_semantics=("arbitrary",), vmem_limit_bytes=48 * 1024 * 1024
        ),
        cost_estimate=pl.CostEstimate(
            flops=flops,
            transcendentals=nq * rows * plen * owners,
            bytes_accessed=recv.size * 2 + 2 * acc.size * 4,
        ),
    )(tab, remap, pos, query_t, recv, recv, cos_tab, sin_tab, m, l, acc)


def per_device(
    questions, w_query, w_key, w_value, passage_keys, passage_values, passage_ids, slot_order
):
    kv_heads = w_key.shape[1] // HD
    q_heads = w_query.shape[1] // HD
    group = q_heads // kv_heads
    tok_rows = questions.shape[0]
    count = tok_rows // QLEN
    stored = passage_keys.shape[0]
    owners_count = lax.axis_size("store")
    me = lax.axis_index("store")

    listed = count * RETR
    my_ids = passage_ids.reshape(-1)
    my_pos = slot_order.reshape(-1)
    my_owner = my_ids // stored
    onehot = (my_owner[:, None] == jnp.arange(owners_count, dtype=jnp.int32)[None, :]).astype(
        jnp.int32
    )
    before = jnp.cumsum(onehot, axis=0) - onehot
    my_rank = jnp.sum(before * onehot, axis=1)
    hits = [onehot * (my_rank == c).astype(jnp.int32)[:, None] for c in range(CAP)]

    request = jnp.stack(
        [
            jnp.stack(
                [jnp.sum(h * (my_ids % stored)[:, None], axis=0),
                 jnp.sum(h * my_pos[:, None], axis=0)],
                axis=1,
            )
            for h in hits
        ],
        axis=1,
    )
    incoming = lax.all_to_all(request, "store", split_axis=0, concat_axis=0, tiled=True)

    cs, sn = angles((jnp.arange(RETR, dtype=jnp.int32) * PLEN).astype(jnp.float32))
    cos_tab = jnp.concatenate([cs, cs], axis=-1)
    sin_tab = jnp.concatenate([-sn, sn], axis=-1)
    req = incoming.reshape(-1)
    sends = [
        build_send(c, req, cos_tab, sin_tab, passage_keys, passage_values) for c in range(CAP)
    ]

    recvs = [
        lax.all_to_all(s, "store", split_axis=0, concat_axis=0, tiled=True) for s in sends
    ]

    parts = lax.axis_size("tensor")
    zi = lax.axis_index("tensor")
    got = [questions] + [
        lax.ppermute(questions, "tensor", [(i, (i + sh) % parts) for i in range(parts)])
        for sh in range(1, parts)
    ]
    got = jnp.stack(got)
    order = (zi - jnp.arange(parts, dtype=jnp.int32)) % parts
    piece = jnp.concatenate(
        [lax.dynamic_index_in_dim(got, order[j], 0, keepdims=False) for j in range(parts)],
        axis=1,
    )
    qf = jnp.dot(piece, w_query, preferred_element_type=jnp.float32)
    kf = jnp.dot(piece, w_key, preferred_element_type=jnp.float32)
    vf = jnp.dot(piece, w_value, preferred_element_type=jnp.float32)
    qpos = (RETR * PLEN + jnp.arange(QLEN)).astype(jnp.float32)
    cosine, sine = angles(qpos)
    cosine = cosine[None, :, None, :]
    sine = sine[None, :, None, :]
    query = rotate(qf.reshape(count, QLEN, q_heads, HD), cosine, sine).astype(jnp.bfloat16)
    self_key = rotate(kf.reshape(count, QLEN, kv_heads, HD), cosine, sine).astype(jnp.bfloat16)
    self_key = self_key.reshape(count, QLEN, HD)
    self_value = vf.astype(jnp.bfloat16).reshape(count, QLEN, HD)
    query = jnp.transpose(query, (0, 2, 1, 3))

    scale = HD ** (-0.5)
    own = jnp.einsum("qhtd,qud->qhtu", query, self_key, preferred_element_type=jnp.float32) * scale
    causal = jnp.arange(QLEN)[:, None] >= jnp.arange(QLEN)[None, :]
    own = jnp.where(causal, own, -1e30)
    own_peak = jnp.max(own, axis=-1, keepdims=True)
    own_expo = jnp.where(causal, jnp.exp(own - own_peak), 0.0)
    own_total = jnp.sum(own_expo, axis=-1, keepdims=True)
    own_part = jnp.einsum(
        "qhtu,qud->qhtd", own_expo.astype(jnp.bfloat16), self_value,
        preferred_element_type=jnp.float32,
    )
    rows = q_heads * QLEN
    m = own_peak.reshape(count, 1, rows)
    l = own_total.reshape(count, 1, rows)
    acc = jnp.transpose(own_part, (0, 3, 1, 2)).reshape(count, HD, rows)
    query_t = jnp.transpose(query, (0, 3, 1, 2)).reshape(count, HD, rows)

    qidx = jnp.arange(listed, dtype=jnp.int32) // RETR
    slots = jnp.arange(owners_count, dtype=jnp.int32)
    for c in range(CAP):
        hit = hits[c]
        valid = jnp.sum(hit, axis=0)
        tab = jnp.sum(hit * qidx[:, None], axis=0) + valid - 1
        steps = owners_count if c == 0 else min(owners_count, listed // CAP)
        order = jnp.argsort(1 - valid, stable=True).astype(jnp.int32)[:steps]
        pos = jnp.sum(hit * my_pos[:, None], axis=0)[order]
        tab = tab[order]
        remap = lax.cummax(jnp.where(tab >= 0, order, 0), axis=0)
        m, l, acc = attend_chunk(
            c == 0, tab, remap, pos, cos_tab, sin_tab, query_t, recvs[c], m, l, acc
        )

    ctx = (acc / l).reshape(count, HD, q_heads, QLEN)
    ctx = jnp.transpose(ctx, (0, 3, 2, 1)).reshape(tok_rows, q_heads * HD)
    return ctx.astype(jnp.bfloat16)


def solution(mesh):
    in_specs = (
        P("store", "tensor"),
        P(None, "tensor"),
        P(None, "tensor"),
        P(None, "tensor"),
        P("store", None, "tensor"),
        P("store", None, "tensor"),
        P("store", None),
        P("store", None),
    )
    out_specs = P("store", "tensor")
    return jax.shard_map(
        per_device, mesh=mesh, in_specs=in_specs, out_specs=out_specs, check_vma=False
    )
```

```python
import functools

import jax
import jax.numpy as jnp
from jax import lax
from jax.experimental import pallas as pl
from jax.experimental.pallas import tpu as pltpu
from jax.sharding import PartitionSpec as P

HD = 128
QLEN = 128
PLEN = 512
RETR = 16
CAP = 2


def angles(positions):
    freqs = 500000.0 ** (-(jnp.arange(HD // 2, dtype=jnp.float32) * 2.0) / HD)
    turned = positions[..., None] * freqs
    return (jnp.cos(turned), jnp.sin(turned))


def rotate(values, cosine, sine):
    half = values.shape[-1] // 2
    first = values[..., :half]
    second = values[..., half:]
    return jnp.concatenate(
        [first * cosine - second * sine, second * cosine + first * sine], axis=-1
    )


def send_kernel(slot, req_ref, k_ref, v_ref, c_ref, s_ref, out_ref):
    per = out_ref.shape[0]
    base = pl.program_id(0) * per

    def body(j, carry):
        at = ((base + j) * CAP + slot) * 2
        loc = req_ref[at]
        pos = req_ref[at + 1]
        if slot == 0:
            out_ref[j, 0] = k_ref[loc]
        else:
            k = k_ref[loc].astype(jnp.float32)
            turned = pltpu.roll(k, k.shape[-1] // 2, 1)
            cos_row = c_ref[pl.ds(pos, 1), :]
            sin_row = s_ref[pl.ds(pos, 1), :]
            out_ref[j, 0] = (k * cos_row + turned * sin_row).astype(jnp.bfloat16)
        out_ref[j, 1] = v_ref[loc]
        return carry

    lax.fori_loop(0, per, body, 0)


def build_send(slot, req, cos_tab, sin_tab, passage_keys, passage_values):
    owners = req.shape[0] // (CAP * 2)
    stored, plen, hd = passage_keys.shape
    per = 8
    full = lambda shape: pl.BlockSpec(shape, lambda i, req: (0,) * len(shape))
    grid_spec = pltpu.PrefetchScalarGridSpec(
        num_scalar_prefetch=1,
        grid=(owners // per,),
        in_specs=[
            full((stored, plen, hd)),
            full((stored, plen, hd)),
            full(cos_tab.shape),
            full(sin_tab.shape),
        ],
        out_specs=pl.BlockSpec((per, 2, plen, hd), lambda i, req: (i, 0, 0, 0)),
    )
    return pl.pallas_call(
        functools.partial(send_kernel, slot),
        grid_spec=grid_spec,
        out_shape=jax.ShapeDtypeStruct((owners, 2, plen, hd), jnp.bfloat16),
        compiler_params=pltpu.CompilerParams(dimension_semantics=("arbitrary",)),
        cost_estimate=pl.CostEstimate(
            flops=4 * owners * plen * hd, transcendentals=0,
            bytes_accessed=owners * plen * hd * 2 * 2 + 2 * passage_keys.size * 2,
        ),
    )(req, passage_keys, passage_values, cos_tab, sin_tab)


ROW_TILE = 1024
LOG2E = 1.4426950408889634


PER_STEP = 4


def block_kernel(rotate_keys, tab_ref, remap_ref, pos_ref, q_ref, *refs):
    kv_refs = refs[:PER_STEP]
    c_ref, s_ref, m_in, l_in, a_in, m_ref, l_ref, a_ref = refs[PER_STEP:]
    o = pl.program_id(0)

    @pl.when(o == 0)
    def _():
        m_ref[...] = m_in[...]
        l_ref[...] = l_in[...]
        a_ref[...] = a_in[...]

    c = (HD ** (-0.5)) * LOG2E
    for j, kv_ref in enumerate(kv_refs):
        qi = tab_ref[PER_STEP * o + j]

        @pl.when(qi >= 0)
        def _():
            k = kv_ref[0, 0]
            if rotate_keys:
                pos = pos_ref[PER_STEP * o + j]
                kf = k.astype(jnp.float32)
                turned = pltpu.roll(kf, kf.shape[-1] // 2, 1)
                k = (
                    kf * c_ref[pl.ds(pos, 1), :] + turned * s_ref[pl.ds(pos, 1), :]
                ).astype(jnp.bfloat16)
            v = kv_ref[0, 1]
            for r0 in range(0, q_ref.shape[2], ROW_TILE):
                cols = pl.ds(r0, ROW_TILE)
                s = jnp.dot(k, q_ref[qi, :, cols], preferred_element_type=jnp.float32)
                m = jnp.max(s, axis=0, keepdims=True)
                e = jnp.exp2(s * c - m * c)
                l = jnp.sum(e, axis=0, keepdims=True)
                p = lax.dot_general(
                    v, e.astype(jnp.bfloat16), (((0,), (0,)), ((), ())),
                    preferred_element_type=jnp.float32,
                )
                m = m * (HD ** (-0.5))
                m_old = m_ref[qi, :, cols]
                m_new = jnp.maximum(m_old, m)
                w_old = jnp.exp(m_old - m_new)
                w_new = jnp.exp(m - m_new)
                l_ref[qi, :, cols] = w_old * l_ref[qi, :, cols] + w_new * l
                a_ref[qi, :, cols] = w_old * a_ref[qi, :, cols] + w_new * p
                m_ref[qi, :, cols] = m_new


def attend_chunk(rotate_keys, tab, remap, pos, cos_tab, sin_tab, query_t, recv, m, l, acc):
    owners = tab.shape[0] // PER_STEP
    nq, hd, rows = query_t.shape
    plen = recv.shape[2]
    full3 = lambda shape: pl.BlockSpec(shape, lambda o, t, r, p: (0, 0, 0))
    grid_spec = pltpu.PrefetchScalarGridSpec(
        num_scalar_prefetch=3,
        grid=(owners,),
        in_specs=[
            full3((nq, hd, rows)),
        ]
        + [
            pl.BlockSpec(
                (1, 2, plen, hd), lambda o, t, r, p, j=j: (r[PER_STEP * o + j], 0, 0, 0)
            )
            for j in range(PER_STEP)
        ]
        + [
            pl.BlockSpec(cos_tab.shape, lambda o, t, r, p: (0, 0)),
            pl.BlockSpec(sin_tab.shape, lambda o, t, r, p: (0, 0)),
            full3((nq, 1, rows)),
            full3((nq, 1, rows)),
            full3((nq, hd, rows)),
        ],
        out_specs=[full3((nq, 1, rows)), full3((nq, 1, rows)), full3((nq, hd, rows))],
    )
    flops = 2 * nq * rows * plen * hd * owners * PER_STEP
    return pl.pallas_call(
        functools.partial(block_kernel, rotate_keys),
        grid_spec=grid_spec,
        out_shape=[
            jax.ShapeDtypeStruct(m.shape, jnp.float32),
            jax.ShapeDtypeStruct(l.shape, jnp.float32),
            jax.ShapeDtypeStruct(acc.shape, jnp.float32),
        ],
        input_output_aliases={6 + PER_STEP: 0, 7 + PER_STEP: 1, 8 + PER_STEP: 2},
        compiler_params=pltpu.CompilerParams(
            dimension_semantics=("arbitrary",), vmem_limit_bytes=48 * 1024 * 1024
        ),
        cost_estimate=pl.CostEstimate(
            flops=flops,
            transcendentals=nq * rows * plen * owners * PER_STEP // 2,
            bytes_accessed=recv.size * 2 + 2 * acc.size * 4,
        ),
    )(tab, remap, pos, query_t, *([recv] * PER_STEP), cos_tab, sin_tab, m, l, acc)


def per_device(
    questions, w_query, w_key, w_value, passage_keys, passage_values, passage_ids, slot_order
):
    kv_heads = w_key.shape[1] // HD
    q_heads = w_query.shape[1] // HD
    group = q_heads // kv_heads
    tok_rows = questions.shape[0]
    count = tok_rows // QLEN
    stored = passage_keys.shape[0]
    owners_count = lax.axis_size("store")
    me = lax.axis_index("store")

    listed = count * RETR
    my_ids = passage_ids.reshape(-1)
    my_pos = slot_order.reshape(-1)
    my_owner = my_ids // stored
    onehot = (my_owner[:, None] == jnp.arange(owners_count, dtype=jnp.int32)[None, :]).astype(
        jnp.int32
    )
    before = jnp.cumsum(onehot, axis=0) - onehot
    my_rank = jnp.sum(before * onehot, axis=1)
    hits = [onehot * (my_rank == c).astype(jnp.int32)[:, None] for c in range(CAP)]

    request = jnp.stack(
        [
            jnp.stack(
                [jnp.sum(h * (my_ids % stored)[:, None], axis=0),
                 jnp.sum(h * my_pos[:, None], axis=0)],
                axis=1,
            )
            for h in hits
        ],
        axis=1,
    )
    incoming = lax.all_to_all(request, "store", split_axis=0, concat_axis=0, tiled=True)

    cs, sn = angles((jnp.arange(RETR, dtype=jnp.int32) * PLEN).astype(jnp.float32))
    cos_tab = jnp.concatenate([cs, cs], axis=-1)
    sin_tab = jnp.concatenate([-sn, sn], axis=-1)
    req = incoming.reshape(-1)
    sends = [
        build_send(c, req, cos_tab, sin_tab, passage_keys, passage_values) for c in range(CAP)
    ]

    recvs = [
        lax.all_to_all(s, "store", split_axis=0, concat_axis=0, tiled=True) for s in sends
    ]

    parts = lax.axis_size("tensor")
    zi = lax.axis_index("tensor")
    got = [questions] + [
        lax.ppermute(questions, "tensor", [(i, (i + sh) % parts) for i in range(parts)])
        for sh in range(1, parts)
    ]
    got = jnp.stack(got)
    order = (zi - jnp.arange(parts, dtype=jnp.int32)) % parts
    piece = jnp.concatenate(
        [lax.dynamic_index_in_dim(got, order[j], 0, keepdims=False) for j in range(parts)],
        axis=1,
    )
    qf = jnp.dot(piece, w_query, preferred_element_type=jnp.float32)
    kf = jnp.dot(piece, w_key, preferred_element_type=jnp.float32)
    vf = jnp.dot(piece, w_value, preferred_element_type=jnp.float32)
    qpos = (RETR * PLEN + jnp.arange(QLEN)).astype(jnp.float32)
    cosine, sine = angles(qpos)
    cosine = cosine[None, :, None, :]
    sine = sine[None, :, None, :]
    query = rotate(qf.reshape(count, QLEN, q_heads, HD), cosine, sine).astype(jnp.bfloat16)
    self_key = rotate(kf.reshape(count, QLEN, kv_heads, HD), cosine, sine).astype(jnp.bfloat16)
    self_key = self_key.reshape(count, QLEN, HD)
    self_value = vf.astype(jnp.bfloat16).reshape(count, QLEN, HD)
    query = jnp.transpose(query, (0, 2, 1, 3))

    scale = HD ** (-0.5)
    own = jnp.einsum("qhtd,qud->qhtu", query, self_key, preferred_element_type=jnp.float32) * scale
    causal = jnp.arange(QLEN)[:, None] >= jnp.arange(QLEN)[None, :]
    own = jnp.where(causal, own, -1e30)
    own_peak = jnp.max(own, axis=-1, keepdims=True)
    own_expo = jnp.where(causal, jnp.exp(own - own_peak), 0.0)
    own_total = jnp.sum(own_expo, axis=-1, keepdims=True)
    own_part = jnp.einsum(
        "qhtu,qud->qhtd", own_expo.astype(jnp.bfloat16), self_value,
        preferred_element_type=jnp.float32,
    )
    rows = q_heads * QLEN
    m = own_peak.reshape(count, 1, rows)
    l = own_total.reshape(count, 1, rows)
    acc = jnp.transpose(own_part, (0, 3, 1, 2)).reshape(count, HD, rows)
    query_t = jnp.transpose(query, (0, 3, 1, 2)).reshape(count, HD, rows)

    qidx = jnp.arange(listed, dtype=jnp.int32) // RETR
    slots = jnp.arange(owners_count, dtype=jnp.int32)
    for c in range(CAP):
        hit = hits[c]
        valid = jnp.sum(hit, axis=0)
        tab = jnp.sum(hit * qidx[:, None], axis=0) + valid - 1
        steps = owners_count if c == 0 else min(owners_count, listed // CAP)
        order = jnp.argsort(1 - valid, stable=True).astype(jnp.int32)[:steps]
        pos = jnp.sum(hit * my_pos[:, None], axis=0)[order]
        tab = tab[order]
        remap = lax.cummax(jnp.where(tab >= 0, order, 0), axis=0)
        m, l, acc = attend_chunk(
            c == 0, tab, remap, pos, cos_tab, sin_tab, query_t, recvs[c], m, l, acc
        )

    ctx = (acc / l).reshape(count, HD, q_heads, QLEN)
    ctx = jnp.transpose(ctx, (0, 3, 2, 1)).reshape(tok_rows, q_heads * HD)
    return ctx.astype(jnp.bfloat16)


def solution(mesh):
    in_specs = (
        P("store", "tensor"),
        P(None, "tensor"),
        P(None, "tensor"),
        P(None, "tensor"),
        P("store", None, "tensor"),
        P("store", None, "tensor"),
        P("store", None),
        P("store", None),
    )
    out_specs = P("store", "tensor")
    return jax.shard_map(
        per_device, mesh=mesh, in_specs=in_specs, out_specs=out_specs, check_vma=False
    )
```

```python
import functools

import jax
import jax.numpy as jnp
from jax import lax
from jax.experimental import pallas as pl
from jax.experimental.pallas import tpu as pltpu
from jax.sharding import PartitionSpec as P

HD = 128
QLEN = 128
PLEN = 512
RETR = 16
CAP = 2


def angles(positions):
    freqs = 500000.0 ** (-(jnp.arange(HD // 2, dtype=jnp.float32) * 2.0) / HD)
    turned = positions[..., None] * freqs
    return (jnp.cos(turned), jnp.sin(turned))


def rotate(values, cosine, sine):
    half = values.shape[-1] // 2
    first = values[..., :half]
    second = values[..., half:]
    return jnp.concatenate(
        [first * cosine - second * sine, second * cosine + first * sine], axis=-1
    )


def send_kernel(slot, req_ref, k_ref, v_ref, c_ref, s_ref, out_ref):
    per = out_ref.shape[0]
    base = pl.program_id(0) * per

    def body(j, carry):
        at = ((base + j) * CAP + slot) * 2
        loc = req_ref[at]
        pos = req_ref[at + 1]
        if slot == 0:
            out_ref[j, 0] = k_ref[loc]
        else:
            k = k_ref[loc].astype(jnp.float32)
            turned = pltpu.roll(k, k.shape[-1] // 2, 1)
            cos_row = c_ref[pl.ds(pos, 1), :]
            sin_row = s_ref[pl.ds(pos, 1), :]
            out_ref[j, 0] = (k * cos_row + turned * sin_row).astype(jnp.bfloat16)
        out_ref[j, 1] = v_ref[loc]
        return carry

    lax.fori_loop(0, per, body, 0)


def build_send(slot, req, cos_tab, sin_tab, passage_keys, passage_values):
    owners = req.shape[0] // (CAP * 2)
    stored, plen, hd = passage_keys.shape
    per = 8
    full = lambda shape: pl.BlockSpec(shape, lambda i, req: (0,) * len(shape))
    grid_spec = pltpu.PrefetchScalarGridSpec(
        num_scalar_prefetch=1,
        grid=(owners // per,),
        in_specs=[
            full((stored, plen, hd)),
            full((stored, plen, hd)),
            full(cos_tab.shape),
            full(sin_tab.shape),
        ],
        out_specs=pl.BlockSpec((per, 2, plen, hd), lambda i, req: (i, 0, 0, 0)),
    )
    return pl.pallas_call(
        functools.partial(send_kernel, slot),
        grid_spec=grid_spec,
        out_shape=jax.ShapeDtypeStruct((owners, 2, plen, hd), jnp.bfloat16),
        compiler_params=pltpu.CompilerParams(dimension_semantics=("arbitrary",)),
        cost_estimate=pl.CostEstimate(
            flops=4 * owners * plen * hd, transcendentals=0,
            bytes_accessed=owners * plen * hd * 2 * 2 + 2 * passage_keys.size * 2,
        ),
    )(req, passage_keys, passage_values, cos_tab, sin_tab)


ROW_TILE = 1024
LOG2E = 1.4426950408889634


PER_STEP = 4


def block_kernel(rotate_keys, tab_ref, remap_ref, pos_ref, q_ref, *refs):
    kv_refs = refs[:PER_STEP]
    c_ref, s_ref, m_in, l_in, a_in, m_ref, l_ref, a_ref, *out = refs[PER_STEP:]
    o = pl.program_id(0)

    @pl.when(o == 0)
    def _():
        m_ref[...] = m_in[...]
        l_ref[...] = l_in[...]
        a_ref[...] = a_in[...]

    c = (HD ** (-0.5)) * LOG2E
    for j, kv_ref in enumerate(kv_refs):
        qi = tab_ref[PER_STEP * o + j]

        @pl.when(qi >= 0)
        def _():
            k = kv_ref[0, 0]
            if rotate_keys:
                pos = pos_ref[PER_STEP * o + j]
                kf = k.astype(jnp.float32)
                turned = pltpu.roll(kf, kf.shape[-1] // 2, 1)
                k = (
                    kf * c_ref[pl.ds(pos, 1), :] + turned * s_ref[pl.ds(pos, 1), :]
                ).astype(jnp.bfloat16)
            v = kv_ref[0, 1]
            for r0 in range(0, q_ref.shape[2], ROW_TILE):
                cols = pl.ds(r0, ROW_TILE)
                s = jnp.dot(k, q_ref[qi, :, cols], preferred_element_type=jnp.float32)
                m = jnp.max(s, axis=0, keepdims=True)
                e = jnp.exp2(s * c - m * c)
                l = jnp.sum(e, axis=0, keepdims=True)
                p = lax.dot_general(
                    v, e.astype(jnp.bfloat16), (((0,), (0,)), ((), ())),
                    preferred_element_type=jnp.float32,
                )
                m = m * (HD ** (-0.5))
                m_old = m_ref[qi, :, cols]
                m_new = jnp.maximum(m_old, m)
                w_old = jnp.exp(m_old - m_new)
                w_new = jnp.exp(m - m_new)
                l_ref[qi, :, cols] = w_old * l_ref[qi, :, cols] + w_new * l
                a_ref[qi, :, cols] = w_old * a_ref[qi, :, cols] + w_new * p
                m_ref[qi, :, cols] = m_new

    if out:
        (ctx_ref,) = out

        @pl.when(o == pl.num_programs(0) - 1)
        def _():
            ctx_ref[...] = (a_ref[...] / l_ref[...]).astype(ctx_ref.dtype)


def attend_chunk(
    rotate_keys, tab, remap, pos, cos_tab, sin_tab, query_t, recv, m, l, acc, final=False
):
    owners = tab.shape[0] // PER_STEP
    nq, hd, rows = query_t.shape
    plen = recv.shape[2]
    full3 = lambda shape: pl.BlockSpec(shape, lambda o, t, r, p: (0, 0, 0))
    grid_spec = pltpu.PrefetchScalarGridSpec(
        num_scalar_prefetch=3,
        grid=(owners,),
        in_specs=[
            full3((nq, hd, rows)),
        ]
        + [
            pl.BlockSpec(
                (1, 2, plen, hd), lambda o, t, r, p, j=j: (r[PER_STEP * o + j], 0, 0, 0)
            )
            for j in range(PER_STEP)
        ]
        + [
            pl.BlockSpec(cos_tab.shape, lambda o, t, r, p: (0, 0)),
            pl.BlockSpec(sin_tab.shape, lambda o, t, r, p: (0, 0)),
            full3((nq, 1, rows)),
            full3((nq, 1, rows)),
            full3((nq, hd, rows)),
        ],
        out_specs=[full3((nq, 1, rows)), full3((nq, 1, rows)), full3((nq, hd, rows))]
        + ([full3((nq, hd, rows))] if final else []),
    )
    flops = 2 * nq * rows * plen * hd * owners * PER_STEP
    return pl.pallas_call(
        functools.partial(block_kernel, rotate_keys),
        grid_spec=grid_spec,
        out_shape=[
            jax.ShapeDtypeStruct(m.shape, jnp.float32),
            jax.ShapeDtypeStruct(l.shape, jnp.float32),
            jax.ShapeDtypeStruct(acc.shape, jnp.float32),
        ]
        + ([jax.ShapeDtypeStruct(acc.shape, jnp.bfloat16)] if final else []),
        input_output_aliases={6 + PER_STEP: 0, 7 + PER_STEP: 1, 8 + PER_STEP: 2},
        compiler_params=pltpu.CompilerParams(
            dimension_semantics=("arbitrary",), vmem_limit_bytes=48 * 1024 * 1024
        ),
        cost_estimate=pl.CostEstimate(
            flops=flops,
            transcendentals=nq * rows * plen * owners * PER_STEP // 2,
            bytes_accessed=recv.size * 2 + 2 * acc.size * 4,
        ),
    )(tab, remap, pos, query_t, *([recv] * PER_STEP), cos_tab, sin_tab, m, l, acc)


def per_device(
    questions, w_query, w_key, w_value, passage_keys, passage_values, passage_ids, slot_order
):
    kv_heads = w_key.shape[1] // HD
    q_heads = w_query.shape[1] // HD
    group = q_heads // kv_heads
    tok_rows = questions.shape[0]
    count = tok_rows // QLEN
    stored = passage_keys.shape[0]
    owners_count = lax.axis_size("store")
    me = lax.axis_index("store")

    listed = count * RETR
    my_ids = passage_ids.reshape(-1)
    my_pos = slot_order.reshape(-1)
    my_owner = my_ids // stored
    onehot = (my_owner[:, None] == jnp.arange(owners_count, dtype=jnp.int32)[None, :]).astype(
        jnp.int32
    )
    before = jnp.cumsum(onehot, axis=0) - onehot
    my_rank = jnp.sum(before * onehot, axis=1)
    hits = [onehot * (my_rank == c).astype(jnp.int32)[:, None] for c in range(CAP)]

    request = jnp.stack(
        [
            jnp.stack(
                [jnp.sum(h * (my_ids % stored)[:, None], axis=0),
                 jnp.sum(h * my_pos[:, None], axis=0)],
                axis=1,
            )
            for h in hits
        ],
        axis=1,
    )
    incoming = lax.all_to_all(request, "store", split_axis=0, concat_axis=0, tiled=True)

    cs, sn = angles((jnp.arange(RETR, dtype=jnp.int32) * PLEN).astype(jnp.float32))
    cos_tab = jnp.concatenate([cs, cs], axis=-1)
    sin_tab = jnp.concatenate([-sn, sn], axis=-1)
    req = incoming.reshape(-1)
    sends = [
        build_send(c, req, cos_tab, sin_tab, passage_keys, passage_values) for c in range(CAP)
    ]

    recvs = [
        lax.all_to_all(s, "store", split_axis=0, concat_axis=0, tiled=True) for s in sends
    ]

    parts = lax.axis_size("tensor")
    zi = lax.axis_index("tensor")
    got = [questions] + [
        lax.ppermute(questions, "tensor", [(i, (i + sh) % parts) for i in range(parts)])
        for sh in range(1, parts)
    ]
    got = jnp.stack(got)
    order = (zi - jnp.arange(parts, dtype=jnp.int32)) % parts
    piece = jnp.concatenate(
        [lax.dynamic_index_in_dim(got, order[j], 0, keepdims=False) for j in range(parts)],
        axis=1,
    )
    qf = jnp.dot(piece, w_query, preferred_element_type=jnp.float32)
    kf = jnp.dot(piece, w_key, preferred_element_type=jnp.float32)
    vf = jnp.dot(piece, w_value, preferred_element_type=jnp.float32)
    qpos = (RETR * PLEN + jnp.arange(QLEN)).astype(jnp.float32)
    cosine, sine = angles(qpos)
    cosine = cosine[None, :, None, :]
    sine = sine[None, :, None, :]
    query = rotate(qf.reshape(count, QLEN, q_heads, HD), cosine, sine).astype(jnp.bfloat16)
    self_key = rotate(kf.reshape(count, QLEN, kv_heads, HD), cosine, sine).astype(jnp.bfloat16)
    self_key = self_key.reshape(count, QLEN, HD)
    self_value = vf.astype(jnp.bfloat16).reshape(count, QLEN, HD)
    query = jnp.transpose(query, (0, 2, 1, 3))

    scale = HD ** (-0.5)
    own = jnp.einsum("qhtd,qud->qhtu", query, self_key, preferred_element_type=jnp.float32) * scale
    causal = jnp.arange(QLEN)[:, None] >= jnp.arange(QLEN)[None, :]
    own = jnp.where(causal, own, -1e30)
    own_peak = jnp.max(own, axis=-1, keepdims=True)
    own_expo = jnp.where(causal, jnp.exp(own - own_peak), 0.0)
    own_total = jnp.sum(own_expo, axis=-1, keepdims=True)
    own_part = jnp.einsum(
        "qhtu,qud->qhtd", own_expo.astype(jnp.bfloat16), self_value,
        preferred_element_type=jnp.float32,
    )
    rows = q_heads * QLEN
    m = own_peak.reshape(count, 1, rows)
    l = own_total.reshape(count, 1, rows)
    acc = jnp.transpose(own_part, (0, 3, 1, 2)).reshape(count, HD, rows)
    query_t = jnp.transpose(query, (0, 3, 1, 2)).reshape(count, HD, rows)

    qidx = jnp.arange(listed, dtype=jnp.int32) // RETR
    slots = jnp.arange(owners_count, dtype=jnp.int32)
    for c in range(CAP):
        hit = hits[c]
        valid = jnp.sum(hit, axis=0)
        tab = jnp.sum(hit * qidx[:, None], axis=0) + valid - 1
        steps = owners_count if c == 0 else min(owners_count, listed // CAP)
        order = jnp.argsort(1 - valid, stable=True).astype(jnp.int32)[:steps]
        pos = jnp.sum(hit * my_pos[:, None], axis=0)[order]
        tab = tab[order]
        remap = lax.cummax(jnp.where(tab >= 0, order, 0), axis=0)
        outs = attend_chunk(
            c == 0, tab, remap, pos, cos_tab, sin_tab, query_t, recvs[c], m, l, acc,
            final=c == CAP - 1,
        )
        m, l, acc = outs[:3]

    ctx = outs[3].reshape(count, HD, q_heads, QLEN)
    return jnp.transpose(ctx, (0, 3, 2, 1)).reshape(tok_rows, q_heads * HD)


def solution(mesh):
    in_specs = (
        P("store", "tensor"),
        P(None, "tensor"),
        P(None, "tensor"),
        P(None, "tensor"),
        P("store", None, "tensor"),
        P("store", None, "tensor"),
        P("store", None),
        P("store", None),
    )
    out_specs = P("store", "tensor")
    return jax.shard_map(
        per_device, mesh=mesh, in_specs=in_specs, out_specs=out_specs, check_vma=False
    )
```

```python
import functools

import jax
import jax.numpy as jnp
from jax import lax
from jax.experimental import pallas as pl
from jax.experimental.pallas import tpu as pltpu
from jax.sharding import PartitionSpec as P

HD = 128
QLEN = 128
PLEN = 512
RETR = 16
CAP = 2


def angles(positions):
    freqs = 500000.0 ** (-(jnp.arange(HD // 2, dtype=jnp.float32) * 2.0) / HD)
    turned = positions[..., None] * freqs
    return (jnp.cos(turned), jnp.sin(turned))


def rotate(values, cosine, sine):
    half = values.shape[-1] // 2
    first = values[..., :half]
    second = values[..., half:]
    return jnp.concatenate(
        [first * cosine - second * sine, second * cosine + first * sine], axis=-1
    )


def send_kernel(slot, req_ref, k_ref, v_ref, c_ref, s_ref, out_ref):
    per = out_ref.shape[0]
    base = pl.program_id(0) * per

    def body(j, carry):
        at = ((base + j) * CAP + slot) * 2
        loc = req_ref[at]
        pos = req_ref[at + 1]
        if slot == 0:
            out_ref[j, 0] = k_ref[loc]
        else:
            k = k_ref[loc].astype(jnp.float32)
            turned = pltpu.roll(k, k.shape[-1] // 2, 1)
            cos_row = c_ref[pl.ds(pos, 1), :]
            sin_row = s_ref[pl.ds(pos, 1), :]
            out_ref[j, 0] = (k * cos_row + turned * sin_row).astype(jnp.bfloat16)
        out_ref[j, 1] = v_ref[loc]
        return carry

    lax.fori_loop(0, per, body, 0)


def build_send(slot, req, cos_tab, sin_tab, passage_keys, passage_values):
    owners = req.shape[0] // (CAP * 2)
    stored, plen, hd = passage_keys.shape
    per = 16 if slot == 0 else 8
    full = lambda shape: pl.BlockSpec(shape, lambda i, req: (0,) * len(shape))
    grid_spec = pltpu.PrefetchScalarGridSpec(
        num_scalar_prefetch=1,
        grid=(owners // per,),
        in_specs=[
            full((stored, plen, hd)),
            full((stored, plen, hd)),
            full(cos_tab.shape),
            full(sin_tab.shape),
        ],
        out_specs=pl.BlockSpec((per, 2, plen, hd), lambda i, req: (i, 0, 0, 0)),
    )
    return pl.pallas_call(
        functools.partial(send_kernel, slot),
        grid_spec=grid_spec,
        out_shape=jax.ShapeDtypeStruct((owners, 2, plen, hd), jnp.bfloat16),
        compiler_params=pltpu.CompilerParams(dimension_semantics=("arbitrary",)),
        cost_estimate=pl.CostEstimate(
            flops=4 * owners * plen * hd, transcendentals=0,
            bytes_accessed=owners * plen * hd * 2 * 2 + 2 * passage_keys.size * 2,
        ),
    )(req, passage_keys, passage_values, cos_tab, sin_tab)


ROW_TILE = 1024
LOG2E = 1.4426950408889634


PER_STEP = 4


def block_kernel(rotate_keys, tab_ref, remap_ref, pos_ref, q_ref, *refs):
    kv_refs = refs[:PER_STEP]
    c_ref, s_ref, m_in, l_in, a_in, m_ref, l_ref, a_ref, *out = refs[PER_STEP:]
    o = pl.program_id(0)

    @pl.when(o == 0)
    def _():
        m_ref[...] = m_in[...]
        l_ref[...] = l_in[...]
        a_ref[...] = a_in[...]

    c = (HD ** (-0.5)) * LOG2E
    for j, kv_ref in enumerate(kv_refs):
        qi = tab_ref[PER_STEP * o + j]

        @pl.when(qi >= 0)
        def _():
            k = kv_ref[0, 0]
            if rotate_keys:
                pos = pos_ref[PER_STEP * o + j]
                kf = k.astype(jnp.float32)
                turned = pltpu.roll(kf, kf.shape[-1] // 2, 1)
                k = (
                    kf * c_ref[pl.ds(pos, 1), :] + turned * s_ref[pl.ds(pos, 1), :]
                ).astype(jnp.bfloat16)
            v = kv_ref[0, 1]
            for r0 in range(0, q_ref.shape[2], ROW_TILE):
                cols = pl.ds(r0, ROW_TILE)
                s = jnp.dot(k, q_ref[qi, :, cols], preferred_element_type=jnp.float32)
                m = jnp.max(s, axis=0, keepdims=True)
                e = jnp.exp2(s * c - m * c)
                l = jnp.sum(e, axis=0, keepdims=True)
                p = lax.dot_general(
                    v, e.astype(jnp.bfloat16), (((0,), (0,)), ((), ())),
                    preferred_element_type=jnp.float32,
                )
                m = m * (HD ** (-0.5))
                m_old = m_ref[qi, :, cols]
                m_new = jnp.maximum(m_old, m)
                w_old = jnp.exp(m_old - m_new)
                w_new = jnp.exp(m - m_new)
                l_ref[qi, :, cols] = w_old * l_ref[qi, :, cols] + w_new * l
                a_ref[qi, :, cols] = w_old * a_ref[qi, :, cols] + w_new * p
                m_ref[qi, :, cols] = m_new

    if out:
        (ctx_ref,) = out

        @pl.when(o == pl.num_programs(0) - 1)
        def _():
            ctx_ref[...] = (a_ref[...] / l_ref[...]).astype(ctx_ref.dtype)


def attend_chunk(
    rotate_keys, tab, remap, pos, cos_tab, sin_tab, query_t, recv, m, l, acc, final=False
):
    owners = tab.shape[0] // PER_STEP
    nq, hd, rows = query_t.shape
    plen = recv.shape[2]
    full3 = lambda shape: pl.BlockSpec(shape, lambda o, t, r, p: (0, 0, 0))
    grid_spec = pltpu.PrefetchScalarGridSpec(
        num_scalar_prefetch=3,
        grid=(owners,),
        in_specs=[
            full3((nq, hd, rows)),
        ]
        + [
            pl.BlockSpec(
                (1, 2, plen, hd), lambda o, t, r, p, j=j: (r[PER_STEP * o + j], 0, 0, 0)
            )
            for j in range(PER_STEP)
        ]
        + [
            pl.BlockSpec(cos_tab.shape, lambda o, t, r, p: (0, 0)),
            pl.BlockSpec(sin_tab.shape, lambda o, t, r, p: (0, 0)),
            full3((nq, 1, rows)),
            full3((nq, 1, rows)),
            full3((nq, hd, rows)),
        ],
        out_specs=[full3((nq, 1, rows)), full3((nq, 1, rows)), full3((nq, hd, rows))]
        + ([full3((nq, hd, rows))] if final else []),
    )
    flops = 2 * nq * rows * plen * hd * owners * PER_STEP
    return pl.pallas_call(
        functools.partial(block_kernel, rotate_keys),
        grid_spec=grid_spec,
        out_shape=[
            jax.ShapeDtypeStruct(m.shape, jnp.float32),
            jax.ShapeDtypeStruct(l.shape, jnp.float32),
            jax.ShapeDtypeStruct(acc.shape, jnp.float32),
        ]
        + ([jax.ShapeDtypeStruct(acc.shape, jnp.bfloat16)] if final else []),
        input_output_aliases={6 + PER_STEP: 0, 7 + PER_STEP: 1, 8 + PER_STEP: 2},
        compiler_params=pltpu.CompilerParams(
            dimension_semantics=("arbitrary",), vmem_limit_bytes=48 * 1024 * 1024
        ),
        cost_estimate=pl.CostEstimate(
            flops=flops,
            transcendentals=nq * rows * plen * owners * PER_STEP // 2,
            bytes_accessed=recv.size * 2 + 2 * acc.size * 4,
        ),
    )(tab, remap, pos, query_t, *([recv] * PER_STEP), cos_tab, sin_tab, m, l, acc)


def per_device(
    questions, w_query, w_key, w_value, passage_keys, passage_values, passage_ids, slot_order
):
    kv_heads = w_key.shape[1] // HD
    q_heads = w_query.shape[1] // HD
    group = q_heads // kv_heads
    tok_rows = questions.shape[0]
    count = tok_rows // QLEN
    stored = passage_keys.shape[0]
    owners_count = lax.axis_size("store")
    me = lax.axis_index("store")

    listed = count * RETR
    my_ids = passage_ids.reshape(-1)
    my_pos = slot_order.reshape(-1)
    my_owner = my_ids // stored
    onehot = (my_owner[:, None] == jnp.arange(owners_count, dtype=jnp.int32)[None, :]).astype(
        jnp.int32
    )
    before = jnp.cumsum(onehot, axis=0) - onehot
    my_rank = jnp.sum(before * onehot, axis=1)
    hits = [onehot * (my_rank == c).astype(jnp.int32)[:, None] for c in range(CAP)]

    request = jnp.stack(
        [
            jnp.stack(
                [jnp.sum(h * (my_ids % stored)[:, None], axis=0),
                 jnp.sum(h * my_pos[:, None], axis=0)],
                axis=1,
            )
            for h in hits
        ],
        axis=1,
    )
    incoming = lax.all_to_all(request, "store", split_axis=0, concat_axis=0, tiled=True)

    cs, sn = angles((jnp.arange(RETR, dtype=jnp.int32) * PLEN).astype(jnp.float32))
    cos_tab = jnp.concatenate([cs, cs], axis=-1)
    sin_tab = jnp.concatenate([-sn, sn], axis=-1)
    req = incoming.reshape(-1)
    sends = [
        build_send(c, req, cos_tab, sin_tab, passage_keys, passage_values) for c in range(CAP)
    ]

    recvs = [
        lax.all_to_all(s, "store", split_axis=0, concat_axis=0, tiled=True) for s in sends
    ]

    parts = lax.axis_size("tensor")
    zi = lax.axis_index("tensor")
    got = [questions] + [
        lax.ppermute(questions, "tensor", [(i, (i + sh) % parts) for i in range(parts)])
        for sh in range(1, parts)
    ]
    got = jnp.stack(got)
    order = (zi - jnp.arange(parts, dtype=jnp.int32)) % parts
    piece = jnp.concatenate(
        [lax.dynamic_index_in_dim(got, order[j], 0, keepdims=False) for j in range(parts)],
        axis=1,
    )
    qf = jnp.dot(piece, w_query, preferred_element_type=jnp.float32)
    kf = jnp.dot(piece, w_key, preferred_element_type=jnp.float32)
    vf = jnp.dot(piece, w_value, preferred_element_type=jnp.float32)
    qpos = (RETR * PLEN + jnp.arange(QLEN)).astype(jnp.float32)
    cosine, sine = angles(qpos)
    cosine = cosine[None, :, None, :]
    sine = sine[None, :, None, :]
    query = rotate(qf.reshape(count, QLEN, q_heads, HD), cosine, sine).astype(jnp.bfloat16)
    self_key = rotate(kf.reshape(count, QLEN, kv_heads, HD), cosine, sine).astype(jnp.bfloat16)
    self_key = self_key.reshape(count, QLEN, HD)
    self_value = vf.astype(jnp.bfloat16).reshape(count, QLEN, HD)
    query = jnp.transpose(query, (0, 2, 1, 3))

    scale = HD ** (-0.5)
    own = jnp.einsum("qhtd,qud->qhtu", query, self_key, preferred_element_type=jnp.float32) * scale
    causal = jnp.arange(QLEN)[:, None] >= jnp.arange(QLEN)[None, :]
    own = jnp.where(causal, own, -1e30)
    own_peak = jnp.max(own, axis=-1, keepdims=True)
    own_expo = jnp.where(causal, jnp.exp(own - own_peak), 0.0)
    own_total = jnp.sum(own_expo, axis=-1, keepdims=True)
    own_part = jnp.einsum(
        "qhtu,qud->qhtd", own_expo.astype(jnp.bfloat16), self_value,
        preferred_element_type=jnp.float32,
    )
    rows = q_heads * QLEN
    m = own_peak.reshape(count, 1, rows)
    l = own_total.reshape(count, 1, rows)
    acc = jnp.transpose(own_part, (0, 3, 1, 2)).reshape(count, HD, rows)
    query_t = jnp.transpose(query, (0, 3, 1, 2)).reshape(count, HD, rows)

    qidx = jnp.arange(listed, dtype=jnp.int32) // RETR
    slots = jnp.arange(owners_count, dtype=jnp.int32)
    for c in range(CAP):
        hit = hits[c]
        valid = jnp.sum(hit, axis=0)
        tab = jnp.sum(hit * qidx[:, None], axis=0) + valid - 1
        steps = owners_count if c == 0 else min(owners_count, listed // CAP)
        order = jnp.argsort(1 - valid, stable=True).astype(jnp.int32)[:steps]
        pos = jnp.sum(hit * my_pos[:, None], axis=0)[order]
        tab = tab[order]
        remap = lax.cummax(jnp.where(tab >= 0, order, 0), axis=0)
        outs = attend_chunk(
            c == 0, tab, remap, pos, cos_tab, sin_tab, query_t, recvs[c], m, l, acc,
            final=c == CAP - 1,
        )
        m, l, acc = outs[:3]

    ctx = outs[3].reshape(count, HD, q_heads, QLEN)
    return jnp.transpose(ctx, (0, 3, 2, 1)).reshape(tok_rows, q_heads * HD)


def solution(mesh):
    in_specs = (
        P("store", "tensor"),
        P(None, "tensor"),
        P(None, "tensor"),
        P(None, "tensor"),
        P("store", None, "tensor"),
        P("store", None, "tensor"),
        P("store", None),
        P("store", None),
    )
    out_specs = P("store", "tensor")
    return jax.shard_map(
        per_device, mesh=mesh, in_specs=in_specs, out_specs=out_specs, check_vma=False
    )
```

```python
import functools

import jax
import jax.numpy as jnp
from jax import lax
from jax.experimental import pallas as pl
from jax.experimental.pallas import tpu as pltpu
from jax.sharding import PartitionSpec as P

HD = 128
QLEN = 128
PLEN = 512
RETR = 16
CAP = 2


def angles(positions):
    freqs = 500000.0 ** (-(jnp.arange(HD // 2, dtype=jnp.float32) * 2.0) / HD)
    turned = positions[..., None] * freqs
    return (jnp.cos(turned), jnp.sin(turned))


def rotate(values, cosine, sine):
    half = values.shape[-1] // 2
    first = values[..., :half]
    second = values[..., half:]
    return jnp.concatenate(
        [first * cosine - second * sine, second * cosine + first * sine], axis=-1
    )


def send_kernel(slot, req_ref, k_ref, v_ref, c_ref, s_ref, out_ref):
    per = out_ref.shape[0]
    base = pl.program_id(0) * per

    def body(j, carry):
        at = ((base + j) * CAP + slot) * 2
        loc = req_ref[at]
        pos = req_ref[at + 1]
        if slot == 0:
            out_ref[j, 0] = k_ref[loc]
        else:
            k = k_ref[loc].astype(jnp.float32)
            turned = pltpu.roll(k, k.shape[-1] // 2, 1)
            cos_row = c_ref[pl.ds(pos, 1), :]
            sin_row = s_ref[pl.ds(pos, 1), :]
            out_ref[j, 0] = (k * cos_row + turned * sin_row).astype(jnp.bfloat16)
        out_ref[j, 1] = v_ref[loc]
        return carry

    lax.fori_loop(0, per, body, 0)


def build_send(slot, req, cos_tab, sin_tab, passage_keys, passage_values):
    owners = req.shape[0] // (CAP * 2)
    stored, plen, hd = passage_keys.shape
    per = 8
    full = lambda shape: pl.BlockSpec(shape, lambda i, req: (0,) * len(shape))
    grid_spec = pltpu.PrefetchScalarGridSpec(
        num_scalar_prefetch=1,
        grid=(owners // per,),
        in_specs=[
            full((stored, plen, hd)),
            full((stored, plen, hd)),
            full(cos_tab.shape),
            full(sin_tab.shape),
        ],
        out_specs=pl.BlockSpec((per, 2, plen, hd), lambda i, req: (i, 0, 0, 0)),
    )
    return pl.pallas_call(
        functools.partial(send_kernel, slot),
        grid_spec=grid_spec,
        out_shape=jax.ShapeDtypeStruct((owners, 2, plen, hd), jnp.bfloat16),
        compiler_params=pltpu.CompilerParams(dimension_semantics=("arbitrary",)),
        cost_estimate=pl.CostEstimate(
            flops=4 * owners * plen * hd, transcendentals=0,
            bytes_accessed=owners * plen * hd * 2 * 2 + 2 * passage_keys.size * 2,
        ),
    )(req, passage_keys, passage_values, cos_tab, sin_tab)


ROW_TILE = 1024
LOG2E = 1.4426950408889634


PER_STEP = 8


def block_kernel(rotate_keys, tab_ref, remap_ref, pos_ref, q_ref, *refs):
    kv_refs = refs[:PER_STEP]
    c_ref, s_ref, m_in, l_in, a_in, m_ref, l_ref, a_ref, *out = refs[PER_STEP:]
    o = pl.program_id(0)

    @pl.when(o == 0)
    def _():
        m_ref[...] = m_in[...]
        l_ref[...] = l_in[...]
        a_ref[...] = a_in[...]

    c = (HD ** (-0.5)) * LOG2E
    for j, kv_ref in enumerate(kv_refs):
        qi = tab_ref[PER_STEP * o + j]

        @pl.when(qi >= 0)
        def _():
            k = kv_ref[0, 0]
            if rotate_keys:
                pos = pos_ref[PER_STEP * o + j]
                kf = k.astype(jnp.float32)
                turned = pltpu.roll(kf, kf.shape[-1] // 2, 1)
                k = (
                    kf * c_ref[pl.ds(pos, 1), :] + turned * s_ref[pl.ds(pos, 1), :]
                ).astype(jnp.bfloat16)
            v = kv_ref[0, 1]
            for r0 in range(0, q_ref.shape[2], ROW_TILE):
                cols = pl.ds(r0, ROW_TILE)
                s = jnp.dot(k, q_ref[qi, :, cols], preferred_element_type=jnp.float32)
                m = jnp.max(s, axis=0, keepdims=True)
                e = jnp.exp2(s * c - m * c)
                l = jnp.sum(e, axis=0, keepdims=True)
                p = lax.dot_general(
                    v, e.astype(jnp.bfloat16), (((0,), (0,)), ((), ())),
                    preferred_element_type=jnp.float32,
                )
                m = m * (HD ** (-0.5))
                m_old = m_ref[qi, :, cols]
                m_new = jnp.maximum(m_old, m)
                w_old = jnp.exp(m_old - m_new)
                w_new = jnp.exp(m - m_new)
                l_ref[qi, :, cols] = w_old * l_ref[qi, :, cols] + w_new * l
                a_ref[qi, :, cols] = w_old * a_ref[qi, :, cols] + w_new * p
                m_ref[qi, :, cols] = m_new

    if out:
        (ctx_ref,) = out

        @pl.when(o == pl.num_programs(0) - 1)
        def _():
            ctx_ref[...] = (a_ref[...] / l_ref[...]).astype(ctx_ref.dtype)


def attend_chunk(
    rotate_keys, tab, remap, pos, cos_tab, sin_tab, query_t, recv, m, l, acc, final=False
):
    owners = tab.shape[0] // PER_STEP
    nq, hd, rows = query_t.shape
    plen = recv.shape[2]
    full3 = lambda shape: pl.BlockSpec(shape, lambda o, t, r, p: (0, 0, 0))
    grid_spec = pltpu.PrefetchScalarGridSpec(
        num_scalar_prefetch=3,
        grid=(owners,),
        in_specs=[
            full3((nq, hd, rows)),
        ]
        + [
            pl.BlockSpec(
                (1, 2, plen, hd), lambda o, t, r, p, j=j: (r[PER_STEP * o + j], 0, 0, 0)
            )
            for j in range(PER_STEP)
        ]
        + [
            pl.BlockSpec(cos_tab.shape, lambda o, t, r, p: (0, 0)),
            pl.BlockSpec(sin_tab.shape, lambda o, t, r, p: (0, 0)),
            full3((nq, 1, rows)),
            full3((nq, 1, rows)),
            full3((nq, hd, rows)),
        ],
        out_specs=[full3((nq, 1, rows)), full3((nq, 1, rows)), full3((nq, hd, rows))]
        + ([full3((nq, hd, rows))] if final else []),
    )
    flops = 2 * nq * rows * plen * hd * owners * PER_STEP
    return pl.pallas_call(
        functools.partial(block_kernel, rotate_keys),
        grid_spec=grid_spec,
        out_shape=[
            jax.ShapeDtypeStruct(m.shape, jnp.float32),
            jax.ShapeDtypeStruct(l.shape, jnp.float32),
            jax.ShapeDtypeStruct(acc.shape, jnp.float32),
        ]
        + ([jax.ShapeDtypeStruct(acc.shape, jnp.bfloat16)] if final else []),
        input_output_aliases={6 + PER_STEP: 0, 7 + PER_STEP: 1, 8 + PER_STEP: 2},
        compiler_params=pltpu.CompilerParams(
            dimension_semantics=("arbitrary",), vmem_limit_bytes=48 * 1024 * 1024
        ),
        cost_estimate=pl.CostEstimate(
            flops=flops,
            transcendentals=nq * rows * plen * owners * PER_STEP // 2,
            bytes_accessed=recv.size * 2 + 2 * acc.size * 4,
        ),
    )(tab, remap, pos, query_t, *([recv] * PER_STEP), cos_tab, sin_tab, m, l, acc)


def per_device(
    questions, w_query, w_key, w_value, passage_keys, passage_values, passage_ids, slot_order
):
    kv_heads = w_key.shape[1] // HD
    q_heads = w_query.shape[1] // HD
    group = q_heads // kv_heads
    tok_rows = questions.shape[0]
    count = tok_rows // QLEN
    stored = passage_keys.shape[0]
    owners_count = lax.axis_size("store")
    me = lax.axis_index("store")

    listed = count * RETR
    my_ids = passage_ids.reshape(-1)
    my_pos = slot_order.reshape(-1)
    my_owner = my_ids // stored
    onehot = (my_owner[:, None] == jnp.arange(owners_count, dtype=jnp.int32)[None, :]).astype(
        jnp.int32
    )
    before = jnp.cumsum(onehot, axis=0) - onehot
    my_rank = jnp.sum(before * onehot, axis=1)
    hits = [onehot * (my_rank == c).astype(jnp.int32)[:, None] for c in range(CAP)]

    request = jnp.stack(
        [
            jnp.stack(
                [jnp.sum(h * (my_ids % stored)[:, None], axis=0),
                 jnp.sum(h * my_pos[:, None], axis=0)],
                axis=1,
            )
            for h in hits
        ],
        axis=1,
    )
    incoming = lax.all_to_all(request, "store", split_axis=0, concat_axis=0, tiled=True)

    cs, sn = angles((jnp.arange(RETR, dtype=jnp.int32) * PLEN).astype(jnp.float32))
    cos_tab = jnp.concatenate([cs, cs], axis=-1)
    sin_tab = jnp.concatenate([-sn, sn], axis=-1)
    req = incoming.reshape(-1)
    sends = [
        build_send(c, req, cos_tab, sin_tab, passage_keys, passage_values) for c in range(CAP)
    ]

    recvs = [
        lax.all_to_all(s, "store", split_axis=0, concat_axis=0, tiled=True) for s in sends
    ]

    parts = lax.axis_size("tensor")
    zi = lax.axis_index("tensor")
    got = [questions] + [
        lax.ppermute(questions, "tensor", [(i, (i + sh) % parts) for i in range(parts)])
        for sh in range(1, parts)
    ]
    got = jnp.stack(got)
    order = (zi - jnp.arange(parts, dtype=jnp.int32)) % parts
    piece = jnp.concatenate(
        [lax.dynamic_index_in_dim(got, order[j], 0, keepdims=False) for j in range(parts)],
        axis=1,
    )
    qf = jnp.dot(piece, w_query, preferred_element_type=jnp.float32)
    kf = jnp.dot(piece, w_key, preferred_element_type=jnp.float32)
    vf = jnp.dot(piece, w_value, preferred_element_type=jnp.float32)
    qpos = (RETR * PLEN + jnp.arange(QLEN)).astype(jnp.float32)
    cosine, sine = angles(qpos)
    cosine = cosine[None, :, None, :]
    sine = sine[None, :, None, :]
    query = rotate(qf.reshape(count, QLEN, q_heads, HD), cosine, sine).astype(jnp.bfloat16)
    self_key = rotate(kf.reshape(count, QLEN, kv_heads, HD), cosine, sine).astype(jnp.bfloat16)
    self_key = self_key.reshape(count, QLEN, HD)
    self_value = vf.astype(jnp.bfloat16).reshape(count, QLEN, HD)
    query = jnp.transpose(query, (0, 2, 1, 3))

    scale = HD ** (-0.5)
    own = jnp.einsum("qhtd,qud->qhtu", query, self_key, preferred_element_type=jnp.float32) * scale
    causal = jnp.arange(QLEN)[:, None] >= jnp.arange(QLEN)[None, :]
    own = jnp.where(causal, own, -1e30)
    own_peak = jnp.max(own, axis=-1, keepdims=True)
    own_expo = jnp.where(causal, jnp.exp(own - own_peak), 0.0)
    own_total = jnp.sum(own_expo, axis=-1, keepdims=True)
    own_part = jnp.einsum(
        "qhtu,qud->qhtd", own_expo.astype(jnp.bfloat16), self_value,
        preferred_element_type=jnp.float32,
    )
    rows = q_heads * QLEN
    m = own_peak.reshape(count, 1, rows)
    l = own_total.reshape(count, 1, rows)
    acc = jnp.transpose(own_part, (0, 3, 1, 2)).reshape(count, HD, rows)
    query_t = jnp.transpose(query, (0, 3, 1, 2)).reshape(count, HD, rows)

    qidx = jnp.arange(listed, dtype=jnp.int32) // RETR
    slots = jnp.arange(owners_count, dtype=jnp.int32)
    for c in range(CAP):
        hit = hits[c]
        valid = jnp.sum(hit, axis=0)
        tab = jnp.sum(hit * qidx[:, None], axis=0) + valid - 1
        steps = owners_count if c == 0 else min(owners_count, listed // CAP)
        order = jnp.argsort(1 - valid, stable=True).astype(jnp.int32)[:steps]
        pos = jnp.sum(hit * my_pos[:, None], axis=0)[order]
        tab = tab[order]
        remap = lax.cummax(jnp.where(tab >= 0, order, 0), axis=0)
        outs = attend_chunk(
            c == 0, tab, remap, pos, cos_tab, sin_tab, query_t, recvs[c], m, l, acc,
            final=c == CAP - 1,
        )
        m, l, acc = outs[:3]

    ctx = outs[3].reshape(count, HD, q_heads, QLEN)
    return jnp.transpose(ctx, (0, 3, 2, 1)).reshape(tok_rows, q_heads * HD)


def solution(mesh):
    in_specs = (
        P("store", "tensor"),
        P(None, "tensor"),
        P(None, "tensor"),
        P(None, "tensor"),
        P("store", None, "tensor"),
        P("store", None, "tensor"),
        P("store", None),
        P("store", None),
    )
    out_specs = P("store", "tensor")
    return jax.shard_map(
        per_device, mesh=mesh, in_specs=in_specs, out_specs=out_specs, check_vma=False
    )
```

```python
import functools

import jax
import jax.numpy as jnp
from jax import lax
from jax.experimental import pallas as pl
from jax.experimental.pallas import tpu as pltpu
from jax.sharding import PartitionSpec as P

HD = 128
QLEN = 128
PLEN = 512
RETR = 16
CAP = 2


def angles(positions):
    freqs = 500000.0 ** (-(jnp.arange(HD // 2, dtype=jnp.float32) * 2.0) / HD)
    turned = positions[..., None] * freqs
    return (jnp.cos(turned), jnp.sin(turned))


def rotate(values, cosine, sine):
    half = values.shape[-1] // 2
    first = values[..., :half]
    second = values[..., half:]
    return jnp.concatenate(
        [first * cosine - second * sine, second * cosine + first * sine], axis=-1
    )


def send_kernel(slot, req_ref, k_ref, v_ref, c_ref, s_ref, out_ref):
    per = out_ref.shape[0]
    base = pl.program_id(0) * per

    def body(j, carry):
        at = ((base + j) * CAP + slot) * 2
        loc = req_ref[at]
        pos = req_ref[at + 1]
        if slot == 0:
            out_ref[j, 0] = k_ref[loc]
        else:
            k = k_ref[loc].astype(jnp.float32)
            turned = pltpu.roll(k, k.shape[-1] // 2, 1)
            cos_row = c_ref[pl.ds(pos, 1), :]
            sin_row = s_ref[pl.ds(pos, 1), :]
            out_ref[j, 0] = (k * cos_row + turned * sin_row).astype(jnp.bfloat16)
        out_ref[j, 1] = v_ref[loc]
        return carry

    lax.fori_loop(0, per, body, 0)


def build_send(slot, req, cos_tab, sin_tab, passage_keys, passage_values):
    owners = req.shape[0] // (CAP * 2)
    stored, plen, hd = passage_keys.shape
    per = 8
    full = lambda shape: pl.BlockSpec(shape, lambda i, req: (0,) * len(shape))
    grid_spec = pltpu.PrefetchScalarGridSpec(
        num_scalar_prefetch=1,
        grid=(owners // per,),
        in_specs=[
            full((stored, plen, hd)),
            full((stored, plen, hd)),
            full(cos_tab.shape),
            full(sin_tab.shape),
        ],
        out_specs=pl.BlockSpec((per, 2, plen, hd), lambda i, req: (i, 0, 0, 0)),
    )
    return pl.pallas_call(
        functools.partial(send_kernel, slot),
        grid_spec=grid_spec,
        out_shape=jax.ShapeDtypeStruct((owners, 2, plen, hd), jnp.bfloat16),
        compiler_params=pltpu.CompilerParams(dimension_semantics=("arbitrary",)),
        cost_estimate=pl.CostEstimate(
            flops=4 * owners * plen * hd, transcendentals=0,
            bytes_accessed=owners * plen * hd * 2 * 2 + 2 * passage_keys.size * 2,
        ),
    )(req, passage_keys, passage_values, cos_tab, sin_tab)


ROW_TILE = 1024
LOG2E = 1.4426950408889634


PER_STEP = 4


def block_kernel(rotate_keys, per_step, tab_ref, remap_ref, pos_ref, q_ref, *refs):
    kv_refs = refs[:per_step]
    c_ref, s_ref, m_in, l_in, a_in, m_ref, l_ref, a_ref, *out = refs[per_step:]
    o = pl.program_id(0)

    @pl.when(o == 0)
    def _():
        m_ref[...] = m_in[...]
        l_ref[...] = l_in[...]
        a_ref[...] = a_in[...]

    c = (HD ** (-0.5)) * LOG2E
    for j, kv_ref in enumerate(kv_refs):
        qi = tab_ref[per_step * o + j]

        @pl.when(qi >= 0)
        def _():
            k = kv_ref[0, 0]
            if rotate_keys:
                pos = pos_ref[per_step * o + j]
                kf = k.astype(jnp.float32)
                turned = pltpu.roll(kf, kf.shape[-1] // 2, 1)
                k = (
                    kf * c_ref[pl.ds(pos, 1), :] + turned * s_ref[pl.ds(pos, 1), :]
                ).astype(jnp.bfloat16)
            v = kv_ref[0, 1]
            for r0 in range(0, q_ref.shape[2], ROW_TILE):
                cols = pl.ds(r0, ROW_TILE)
                s = jnp.dot(k, q_ref[qi, :, cols], preferred_element_type=jnp.float32)
                m = jnp.max(s, axis=0, keepdims=True)
                e = jnp.exp2(s * c - m * c)
                l = jnp.sum(e, axis=0, keepdims=True)
                p = lax.dot_general(
                    v, e.astype(jnp.bfloat16), (((0,), (0,)), ((), ())),
                    preferred_element_type=jnp.float32,
                )
                m = m * (HD ** (-0.5))
                m_old = m_ref[qi, :, cols]
                m_new = jnp.maximum(m_old, m)
                w_old = jnp.exp(m_old - m_new)
                w_new = jnp.exp(m - m_new)
                l_ref[qi, :, cols] = w_old * l_ref[qi, :, cols] + w_new * l
                a_ref[qi, :, cols] = w_old * a_ref[qi, :, cols] + w_new * p
                m_ref[qi, :, cols] = m_new

    if out:
        (ctx_ref,) = out

        @pl.when(o == pl.num_programs(0) - 1)
        def _():
            ctx_ref[...] = (a_ref[...] / l_ref[...]).astype(ctx_ref.dtype)


def attend_chunk(
    rotate_keys, tab, remap, pos, cos_tab, sin_tab, query_t, recv, m, l, acc, final=False
):
    per_step = PER_STEP if rotate_keys else 2 * PER_STEP
    owners = tab.shape[0] // per_step
    nq, hd, rows = query_t.shape
    plen = recv.shape[2]
    full3 = lambda shape: pl.BlockSpec(shape, lambda o, t, r, p: (0, 0, 0))
    grid_spec = pltpu.PrefetchScalarGridSpec(
        num_scalar_prefetch=3,
        grid=(owners,),
        in_specs=[
            full3((nq, hd, rows)),
        ]
        + [
            pl.BlockSpec(
                (1, 2, plen, hd), lambda o, t, r, p, j=j: (r[per_step * o + j], 0, 0, 0)
            )
            for j in range(per_step)
        ]
        + [
            pl.BlockSpec(cos_tab.shape, lambda o, t, r, p: (0, 0)),
            pl.BlockSpec(sin_tab.shape, lambda o, t, r, p: (0, 0)),
            full3((nq, 1, rows)),
            full3((nq, 1, rows)),
            full3((nq, hd, rows)),
        ],
        out_specs=[full3((nq, 1, rows)), full3((nq, 1, rows)), full3((nq, hd, rows))]
        + ([full3((nq, hd, rows))] if final else []),
    )
    flops = 2 * nq * rows * plen * hd * owners * per_step
    return pl.pallas_call(
        functools.partial(block_kernel, rotate_keys, per_step),
        grid_spec=grid_spec,
        out_shape=[
            jax.ShapeDtypeStruct(m.shape, jnp.float32),
            jax.ShapeDtypeStruct(l.shape, jnp.float32),
            jax.ShapeDtypeStruct(acc.shape, jnp.float32),
        ]
        + ([jax.ShapeDtypeStruct(acc.shape, jnp.bfloat16)] if final else []),
        input_output_aliases={6 + per_step: 0, 7 + per_step: 1, 8 + per_step: 2},
        compiler_params=pltpu.CompilerParams(
            dimension_semantics=("arbitrary",), vmem_limit_bytes=48 * 1024 * 1024
        ),
        cost_estimate=pl.CostEstimate(
            flops=flops,
            transcendentals=nq * rows * plen * owners * per_step // 2,
            bytes_accessed=recv.size * 2 + 2 * acc.size * 4,
        ),
    )(tab, remap, pos, query_t, *([recv] * per_step), cos_tab, sin_tab, m, l, acc)


def per_device(
    questions, w_query, w_key, w_value, passage_keys, passage_values, passage_ids, slot_order
):
    kv_heads = w_key.shape[1] // HD
    q_heads = w_query.shape[1] // HD
    group = q_heads // kv_heads
    tok_rows = questions.shape[0]
    count = tok_rows // QLEN
    stored = passage_keys.shape[0]
    owners_count = lax.axis_size("store")
    me = lax.axis_index("store")

    listed = count * RETR
    my_ids = passage_ids.reshape(-1)
    my_pos = slot_order.reshape(-1)
    my_owner = my_ids // stored
    onehot = (my_owner[:, None] == jnp.arange(owners_count, dtype=jnp.int32)[None, :]).astype(
        jnp.int32
    )
    before = jnp.cumsum(onehot, axis=0) - onehot
    my_rank = jnp.sum(before * onehot, axis=1)
    hits = [onehot * (my_rank == c).astype(jnp.int32)[:, None] for c in range(CAP)]

    request = jnp.stack(
        [
            jnp.stack(
                [jnp.sum(h * (my_ids % stored)[:, None], axis=0),
                 jnp.sum(h * my_pos[:, None], axis=0)],
                axis=1,
            )
            for h in hits
        ],
        axis=1,
    )
    incoming = lax.all_to_all(request, "store", split_axis=0, concat_axis=0, tiled=True)

    cs, sn = angles((jnp.arange(RETR, dtype=jnp.int32) * PLEN).astype(jnp.float32))
    cos_tab = jnp.concatenate([cs, cs], axis=-1)
    sin_tab = jnp.concatenate([-sn, sn], axis=-1)
    req = incoming.reshape(-1)
    sends = [
        build_send(c, req, cos_tab, sin_tab, passage_keys, passage_values) for c in range(CAP)
    ]

    recvs = [
        lax.all_to_all(s, "store", split_axis=0, concat_axis=0, tiled=True) for s in sends
    ]

    parts = lax.axis_size("tensor")
    zi = lax.axis_index("tensor")
    got = [questions] + [
        lax.ppermute(questions, "tensor", [(i, (i + sh) % parts) for i in range(parts)])
        for sh in range(1, parts)
    ]
    got = jnp.stack(got)
    order = (zi - jnp.arange(parts, dtype=jnp.int32)) % parts
    piece = jnp.concatenate(
        [lax.dynamic_index_in_dim(got, order[j], 0, keepdims=False) for j in range(parts)],
        axis=1,
    )
    qf = jnp.dot(piece, w_query, preferred_element_type=jnp.float32)
    kf = jnp.dot(piece, w_key, preferred_element_type=jnp.float32)
    vf = jnp.dot(piece, w_value, preferred_element_type=jnp.float32)
    qpos = (RETR * PLEN + jnp.arange(QLEN)).astype(jnp.float32)
    cosine, sine = angles(qpos)
    cosine = cosine[None, :, None, :]
    sine = sine[None, :, None, :]
    query = rotate(qf.reshape(count, QLEN, q_heads, HD), cosine, sine).astype(jnp.bfloat16)
    self_key = rotate(kf.reshape(count, QLEN, kv_heads, HD), cosine, sine).astype(jnp.bfloat16)
    self_key = self_key.reshape(count, QLEN, HD)
    self_value = vf.astype(jnp.bfloat16).reshape(count, QLEN, HD)
    query = jnp.transpose(query, (0, 2, 1, 3))

    scale = HD ** (-0.5)
    own = jnp.einsum("qhtd,qud->qhtu", query, self_key, preferred_element_type=jnp.float32) * scale
    causal = jnp.arange(QLEN)[:, None] >= jnp.arange(QLEN)[None, :]
    own = jnp.where(causal, own, -1e30)
    own_peak = jnp.max(own, axis=-1, keepdims=True)
    own_expo = jnp.where(causal, jnp.exp(own - own_peak), 0.0)
    own_total = jnp.sum(own_expo, axis=-1, keepdims=True)
    own_part = jnp.einsum(
        "qhtu,qud->qhtd", own_expo.astype(jnp.bfloat16), self_value,
        preferred_element_type=jnp.float32,
    )
    rows = q_heads * QLEN
    m = own_peak.reshape(count, 1, rows)
    l = own_total.reshape(count, 1, rows)
    acc = jnp.transpose(own_part, (0, 3, 1, 2)).reshape(count, HD, rows)
    query_t = jnp.transpose(query, (0, 3, 1, 2)).reshape(count, HD, rows)

    qidx = jnp.arange(listed, dtype=jnp.int32) // RETR
    slots = jnp.arange(owners_count, dtype=jnp.int32)
    for c in range(CAP):
        hit = hits[c]
        valid = jnp.sum(hit, axis=0)
        tab = jnp.sum(hit * qidx[:, None], axis=0) + valid - 1
        steps = owners_count if c == 0 else min(owners_count, listed // CAP)
        order = jnp.argsort(1 - valid, stable=True).astype(jnp.int32)[:steps]
        pos = jnp.sum(hit * my_pos[:, None], axis=0)[order]
        tab = tab[order]
        remap = lax.cummax(jnp.where(tab >= 0, order, 0), axis=0)
        outs = attend_chunk(
            c == 0, tab, remap, pos, cos_tab, sin_tab, query_t, recvs[c], m, l, acc,
            final=c == CAP - 1,
        )
        m, l, acc = outs[:3]

    ctx = outs[3].reshape(count, HD, q_heads, QLEN)
    return jnp.transpose(ctx, (0, 3, 2, 1)).reshape(tok_rows, q_heads * HD)


def solution(mesh):
    in_specs = (
        P("store", "tensor"),
        P(None, "tensor"),
        P(None, "tensor"),
        P(None, "tensor"),
        P("store", None, "tensor"),
        P("store", None, "tensor"),
        P("store", None),
        P("store", None),
    )
    out_specs = P("store", "tensor")
    return jax.shard_map(
        per_device, mesh=mesh, in_specs=in_specs, out_specs=out_specs, check_vma=False
    )
```
